32 devices in a mesh: fsdp: 16 (over z, x, core), dp: 2 (over y).
Axes of the slice: x: 2, y: 2, z: 4, core: 2. Of those that a mesh axis runs over, the one named last changes fastest.
Arguments:
- tokens: bfloat16 [16384, 768], P(('fsdp', 'dp')), may hold values from -6 to 6
- cotangent: float32 [16384, 768], P(('fsdp', 'dp')), may hold values from -6 to 6
- lengths: int32 [32], P(('fsdp', 'dp')), may hold values from 128 to 512, as said below
- step_count: int32 [1], replicated, may hold values from 1 to 3
- attention_master: float32 [3072, 768], P(('fsdp', 'dp')), may hold values from -0.4330127 to 0.4330127
- attention_first: float32 [3072, 768], P(('fsdp', 'dp')), may hold values from -224 to 224
- attention_second: float32 [3072, 768], P(('fsdp', 'dp')), may hold values from 589.824 to 9584.64
- feed_master: float32 [6144, 768], P(('fsdp', 'dp')), may hold values from -0.14433757 to 0.14433757
- feed_first: float32 [6144, 768], P(('fsdp', 'dp')), may hold values from -320 to 320
- feed_second: float32 [6144, 768], P(('fsdp', 'dp')), may hold values from 1048.576 to 17039.36
- small_master: float32 [9216], P(('fsdp', 'dp')), may hold values from -2 to 2
- small_first: float32 [9216], P(('fsdp', 'dp')), may hold values from -640 to 640
- small_second: float32 [9216], P(('fsdp', 'dp')), may hold values from 4194.304 to 68157.44
Outputs:
- layer_out: bfloat16 [16384, 768], P(('fsdp', 'dp'))
- tokens_grad: float32 [16384, 768], P(('fsdp', 'dp'))
- attention_new: float32 [3072, 768], P(('fsdp', 'dp'))
- attention_first_new: float32 [3072, 768], P(('fsdp', 'dp'))
- attention_second_new: float32 [3072, 768], P(('fsdp', 'dp'))
- attention_copy: bfloat16 [3072, 768], P(('fsdp', 'dp'))
- feed_new: float32 [6144, 768], P(('fsdp', 'dp'))
- feed_first_new: float32 [6144, 768], P(('fsdp', 'dp'))
- feed_second_new: float32 [6144, 768], P(('fsdp', 'dp'))
- feed_copy: bfloat16 [6144, 768], P(('fsdp', 'dp'))
- small_new: float32 [9216], P(('fsdp', 'dp'))
- small_first_new: float32 [9216], P(('fsdp', 'dp'))
- small_second_new: float32 [9216], P(('fsdp', 'dp'))
- small_copy: bfloat16 [9216], P(('fsdp', 'dp'))
- rms_values: float32 [3], replicated
The draws below stay inside these ranges and needn't reach their ends.
Inputs may be any that keep to these rules, and one draw needn't show every extreme that they name: `lengths`: one sequence has exactly 512 valid tokens and one exactly 128.
All inputs are finite; a program needn't handle non-finite values.
Results may differ from the reference program's by a relative error of at most 0.011.
The reference program's roundings to bfloat16 on the way count: a program that leaves them out, or rounds other values in their place, can miss the bound.
Values may be sent and summed in bfloat16 or wider, within the bound.
No kernel may reach another device: no remote copies, remote signals or barrier semaphores. Data moves between devices by JAX's collectives and lax.ppermute only.
A program may use at most 192 MiB of HBM per device.

```python
import math
import jax
import jax.numpy as jnp
from jax import lax

D = 768
HEADS = 12
HDIM = 64
FF = 3072
SEQ = 512
SEQS = 32
TOKENS = 16384
SMALL = 9216


def draw_lengths(key, part):
    entries = jax.random.randint(jax.random.fold_in(key, 11), (SEQS,), SEQ // 4, SEQ + 1)
    chosen = jax.random.permutation(jax.random.fold_in(key, 12), SEQS)
    entries = entries.at[chosen[0]].set(SEQ)
    entries = entries.at[chosen[1]].set(SEQ // 4)
    return entries.astype(jnp.int32)


def unit_draw(key, shape):
    return jnp.clip(jax.random.normal(key, shape, jnp.float32), -4.0, 4.0)


def draw_attention_master(key, part):
    entries = unit_draw(jax.random.fold_in(key, 21), (4 * D, D))
    block_index = jnp.arange(4 * D) // D
    factor = jnp.where(block_index == 0, 2.0, jnp.where(block_index == 3, 3.0, 1.0)) / D ** 0.5
    return entries * factor[:, None]


def draw_feed_master(key, part):
    entries = unit_draw(jax.random.fold_in(key, 22), (2 * FF, D))
    row_index = jnp.arange(2 * FF)
    factor = jnp.where(row_index < FF, 1.0 / D ** 0.5, 1.5 / FF ** 0.5)
    return entries * factor[:, None]


def draw_small_master(key, part):
    bias_part = 0.5 * unit_draw(jax.random.fold_in(key, 31), (4 * D + FF,))
    gain_one = jax.random.uniform(jax.random.fold_in(key, 32), (D,), jnp.float32, 0.7, 1.3)
    shift_one = 0.3 * unit_draw(jax.random.fold_in(key, 33), (D,))
    gain_two = jax.random.uniform(jax.random.fold_in(key, 34), (D,), jnp.float32, 0.7, 1.3)
    shift_two = 0.3 * unit_draw(jax.random.fold_in(key, 35), (D,))
    return jnp.concatenate([bias_part, gain_one, shift_one, gain_two, shift_two])


def block_scale(rng, extent, cuts, low, top_value):
    factor_of, own = 1.0, jax.random.fold_in(rng, 6)
    for axis_at, blocks in cuts:
        heights = jnp.exp(jax.random.uniform(jax.random.fold_in(own, axis_at), (blocks,), jnp.float32, low / len(cuts), top_value / len(cuts)))
        factor_of = factor_of * jnp.repeat(heights, extent[axis_at] // blocks).reshape([-1 if axis == axis_at else 1 for axis in range(len(extent))])
    return factor_of


def gaussian(stream_key, extent, scale, bound, cuts=(), kind=jnp.bfloat16):
    values = scale * jax.random.normal(stream_key, extent, jnp.float32)
    if cuts:
        values = values * block_scale(stream_key, extent, cuts, -0.22, 0.18)
    return jnp.clip(values, -bound, bound).astype(kind)


def setup_inputs(seed: int = 0) -> dict:
    splits = jax.random.split(jax.random.key(seed), 14)
    tokens = gaussian(splits[0], (TOKENS, D), 1.0, 6.0, ((0, 32),))
    cotangent = gaussian(splits[1], (TOKENS, D), 1.0, 6.0, ((0, 32),), jnp.float32)
    lengths = draw_lengths(jax.random.fold_in(splits[13], 71), 0)
    step_count = jax.random.randint(splits[3], (1,), 1, 4).astype(jnp.int32)
    attention_master = draw_attention_master(jax.random.fold_in(splits[13], 71), 0)
    attention_first = gaussian(splits[5], (4 * D, D), (0.3 * TOKENS ** 0.5), 224.0, ((0, 32),), jnp.float32)
    attention_second = jnp.clip(jnp.exp(math.log(9584.64) - 2.7880929 * jax.random.uniform(splits[6], (4 * D, D), jnp.float32) ** block_scale(splits[6], (4 * D, D), ((0, 32),), -0.2, 0.2)), 589.824, 9584.64)
    feed_master = draw_feed_master(jax.random.fold_in(splits[13], 71), 0)
    feed_first = gaussian(splits[8], (2 * FF, D), (0.4 * TOKENS ** 0.5), 320.0, ((0, 32),), jnp.float32)
    feed_second = jnp.clip(jnp.exp(math.log(17039.36) - 2.7880928 * jax.random.uniform(splits[9], (2 * FF, D), jnp.float32) ** block_scale(splits[9], (2 * FF, D), ((0, 32),), -0.2, 0.2)), 1048.576, 17039.36)
    small_master = draw_small_master(jax.random.fold_in(splits[13], 71), 0)
    small_first = gaussian(splits[11], (SMALL,), (0.8 * TOKENS ** 0.5), 640.0, ((0, 32),), jnp.float32)
    small_second = jnp.clip(jnp.exp(math.log(68157.44) - 2.7880928 * jax.random.uniform(splits[12], (SMALL,), jnp.float32) ** block_scale(splits[12], (SMALL,), ((0, 32),), -0.2, 0.2)), 4194.304, 68157.44)
    return {"tokens": tokens, "cotangent": cotangent, "lengths": lengths, "step_count": step_count, "attention_master": attention_master, "attention_first": attention_first, "attention_second": attention_second, "feed_master": feed_master, "feed_first": feed_first, "feed_second": feed_second, "small_master": small_master, "small_first": small_first, "small_second": small_second}


ln_epsilon = 1e-12
beta_first = 0.5
beta_second = 0.55
adam_epsilon = 1e-06
rate_matrix = 0.04
rate_small = 0.25
weight_decay = 0.01

@jax.custom_vjp
def low(v):
    return lax.optimization_barrier(v.astype(jnp.bfloat16)).astype(jnp.float32)

@jax.custom_vjp
def low_back(v):
    return v

def low_keep(v):
    return (low(v), None)

def low_pass(kept, grad):
    return (grad,)

def back_keep(v):
    return (v, None)

def back_low(kept, grad):
    return (low(grad),)
low.defvjp(low_keep, low_pass)
low_back.defvjp(back_keep, back_low)

def matmul(left_side, right_side):
    return jnp.dot(left_side, right_side, precision=lax.Precision.HIGHEST, preferred_element_type=jnp.float32)

def layer_norm(entries, norm_gain, norm_shift):
    center = lax.optimization_barrier(jnp.mean(entries, axis=-1, keepdims=True))
    offset = entries - center
    spread = lax.optimization_barrier(jnp.mean(offset * offset, axis=-1, keepdims=True))
    return offset * lax.rsqrt(spread + ln_epsilon) * norm_gain + norm_shift

def split_small(small_weights):
    pieces = []
    position = 0
    for length in (D, D, D, FF, D, D, D, D, D):
        pieces.append(small_weights[position:position + length])
        position = position + length
    return pieces

def forward(hidden, attention_weights, feed_weights, small_weights, token_valid):
    query_bias, value_bias, output_bias, inner_bias, outer_bias, first_gain, first_shift, second_gain, second_shift = split_small(small_weights)
    query_weight = attention_weights[0:D]
    key_weight = attention_weights[D:2 * D]
    value_weight = attention_weights[2 * D:3 * D]
    output_weight = attention_weights[3 * D:4 * D]
    inner_weight = feed_weights[0:FF]
    outer_weight = feed_weights[FF:2 * FF]
    queries = low_back(low(matmul(hidden, query_weight) + query_bias))
    key_vectors = low_back(low(matmul(hidden, key_weight)))
    values = low_back(low(matmul(hidden, value_weight) + value_bias))
    groups = hidden.shape[0] // SEQ
    head_shape = (groups, SEQ, HEADS, HDIM)
    scores = jnp.einsum('gqhd,gkhd->ghqk', queries.reshape(head_shape), key_vectors.reshape(head_shape), precision=lax.Precision.HIGHEST) * (1.0 / math.sqrt(HDIM))
    scores = low_back(scores)
    key_valid = token_valid.reshape(groups, 1, 1, SEQ)
    scores = jnp.where(key_valid > 0, scores, -1e+30)
    weights_soft = low(jax.nn.softmax(scores, axis=-1))
    attended = jnp.einsum('ghqk,gkhd->gqhd', weights_soft, values.reshape(head_shape), precision=lax.Precision.HIGHEST)
    attended = low_back(low(attended.reshape(hidden.shape[0], D)))
    branch_attention = low_back(matmul(attended, output_weight) + output_bias)
    normed = layer_norm(hidden + branch_attention, first_gain, first_shift)
    inner_sum = low_back(matmul(low(normed), inner_weight.T) + inner_bias)
    active = low(jax.nn.gelu(inner_sum, approximate=False))
    branch_feed = low_back(matmul(active, outer_weight) + outer_bias)
    residual = normed + branch_feed
    result = layer_norm(residual, second_gain, second_shift)
    return (result, (residual, branch_attention, branch_feed))

def adam_step(master, first_moment, second, gradient, step_rate, decay_rate, step_float):
    first_new = beta_first * first_moment + (1.0 - beta_first) * gradient
    second_new = beta_second * second + (1.0 - beta_second) * gradient * gradient
    first_hat = first_new / (1.0 - beta_first ** step_float)
    second_hat = second_new / (1.0 - beta_second ** step_float)
    master_new = master - step_rate * (first_hat / (jnp.sqrt(second_hat) + adam_epsilon) + decay_rate * master)
    return (master_new, first_new, second_new)

def reference(tokens, cotangent, lengths, step_count, attention_master, attention_first, attention_second, feed_master, feed_first, feed_second, small_master, small_first, small_second):
    attention_weights = low(attention_master)
    feed_weights = low(feed_master)
    small_weights = low(small_master)
    group_seqs = math.gcd(SEQS, max(1, 4096 // SEQ))
    group_count = SEQS // group_seqs
    group_rows = group_seqs * SEQ
    positions = jnp.arange(SEQ, dtype=jnp.int32)
    valid_all = (positions[None, :] < lengths[:, None]).astype(jnp.float32).reshape(group_count, group_rows)
    hidden_all = tokens.astype(jnp.float32).reshape(group_count, group_rows, D)
    back_all = cotangent.astype(jnp.float32).reshape(group_count, group_rows, D)

    def one_group(running, inputs):
        attention_total, feed_total, small_total, squares, counted = running
        hidden, back_rows, token_valid = inputs

        def local_forward(hidden_in, attention_in, feed_in, small_in):
            return forward(hidden_in, attention_in, feed_in, small_in, token_valid)
        result, pullback, branches = jax.vjp(local_forward, hidden, attention_weights, feed_weights, small_weights, has_aux=True)
        hidden_grad, attention_grad, feed_grad, small_grad = pullback(back_rows)
        column = token_valid[:, None]
        group_squares = jnp.stack([jnp.sum(branch * branch * column) for branch in branches])
        running_new = (attention_total + attention_grad, feed_total + feed_grad, small_total + small_grad, squares + group_squares, counted + jnp.sum(token_valid))
        return (running_new, (result.astype(jnp.bfloat16), hidden_grad))
    start_state = (jnp.zeros((4 * D, D), jnp.float32), jnp.zeros((2 * FF, D), jnp.float32), jnp.zeros((SMALL,), jnp.float32), jnp.zeros((3,), jnp.float32), jnp.zeros((), jnp.float32))
    final_state, outputs = lax.scan(one_group, start_state, (hidden_all, back_all, valid_all))
    attention_grad, feed_grad, small_grad, squares, counted = final_state
    layer_out = outputs[0].reshape(TOKENS, D)
    tokens_grad = outputs[1].reshape(TOKENS, D)
    rms_values = jnp.sqrt(squares / (counted * D))
    step_float = step_count[0].astype(jnp.float32)
    attention_new, attention_first_new, attention_second_new = adam_step(attention_master, attention_first, attention_second, attention_grad, rate_matrix, weight_decay, step_float)
    feed_new, feed_first_new, feed_second_new = adam_step(feed_master, feed_first, feed_second, feed_grad, rate_matrix, weight_decay, step_float)
    small_new, small_first_new, small_second_new = adam_step(small_master, small_first, small_second, small_grad, rate_small, 0.0, step_float)
    return (layer_out, tokens_grad, attention_new, attention_first_new, attention_second_new, attention_new.astype(jnp.bfloat16), feed_new, feed_first_new, feed_second_new, feed_new.astype(jnp.bfloat16), small_new, small_first_new, small_second_new, small_new.astype(jnp.bfloat16), rms_values)
```

```python
import math

import jax
import jax.numpy as jnp
from jax import lax
from jax.sharding import PartitionSpec as P

D = 768
HEADS = 12
HDIM = 64
FF = 3072
SEQ = 512


ln_epsilon = 1e-12
beta_first = 0.5
beta_second = 0.55
adam_epsilon = 1e-06
rate_matrix = 0.04
rate_small = 0.25
weight_decay = 0.01


def product(left_side, right_side):
    return jnp.dot(left_side, right_side, preferred_element_type=jnp.float32)


def product_rows(left_side, right_side):
    return lax.dot_general(
        left_side, right_side, (((0,), (0,)), ((), ())), preferred_element_type=jnp.float32
    )


def product_cols(left_side, right_side):
    return lax.dot_general(
        left_side, right_side, (((1,), (1,)), ((), ())), preferred_element_type=jnp.float32
    )


def column_total(entries):
    return jnp.sum(entries, axis=0, dtype=jnp.float32)


def layer_norm(entries, norm_gain, norm_shift):
    center = jnp.mean(entries, axis=-1, keepdims=True)
    offset = entries - center
    spread = jnp.mean(offset * offset, axis=-1, keepdims=True)
    return offset * lax.rsqrt(spread + ln_epsilon) * norm_gain + norm_shift


def gelu_exact(entries):
    return jax.nn.gelu(entries, approximate=False)


def split_small(small_full):
    pieces = []
    position = 0
    for length in (D, D, D, FF, D, D, D, D, D):
        pieces.append(small_full[position : position + length].astype(jnp.float32))
        position = position + length
    return pieces


def head_view(entries):
    return entries.reshape(SEQ, HEADS, HDIM)


def masked_scores(queries, key_vectors, key_valid):
    scores = jnp.einsum(
        "qhd,khd->hqk",
        head_view(queries),
        head_view(key_vectors),
        preferred_element_type=jnp.float32,
    ) * (1.0 / math.sqrt(HDIM))
    return jnp.where(key_valid[None, None, :] > 0, scores, -1e30)


def attend_forward(pieces):
    queries, key_vectors, values, key_valid = pieces
    scores = masked_scores(queries, key_vectors, key_valid)
    row_max = jnp.max(scores, axis=-1, keepdims=True)
    exponent = jnp.exp(scores - row_max)
    row_total = jnp.sum(exponent, axis=-1, keepdims=True)
    probability = (exponent / row_total).astype(jnp.bfloat16)
    attended = jnp.einsum(
        "hqk,khd->qhd", probability, head_view(values), preferred_element_type=jnp.float32
    )
    return (attended.reshape(SEQ, D).astype(jnp.bfloat16), (row_max + jnp.log(row_total))[:, :, 0])


def attend_backward(pieces):
    queries, key_vectors, values, key_valid, log_total, attended_grad = pieces
    scores = masked_scores(queries, key_vectors, key_valid)
    probability = jnp.exp(scores - log_total[:, :, None])
    probability_low = probability.astype(jnp.bfloat16)
    grad_heads = head_view(attended_grad)
    value_grad = jnp.einsum(
        "hqk,qhd->khd", probability_low, grad_heads, preferred_element_type=jnp.float32
    )
    probability_grad = jnp.einsum(
        "qhd,khd->hqk", grad_heads, head_view(values), preferred_element_type=jnp.float32
    )
    inner_total = jnp.sum(probability * probability_grad, axis=-1, keepdims=True)
    score_grad = (probability * (probability_grad - inner_total)).astype(jnp.bfloat16)
    score_scale = 1.0 / math.sqrt(HDIM)
    query_grad = (
        jnp.einsum(
            "hqk,khd->qhd", score_grad, head_view(key_vectors), preferred_element_type=jnp.float32
        )
        * score_scale
    )
    key_grad = (
        jnp.einsum(
            "hqk,qhd->khd", score_grad, head_view(queries), preferred_element_type=jnp.float32
        )
        * score_scale
    )
    return (
        query_grad.reshape(SEQ, D).astype(jnp.bfloat16),
        key_grad.reshape(SEQ, D).astype(jnp.bfloat16),
        value_grad.reshape(SEQ, D).astype(jnp.bfloat16),
    )


def adam_step(master, first_moment, second, gradient, step_rate, decay_rate, step_float):
    first_new = beta_first * first_moment + (1.0 - beta_first) * gradient
    second_new = beta_second * second + (1.0 - beta_second) * gradient * gradient
    first_hat = first_new / (1.0 - beta_first**step_float)
    second_hat = second_new / (1.0 - beta_second**step_float)
    master_new = master - step_rate * (
        first_hat / (jnp.sqrt(second_hat) + adam_epsilon) + decay_rate * master
    )
    return (master_new, first_new, second_new)


def padded_rows(rows, multiple):
    return -(-rows // multiple) * multiple


def gather_working(attention_master, feed_master, small_master):
    attention_rows = attention_master.shape[0]
    feed_rows = feed_master.shape[0]
    small_count = small_master.shape[0]
    main_rows = attention_rows + feed_rows
    extra_rows = padded_rows(main_rows + padded_rows(small_count, D) // D, 16) - main_rows
    small_flat = jnp.zeros((extra_rows * D,), jnp.bfloat16)
    small_flat = small_flat.at[:small_count].set(small_master.astype(jnp.bfloat16))
    block = jnp.concatenate(
        [
            attention_master.astype(jnp.bfloat16),
            feed_master.astype(jnp.bfloat16),
            small_flat.reshape(extra_rows, D),
        ],
        axis=0,
    )
    gathered = lax.all_gather(block, ("fsdp", "dp"), axis=0, tiled=False)
    owners = gathered.shape[0]
    attention_full = gathered[:, :attention_rows].reshape(owners * attention_rows, D)
    feed_full = gathered[:, attention_rows:main_rows].reshape(owners * feed_rows, D)
    small_full = gathered[:, main_rows:].reshape(owners, extra_rows * D)[:, :small_count]
    return attention_full, feed_full, small_full.reshape(owners * small_count)


def scatter_gradients(attention_grad_all, feed_grad_all, small_grad_all, partials):
    owners = lax.psum(1, ("fsdp", "dp"))
    me = lax.axis_index(("fsdp", "dp"))
    attention_rows = attention_grad_all.shape[0] // owners
    feed_rows = feed_grad_all.shape[0] // owners
    small_count = small_grad_all.shape[0] // owners
    main_rows = attention_rows + feed_rows
    slots = partials.shape[0]
    extra_count = small_count + owners * slots
    extra_rows = padded_rows(main_rows + padded_rows(extra_count, D) // D, 8) - main_rows
    slot_row = jnp.zeros((owners * slots,), jnp.float32)
    slot_row = lax.dynamic_update_slice(slot_row, partials, (me * slots,))
    extra = jnp.concatenate(
        [
            small_grad_all.reshape(owners, small_count),
            jnp.broadcast_to(slot_row[None], (owners, owners * slots)),
            jnp.zeros((owners, extra_rows * D - extra_count), jnp.float32),
        ],
        axis=1,
    ).reshape(owners, extra_rows, D)
    packed = jnp.concatenate(
        [
            attention_grad_all.reshape(owners, attention_rows, D),
            feed_grad_all.reshape(owners, feed_rows, D),
            extra,
        ],
        axis=1,
    ).reshape(owners * (main_rows + extra_rows), D)
    owned = lax.psum_scatter(packed, ("fsdp", "dp"), scatter_dimension=0, tiled=True)
    attention_owned = owned[:attention_rows]
    feed_owned = owned[attention_rows:main_rows]
    extra_owned = owned[main_rows:].reshape(extra_rows * D)
    small_owned = extra_owned[:small_count]
    gathered_partials = extra_owned[small_count:extra_count].reshape(owners, slots)
    totals = gathered_partials[0]
    for index in range(1, owners):
        totals = totals + gathered_partials[index]
    return attention_owned, feed_owned, small_owned, totals


def on_device(
    tokens,
    cotangent,
    lengths,
    step_count,
    attention_master,
    attention_first,
    attention_second,
    feed_master,
    feed_first,
    feed_second,
    small_master,
    small_first,
    small_second,
):
    row_count = tokens.shape[0]
    sequence_count = row_count // SEQ
    attention_full, feed_full, small_full = gather_working(attention_master, feed_master, small_master)
    key_valid = (
        lax.broadcasted_iota(jnp.int32, (sequence_count, SEQ), 1) < lengths[:, None]
    ).astype(jnp.float32)
    token_valid = key_valid.reshape(row_count)
    (
        query_bias,
        value_bias,
        output_bias,
        inner_bias,
        outer_bias,
        first_gain,
        first_shift,
        second_gain,
        second_shift,
    ) = split_small(small_full)
    queries = (product(tokens, attention_full[0:D]) + query_bias).astype(jnp.bfloat16)
    key_vectors = product(tokens, attention_full[D : 2 * D]).astype(jnp.bfloat16)
    values = (product(tokens, attention_full[2 * D : 3 * D]) + value_bias).astype(jnp.bfloat16)
    seq_shape = (sequence_count, SEQ, D)
    attended, log_total = lax.map(
        attend_forward,
        (
            queries.reshape(seq_shape),
            key_vectors.reshape(seq_shape),
            values.reshape(seq_shape),
            key_valid,
        ),
    )
    attended = attended.reshape(row_count, D)
    branch_attention = product(attended, attention_full[3 * D : 4 * D]) + output_bias
    first_sum = tokens.astype(jnp.float32) + branch_attention
    normed = layer_norm(first_sum, first_gain, first_shift)
    normed_low = normed.astype(jnp.bfloat16)
    inner_sum = product_cols(normed_low, feed_full[0:FF]) + inner_bias
    active = gelu_exact(inner_sum).astype(jnp.bfloat16)
    branch_feed = product(active, feed_full[FF : 2 * FF]) + outer_bias
    residual = normed + branch_feed
    layer_out = layer_norm(residual, second_gain, second_shift).astype(jnp.bfloat16)
    column = token_valid[:, None]
    partials = jnp.stack(
        [
            jnp.sum(residual * residual * column),
            jnp.sum(branch_attention * branch_attention * column),
            jnp.sum(branch_feed * branch_feed * column),
            jnp.sum(token_valid),
        ]
    )
    query_weight = attention_full[0:D]
    key_weight = attention_full[D : 2 * D]
    value_weight = attention_full[2 * D : 3 * D]
    output_weight = attention_full[3 * D : 4 * D]
    outer_weight = feed_full[FF : 2 * FF]
    inner_weight = feed_full[0:FF]
    second_pull = jax.vjp(layer_norm, residual, second_gain, second_shift)[1]
    residual_grad, second_gain_grad, second_shift_grad = second_pull(cotangent)
    feed_out_grad = residual_grad.astype(jnp.bfloat16)
    outer_bias_grad = column_total(feed_out_grad)
    outer_weight_grad = product_rows(active, feed_out_grad)
    active_grad = product_cols(feed_out_grad, outer_weight)
    inner_grad = jax.vjp(gelu_exact, inner_sum)[1](active_grad)[0].astype(jnp.bfloat16)
    inner_bias_grad = column_total(inner_grad)
    inner_weight_grad = product_rows(inner_grad, normed_low)
    normed_grad = residual_grad + product(inner_grad, inner_weight)
    feed_grad_all = jnp.concatenate([inner_weight_grad, outer_weight_grad], axis=0)
    first_pull = jax.vjp(layer_norm, first_sum, first_gain, first_shift)[1]
    first_sum_grad, first_gain_grad, first_shift_grad = first_pull(normed_grad)
    branch_grad_low = first_sum_grad.astype(jnp.bfloat16)
    output_bias_grad = column_total(branch_grad_low)
    output_weight_grad = product_rows(attended, branch_grad_low)
    attended_grad = product_cols(branch_grad_low, output_weight).astype(jnp.bfloat16)
    query_grad, key_grad, value_grad = lax.map(
        attend_backward,
        (
            queries.reshape(seq_shape),
            key_vectors.reshape(seq_shape),
            values.reshape(seq_shape),
            key_valid,
            log_total,
            attended_grad.reshape(seq_shape),
        ),
    )
    query_grad = query_grad.reshape(row_count, D)
    key_grad = key_grad.reshape(row_count, D)
    value_grad = value_grad.reshape(row_count, D)
    query_weight_grad = product_rows(tokens, query_grad)
    key_weight_grad = product_rows(tokens, key_grad)
    value_weight_grad = product_rows(tokens, value_grad)
    query_bias_grad = column_total(query_grad)
    value_bias_grad = column_total(value_grad)
    tokens_grad = (
        first_sum_grad
        + product_cols(query_grad, query_weight)
        + product_cols(key_grad, key_weight)
        + product_cols(value_grad, value_weight)
    )
    attention_grad_all = jnp.concatenate(
        [query_weight_grad, key_weight_grad, value_weight_grad, output_weight_grad], axis=0
    )
    small_grad_all = jnp.concatenate(
        [
            query_bias_grad,
            value_bias_grad,
            output_bias_grad,
            inner_bias_grad,
            outer_bias_grad,
            first_gain_grad,
            first_shift_grad,
            second_gain_grad,
            second_shift_grad,
        ]
    )
    attention_owned, feed_owned, small_owned, totals = scatter_gradients(
        attention_grad_all, feed_grad_all, small_grad_all, partials
    )
    rms_values = jnp.sqrt(totals[:3] / (totals[3] * D))
    step_float = step_count[0].astype(jnp.float32)
    attention_new, attention_first_new, attention_second_new = adam_step(
        attention_master,
        attention_first,
        attention_second,
        attention_owned,
        rate_matrix,
        weight_decay,
        step_float,
    )
    feed_new, feed_first_new, feed_second_new = adam_step(
        feed_master, feed_first, feed_second, feed_owned, rate_matrix, weight_decay, step_float
    )
    small_new, small_first_new, small_second_new = adam_step(
        small_master, small_first, small_second, small_owned, rate_small, 0.0, step_float
    )
    return (
        layer_out,
        tokens_grad,
        attention_new,
        attention_first_new,
        attention_second_new,
        attention_new.astype(jnp.bfloat16),
        feed_new,
        feed_first_new,
        feed_second_new,
        feed_new.astype(jnp.bfloat16),
        small_new,
        small_first_new,
        small_second_new,
        small_new.astype(jnp.bfloat16),
        rms_values,
    )


def solution(mesh):
    placed = (
        P(("fsdp", "dp"), None),
        P(("fsdp", "dp"), None),
        P(("fsdp", "dp")),
        P(),
        P(("fsdp", "dp"), None),
        P(("fsdp", "dp"), None),
        P(("fsdp", "dp"), None),
        P(("fsdp", "dp"), None),
        P(("fsdp", "dp"), None),
        P(("fsdp", "dp"), None),
        P(("fsdp", "dp")),
        P(("fsdp", "dp")),
        P(("fsdp", "dp")),
    )
    return jax.shard_map(
        on_device,
        mesh=mesh,
        in_specs=placed,
        out_specs=(
            P(("fsdp", "dp"), None),
            P(("fsdp", "dp"), None),
            P(("fsdp", "dp"), None),
            P(("fsdp", "dp"), None),
            P(("fsdp", "dp"), None),
            P(("fsdp", "dp"), None),
            P(("fsdp", "dp"), None),
            P(("fsdp", "dp"), None),
            P(("fsdp", "dp"), None),
            P(("fsdp", "dp"), None),
            P(("fsdp", "dp")),
            P(("fsdp", "dp")),
            P(("fsdp", "dp")),
            P(("fsdp", "dp")),
            P(),
        ),
        check_vma=False,
    )
```

```python
import math

import jax
import jax.numpy as jnp
from jax import lax
from jax.sharding import PartitionSpec as P

D = 768
HEADS = 12
HDIM = 64
FF = 3072
SEQ = 512


ln_epsilon = 1e-12
beta_first = 0.5
beta_second = 0.55
adam_epsilon = 1e-06
rate_matrix = 0.04
rate_small = 0.25
weight_decay = 0.01


def product(left_side, right_side):
    return jnp.dot(left_side, right_side, preferred_element_type=jnp.float32)


def product_rows(left_side, right_side):
    return lax.dot_general(
        left_side, right_side, (((0,), (0,)), ((), ())), preferred_element_type=jnp.float32
    )


def product_cols(left_side, right_side):
    return lax.dot_general(
        left_side, right_side, (((1,), (1,)), ((), ())), preferred_element_type=jnp.float32
    )


def column_total(entries):
    return jnp.sum(entries, axis=0, dtype=jnp.float32)


def layer_norm(entries, norm_gain, norm_shift):
    center = jnp.mean(entries, axis=-1, keepdims=True)
    offset = entries - center
    spread = jnp.mean(offset * offset, axis=-1, keepdims=True)
    return offset * lax.rsqrt(spread + ln_epsilon) * norm_gain + norm_shift


def gelu_exact(entries):
    return jax.nn.gelu(entries, approximate=False)


def split_small(small_full):
    pieces = []
    position = 0
    for length in (D, D, D, FF, D, D, D, D, D):
        pieces.append(small_full[position : position + length].astype(jnp.float32))
        position = position + length
    return pieces


def head_view(entries):
    return entries.reshape(SEQ, HEADS, HDIM)


def masked_scores(queries, key_vectors, key_valid):
    scores = jnp.einsum(
        "qhd,khd->hqk",
        head_view(queries),
        head_view(key_vectors),
        preferred_element_type=jnp.float32,
    ) * (1.0 / math.sqrt(HDIM))
    return jnp.where(key_valid[None, None, :] > 0, scores, -1e30)


def attend_forward(pieces):
    queries, key_vectors, values, key_valid = pieces
    scores = masked_scores(queries, key_vectors, key_valid)
    row_max = jnp.max(scores, axis=-1, keepdims=True)
    exponent = jnp.exp(scores - row_max)
    row_total = jnp.sum(exponent, axis=-1, keepdims=True)
    probability = (exponent / row_total).astype(jnp.bfloat16)
    attended = jnp.einsum(
        "hqk,khd->qhd", probability, head_view(values), preferred_element_type=jnp.float32
    )
    return (attended.reshape(SEQ, D).astype(jnp.bfloat16), (row_max + jnp.log(row_total))[:, :, 0])


def attend_backward(pieces):
    queries, key_vectors, values, key_valid, log_total, attended_grad = pieces
    scores = masked_scores(queries, key_vectors, key_valid)
    probability = jnp.exp(scores - log_total[:, :, None])
    probability_low = probability.astype(jnp.bfloat16)
    grad_heads = head_view(attended_grad)
    value_grad = jnp.einsum(
        "hqk,qhd->khd", probability_low, grad_heads, preferred_element_type=jnp.float32
    )
    probability_grad = jnp.einsum(
        "qhd,khd->hqk", grad_heads, head_view(values), preferred_element_type=jnp.float32
    )
    inner_total = jnp.sum(probability * probability_grad, axis=-1, keepdims=True)
    score_grad = (probability * (probability_grad - inner_total)).astype(jnp.bfloat16)
    score_scale = 1.0 / math.sqrt(HDIM)
    query_grad = (
        jnp.einsum(
            "hqk,khd->qhd", score_grad, head_view(key_vectors), preferred_element_type=jnp.float32
        )
        * score_scale
    )
    key_grad = (
        jnp.einsum(
            "hqk,qhd->khd", score_grad, head_view(queries), preferred_element_type=jnp.float32
        )
        * score_scale
    )
    return (
        query_grad.reshape(SEQ, D).astype(jnp.bfloat16),
        key_grad.reshape(SEQ, D).astype(jnp.bfloat16),
        value_grad.reshape(SEQ, D).astype(jnp.bfloat16),
    )


def adam_step(master, first_moment, second, gradient, step_rate, decay_rate, step_float):
    first_new = beta_first * first_moment + (1.0 - beta_first) * gradient
    second_new = beta_second * second + (1.0 - beta_second) * gradient * gradient
    first_hat = first_new / (1.0 - beta_first**step_float)
    second_hat = second_new / (1.0 - beta_second**step_float)
    master_new = master - step_rate * (
        first_hat / (jnp.sqrt(second_hat) + adam_epsilon) + decay_rate * master
    )
    return (master_new, first_new, second_new)


def padded_rows(rows, multiple):
    return -(-rows // multiple) * multiple


def gather_working(attention_master, feed_master, small_master):
    attention_rows = attention_master.shape[0]
    feed_rows = feed_master.shape[0]
    small_count = small_master.shape[0]
    main_rows = attention_rows + feed_rows
    extra_rows = padded_rows(main_rows + padded_rows(small_count, D) // D, 16) - main_rows
    small_flat = jnp.zeros((extra_rows * D,), jnp.bfloat16)
    small_flat = small_flat.at[:small_count].set(small_master.astype(jnp.bfloat16))
    block = jnp.concatenate(
        [
            attention_master.astype(jnp.bfloat16),
            feed_master.astype(jnp.bfloat16),
            small_flat.reshape(extra_rows, D),
        ],
        axis=0,
    )
    gathered = lax.all_gather(block, ("fsdp", "dp"), axis=0, tiled=False)
    owners = gathered.shape[0]
    attention_full = gathered[:, :attention_rows].reshape(owners * attention_rows, D)
    feed_full = gathered[:, attention_rows:main_rows].reshape(owners * feed_rows, D)
    small_full = gathered[:, main_rows:].reshape(owners, extra_rows * D)[:, :small_count]
    return attention_full, feed_full, small_full.reshape(owners * small_count)


def scatter_gradients(attention_pieces, feed_pieces, small_grad_all, partials):
    owners = lax.psum(1, ("fsdp", "dp"))
    me = lax.axis_index(("fsdp", "dp"))
    attention_grad_all = jnp.concatenate(attention_pieces, axis=0).astype(jnp.bfloat16)
    feed_grad_all = jnp.concatenate(feed_pieces, axis=0).astype(jnp.bfloat16)
    attention_rows = attention_grad_all.shape[0] // owners
    feed_rows = feed_grad_all.shape[0] // owners
    small_count = small_grad_all.shape[0] // owners
    main_rows = attention_rows + feed_rows
    partials_high = partials.astype(jnp.bfloat16)
    partials_low = (partials - partials_high.astype(jnp.float32)).astype(jnp.bfloat16)
    split_partials = jnp.concatenate([partials_high, partials_low])
    slots = split_partials.shape[0]
    extra_count = small_count + owners * slots
    extra_rows = padded_rows(main_rows + padded_rows(extra_count, D) // D, 16) - main_rows
    slot_row = jnp.zeros((owners * slots,), jnp.bfloat16)
    slot_row = lax.dynamic_update_slice(slot_row, split_partials, (me * slots,))
    extra = jnp.concatenate(
        [
            small_grad_all.astype(jnp.bfloat16).reshape(owners, small_count),
            jnp.broadcast_to(slot_row[None], (owners, owners * slots)),
            jnp.zeros((owners, extra_rows * D - extra_count), jnp.bfloat16),
        ],
        axis=1,
    ).reshape(owners, extra_rows, D)
    packed = jnp.concatenate(
        [
            attention_grad_all.reshape(owners, attention_rows, D),
            feed_grad_all.reshape(owners, feed_rows, D),
            extra,
        ],
        axis=1,
    ).reshape(owners * (main_rows + extra_rows), D)
    owned = lax.psum_scatter(packed, ("fsdp", "dp"), scatter_dimension=0, tiled=True)
    attention_owned = owned[:attention_rows].astype(jnp.float32)
    feed_owned = owned[attention_rows:main_rows].astype(jnp.float32)
    extra_owned = owned[main_rows:].reshape(extra_rows * D).astype(jnp.float32)
    small_owned = extra_owned[:small_count]
    gathered_partials = extra_owned[small_count:extra_count].reshape(owners, slots)
    half = slots // 2
    totals = gathered_partials[0, :half] + gathered_partials[0, half:]
    for index in range(1, owners):
        totals = totals + (gathered_partials[index, :half] + gathered_partials[index, half:])
    return attention_owned, feed_owned, small_owned, totals


def on_device(
    tokens,
    cotangent,
    lengths,
    step_count,
    attention_master,
    attention_first,
    attention_second,
    feed_master,
    feed_first,
    feed_second,
    small_master,
    small_first,
    small_second,
):
    row_count = tokens.shape[0]
    sequence_count = row_count // SEQ
    attention_full, feed_full, small_full = gather_working(attention_master, feed_master, small_master)
    key_valid = (
        lax.broadcasted_iota(jnp.int32, (sequence_count, SEQ), 1) < lengths[:, None]
    ).astype(jnp.float32)
    token_valid = key_valid.reshape(row_count)
    (
        query_bias,
        value_bias,
        output_bias,
        inner_bias,
        outer_bias,
        first_gain,
        first_shift,
        second_gain,
        second_shift,
    ) = split_small(small_full)
    queries = (product(tokens, attention_full[0:D]) + query_bias).astype(jnp.bfloat16)
    key_vectors = product(tokens, attention_full[D : 2 * D]).astype(jnp.bfloat16)
    values = (product(tokens, attention_full[2 * D : 3 * D]) + value_bias).astype(jnp.bfloat16)
    seq_shape = (sequence_count, SEQ, D)
    attended, log_total = lax.map(
        attend_forward,
        (
            queries.reshape(seq_shape),
            key_vectors.reshape(seq_shape),
            values.reshape(seq_shape),
            key_valid,
        ),
    )
    attended = attended.reshape(row_count, D)
    branch_attention = product(attended, attention_full[3 * D : 4 * D]) + output_bias
    first_sum = tokens.astype(jnp.float32) + branch_attention
    normed = layer_norm(first_sum, first_gain, first_shift)
    normed_low = normed.astype(jnp.bfloat16)
    inner_sum = product_cols(normed_low, feed_full[0:FF]) + inner_bias
    active = gelu_exact(inner_sum).astype(jnp.bfloat16)
    branch_feed = product(active, feed_full[FF : 2 * FF]) + outer_bias
    residual = normed + branch_feed
    layer_out = layer_norm(residual, second_gain, second_shift).astype(jnp.bfloat16)
    column = token_valid[:, None]
    partials = jnp.stack(
        [
            jnp.sum(residual * residual * column),
            jnp.sum(branch_attention * branch_attention * column),
            jnp.sum(branch_feed * branch_feed * column),
            jnp.sum(token_valid),
        ]
    )
    query_weight = attention_full[0:D]
    key_weight = attention_full[D : 2 * D]
    value_weight = attention_full[2 * D : 3 * D]
    output_weight = attention_full[3 * D : 4 * D]
    outer_weight = feed_full[FF : 2 * FF]
    inner_weight = feed_full[0:FF]
    second_pull = jax.vjp(layer_norm, residual, second_gain, second_shift)[1]
    residual_grad, second_gain_grad, second_shift_grad = second_pull(cotangent)
    feed_out_grad = residual_grad.astype(jnp.bfloat16)
    outer_bias_grad = column_total(feed_out_grad)
    outer_weight_grad = product_rows(active, feed_out_grad)
    active_grad = product_cols(feed_out_grad, outer_weight)
    inner_grad = jax.vjp(gelu_exact, inner_sum)[1](active_grad)[0].astype(jnp.bfloat16)
    inner_bias_grad = column_total(inner_grad)
    inner_weight_grad = product_rows(inner_grad, normed_low)
    normed_grad = residual_grad + product(inner_grad, inner_weight)
    first_pull = jax.vjp(layer_norm, first_sum, first_gain, first_shift)[1]
    first_sum_grad, first_gain_grad, first_shift_grad = first_pull(normed_grad)
    branch_grad_low = first_sum_grad.astype(jnp.bfloat16)
    output_bias_grad = column_total(branch_grad_low)
    output_weight_grad = product_rows(attended, branch_grad_low)
    attended_grad = product_cols(branch_grad_low, output_weight).astype(jnp.bfloat16)
    query_grad, key_grad, value_grad = lax.map(
        attend_backward,
        (
            queries.reshape(seq_shape),
            key_vectors.reshape(seq_shape),
            values.reshape(seq_shape),
            key_valid,
            log_total,
            attended_grad.reshape(seq_shape),
        ),
    )
    query_grad = query_grad.reshape(row_count, D)
    key_grad = key_grad.reshape(row_count, D)
    value_grad = value_grad.reshape(row_count, D)
    query_weight_grad = product_rows(tokens, query_grad)
    key_weight_grad = product_rows(tokens, key_grad)
    value_weight_grad = product_rows(tokens, value_grad)
    query_bias_grad = column_total(query_grad)
    value_bias_grad = column_total(value_grad)
    tokens_grad = (
        first_sum_grad
        + product_cols(query_grad, query_weight)
        + product_cols(key_grad, key_weight)
        + product_cols(value_grad, value_weight)
    )
    small_grad_all = jnp.concatenate(
        [
            query_bias_grad,
            value_bias_grad,
            output_bias_grad,
            inner_bias_grad,
            outer_bias_grad,
            first_gain_grad,
            first_shift_grad,
            second_gain_grad,
            second_shift_grad,
        ]
    )
    attention_owned, feed_owned, small_owned, totals = scatter_gradients(
        [query_weight_grad, key_weight_grad, value_weight_grad, output_weight_grad],
        [inner_weight_grad, outer_weight_grad],
        small_grad_all,
        partials,
    )
    rms_values = jnp.sqrt(totals[:3] / (totals[3] * D))
    step_float = step_count[0].astype(jnp.float32)
    attention_new, attention_first_new, attention_second_new = adam_step(
        attention_master,
        attention_first,
        attention_second,
        attention_owned,
        rate_matrix,
        weight_decay,
        step_float,
    )
    feed_new, feed_first_new, feed_second_new = adam_step(
        feed_master, feed_first, feed_second, feed_owned, rate_matrix, weight_decay, step_float
    )
    small_new, small_first_new, small_second_new = adam_step(
        small_master, small_first, small_second, small_owned, rate_small, 0.0, step_float
    )
    return (
        layer_out,
        tokens_grad,
        attention_new,
        attention_first_new,
        attention_second_new,
        attention_new.astype(jnp.bfloat16),
        feed_new,
        feed_first_new,
        feed_second_new,
        feed_new.astype(jnp.bfloat16),
        small_new,
        small_first_new,
        small_second_new,
        small_new.astype(jnp.bfloat16),
        rms_values,
    )


def solution(mesh):
    placed = (
        P(("fsdp", "dp"), None),
        P(("fsdp", "dp"), None),
        P(("fsdp", "dp")),
        P(),
        P(("fsdp", "dp"), None),
        P(("fsdp", "dp"), None),
        P(("fsdp", "dp"), None),
        P(("fsdp", "dp"), None),
        P(("fsdp", "dp"), None),
        P(("fsdp", "dp"), None),
        P(("fsdp", "dp")),
        P(("fsdp", "dp")),
        P(("fsdp", "dp")),
    )
    return jax.shard_map(
        on_device,
        mesh=mesh,
        in_specs=placed,
        out_specs=(
            P(("fsdp", "dp"), None),
            P(("fsdp", "dp"), None),
            P(("fsdp", "dp"), None),
            P(("fsdp", "dp"), None),
            P(("fsdp", "dp"), None),
            P(("fsdp", "dp"), None),
            P(("fsdp", "dp"), None),
            P(("fsdp", "dp"), None),
            P(("fsdp", "dp"), None),
            P(("fsdp", "dp"), None),
            P(("fsdp", "dp")),
            P(("fsdp", "dp")),
            P(("fsdp", "dp")),
            P(("fsdp", "dp")),
            P(),
        ),
        check_vma=False,
    )
```

```python
import functools
import math

import jax
import jax.numpy as jnp
from jax import lax
from jax.sharding import PartitionSpec as P

D = 768
HEADS = 12
HDIM = 64
FF = 3072
SEQ = 512


ln_epsilon = 1e-12
beta_first = 0.5
beta_second = 0.55
adam_epsilon = 1e-06
rate_matrix = 0.04
rate_small = 0.25
weight_decay = 0.01


def product(left_side, right_side):
    return jnp.dot(left_side, right_side, preferred_element_type=jnp.float32)


def product_rows(left_side, right_side):
    return lax.dot_general(
        left_side, right_side, (((0,), (0,)), ((), ())), preferred_element_type=jnp.float32
    )


def product_cols(left_side, right_side):
    return lax.dot_general(
        left_side, right_side, (((1,), (1,)), ((), ())), preferred_element_type=jnp.float32
    )


def column_total(entries):
    return jnp.sum(entries, axis=0, dtype=jnp.float32)


def layer_norm(entries, norm_gain, norm_shift):
    center = jnp.mean(entries, axis=-1, keepdims=True)
    offset = entries - center
    spread = jnp.mean(offset * offset, axis=-1, keepdims=True)
    return offset * lax.rsqrt(spread + ln_epsilon) * norm_gain + norm_shift


def gelu_exact(entries):
    return jax.nn.gelu(entries, approximate=False)


def split_small(small_full):
    pieces = []
    position = 0
    for length in (D, D, D, FF, D, D, D, D, D):
        pieces.append(small_full[position : position + length].astype(jnp.float32))
        position = position + length
    return pieces


def head_view(entries):
    return entries.reshape(SEQ, HEADS, HDIM)


def masked_scores(queries, key_vectors, key_valid):
    scores = jnp.einsum(
        "qhd,khd->hqk",
        head_view(queries),
        head_view(key_vectors),
        preferred_element_type=jnp.float32,
    ) * (1.0 / math.sqrt(HDIM))
    return jnp.where(key_valid[None, None, :] > 0, scores, -1e30)


def attend_forward(pieces):
    queries, key_vectors, values, key_valid = pieces
    scores = masked_scores(queries, key_vectors, key_valid)
    row_max = jnp.max(scores, axis=-1, keepdims=True)
    exponent = jnp.exp(scores - row_max)
    row_total = jnp.sum(exponent, axis=-1, keepdims=True)
    probability = (exponent / row_total).astype(jnp.bfloat16)
    attended = jnp.einsum(
        "hqk,khd->qhd", probability, head_view(values), preferred_element_type=jnp.float32
    )
    return (attended.reshape(SEQ, D).astype(jnp.bfloat16), (row_max + jnp.log(row_total))[:, :, 0])


def attend_backward(pieces):
    queries, key_vectors, values, key_valid, log_total, attended_grad = pieces
    scores = masked_scores(queries, key_vectors, key_valid)
    probability = jnp.exp(scores - log_total[:, :, None])
    probability_low = probability.astype(jnp.bfloat16)
    grad_heads = head_view(attended_grad)
    value_grad = jnp.einsum(
        "hqk,qhd->khd", probability_low, grad_heads, preferred_element_type=jnp.float32
    )
    probability_grad = jnp.einsum(
        "qhd,khd->hqk", grad_heads, head_view(values), preferred_element_type=jnp.float32
    )
    inner_total = jnp.sum(probability * probability_grad, axis=-1, keepdims=True)
    score_grad = (probability * (probability_grad - inner_total)).astype(jnp.bfloat16)
    score_scale = 1.0 / math.sqrt(HDIM)
    query_grad = (
        jnp.einsum(
            "hqk,khd->qhd", score_grad, head_view(key_vectors), preferred_element_type=jnp.float32
        )
        * score_scale
    )
    key_grad = (
        jnp.einsum(
            "hqk,qhd->khd", score_grad, head_view(queries), preferred_element_type=jnp.float32
        )
        * score_scale
    )
    return (
        query_grad.reshape(SEQ, D).astype(jnp.bfloat16),
        key_grad.reshape(SEQ, D).astype(jnp.bfloat16),
        value_grad.reshape(SEQ, D).astype(jnp.bfloat16),
    )


def adam_step(master, first_moment, second, gradient, step_rate, decay_rate, step_float):
    first_new = beta_first * first_moment + (1.0 - beta_first) * gradient
    second_new = beta_second * second + (1.0 - beta_second) * gradient * gradient
    first_hat = first_new / (1.0 - beta_first**step_float)
    second_hat = second_new / (1.0 - beta_second**step_float)
    master_new = master - step_rate * (
        first_hat / (jnp.sqrt(second_hat) + adam_epsilon) + decay_rate * master
    )
    return (master_new, first_new, second_new)


def padded_rows(rows, multiple):
    return -(-rows // multiple) * multiple


def gather_working(attention_master, feed_master, small_master):
    attention_rows = attention_master.shape[0]
    feed_rows = feed_master.shape[0]
    small_count = small_master.shape[0]
    main_rows = attention_rows + feed_rows
    extra_rows = padded_rows(main_rows + padded_rows(small_count, D) // D, 16) - main_rows
    small_flat = jnp.zeros((extra_rows * D,), jnp.bfloat16)
    small_flat = small_flat.at[:small_count].set(small_master.astype(jnp.bfloat16))
    block = jnp.concatenate(
        [
            attention_master.astype(jnp.bfloat16),
            feed_master.astype(jnp.bfloat16),
            small_flat.reshape(extra_rows, D),
        ],
        axis=0,
    )
    gathered = lax.all_gather(block, ("fsdp", "dp"), axis=0, tiled=False)
    owners = gathered.shape[0]
    attention_full = gathered[:, :attention_rows].reshape(owners * attention_rows, D)
    feed_full = gathered[:, attention_rows:main_rows].reshape(owners * feed_rows, D)
    small_full = gathered[:, main_rows:].reshape(owners, extra_rows * D)[:, :small_count]
    return attention_full, feed_full, small_full.reshape(owners * small_count)


def exchange_half(arrays, own, axis_dim, axis_name, pairs):
    combined = []
    for entries in arrays:
        keep = lax.dynamic_index_in_dim(entries, own, axis=axis_dim, keepdims=False)
        send = lax.dynamic_index_in_dim(entries, 1 - own, axis=axis_dim, keepdims=False)
        received = lax.ppermute(send.astype(jnp.bfloat16), axis_name, pairs)
        combined.append(keep.astype(jnp.float32) + received.astype(jnp.float32))
    return combined


def line_reduce(entries, place, length, stride, size, axis_name):
    zero = jnp.zeros(entries.shape[1:], jnp.float32)
    from_left, from_right = zero, zero
    for step in range(1, length):
        rightward = [
            (f, f + stride) for f in range(size) if (f // stride) % length <= step - 1 and (f // stride) % length < length - 1
        ]
        leftward = [
            (f, f - stride) for f in range(size) if (f // stride) % length >= length - step and (f // stride) % length > 0
        ]
        right_target = jnp.minimum(place + length - step, length - 1)
        left_target = jnp.maximum(place - length + step, 0)
        right_value = lax.dynamic_index_in_dim(entries, right_target, axis=0, keepdims=False) + from_left
        left_value = lax.dynamic_index_in_dim(entries, left_target, axis=0, keepdims=False) + from_right
        from_left = lax.ppermute(right_value.astype(jnp.bfloat16), axis_name, rightward).astype(jnp.float32)
        from_right = lax.ppermute(left_value.astype(jnp.bfloat16), axis_name, leftward).astype(jnp.float32)
    return lax.dynamic_index_in_dim(entries, place, axis=0, keepdims=False) + from_left + from_right


def staged_reduce_scatter(packed):
    fsdp = lax.axis_index("fsdp")
    dp = lax.axis_index("dp")
    core, x_place, z_place = fsdp % 2, (fsdp // 2) % 2, fsdp // 4
    rows, columns = packed.shape[1], packed.shape[2]
    blocks = packed.reshape(4, 2, 2, 2, rows, columns)
    (after_core,) = exchange_half([blocks], core, 2, "fsdp", [(f, f ^ 1) for f in range(16)])
    half = columns // 2
    first, second = after_core[..., :half], after_core[..., half:]
    (first,) = exchange_half([first], x_place, 1, "fsdp", [(f, f ^ 2) for f in range(16)])
    (second,) = exchange_half([second], dp, 2, "dp", [(0, 1), (1, 0)])
    (first,) = exchange_half([first], dp, 1, "dp", [(0, 1), (1, 0)])
    (second,) = exchange_half([second], x_place, 1, "fsdp", [(f, f ^ 2) for f in range(16)])
    along_z = jnp.concatenate([first, second], axis=-1)
    return line_reduce(along_z, z_place, 4, 4, 16, "fsdp")


def scatter_gradients(attention_pieces, feed_pieces, small_grad_all, partials, staged):
    owners = lax.psum(1, ("fsdp", "dp"))
    me = lax.axis_index(("fsdp", "dp"))
    attention_rows = sum(piece.shape[0] for piece in attention_pieces) // owners
    feed_rows = sum(piece.shape[0] for piece in feed_pieces) // owners
    small_count = small_grad_all.shape[0] // owners
    feed_grad_all = jnp.concatenate(feed_pieces, axis=0).astype(jnp.bfloat16)
    feed_owned = lax.psum_scatter(feed_grad_all, ("fsdp", "dp"), scatter_dimension=0, tiled=True)
    partials_high = partials.astype(jnp.bfloat16)
    partials_low = (partials - partials_high.astype(jnp.float32)).astype(jnp.bfloat16)
    split_partials = jnp.concatenate([partials_high, partials_low])
    slots = split_partials.shape[0]
    extra_count = small_count + owners * slots
    extra_rows = padded_rows(attention_rows + padded_rows(extra_count, D) // D, 16) - attention_rows
    slot_row = jnp.zeros((owners * slots,), jnp.bfloat16)
    slot_row = lax.dynamic_update_slice(slot_row, split_partials, (me * slots,))
    extra = jnp.concatenate(
        [
            small_grad_all.astype(jnp.bfloat16).reshape(owners, small_count),
            jnp.broadcast_to(slot_row[None], (owners, owners * slots)),
            jnp.zeros((owners, extra_rows * D - extra_count), jnp.bfloat16),
        ],
        axis=1,
    ).reshape(owners, extra_rows, D)
    block_rows = attention_rows + extra_rows
    packed = jnp.zeros((owners, block_rows, D), jnp.bfloat16)
    packed = lax.dynamic_update_slice(packed, extra, (0, attention_rows, 0))
    owner = 0
    for piece in attention_pieces:
        piece_owners = piece.shape[0] // attention_rows
        packed = lax.dynamic_update_slice(
            packed, piece.astype(jnp.bfloat16).reshape(piece_owners, attention_rows, D), (owner, 0, 0)
        )
        owner = owner + piece_owners
    if staged:
        owned = staged_reduce_scatter(packed)
    else:
        owned = lax.psum_scatter(
            packed.reshape(owners * block_rows, D), ("fsdp", "dp"), scatter_dimension=0, tiled=True
        ).astype(jnp.float32)
    attention_owned = owned[:attention_rows]
    extra_owned = owned[attention_rows:].reshape(extra_rows * D)
    small_owned = extra_owned[:small_count]
    gathered_partials = extra_owned[small_count:extra_count].reshape(owners, slots)
    half = slots // 2
    totals = gathered_partials[0, :half] + gathered_partials[0, half:]
    for index in range(1, owners):
        totals = totals + (gathered_partials[index, :half] + gathered_partials[index, half:])
    return attention_owned, feed_owned.astype(jnp.float32), small_owned, totals


def on_device(
    staged,
    tokens,
    cotangent,
    lengths,
    step_count,
    attention_master,
    attention_first,
    attention_second,
    feed_master,
    feed_first,
    feed_second,
    small_master,
    small_first,
    small_second,
):
    row_count = tokens.shape[0]
    sequence_count = row_count // SEQ
    attention_full, feed_full, small_full = gather_working(attention_master, feed_master, small_master)
    key_valid = (
        lax.broadcasted_iota(jnp.int32, (sequence_count, SEQ), 1) < lengths[:, None]
    ).astype(jnp.float32)
    token_valid = key_valid.reshape(row_count)
    (
        query_bias,
        value_bias,
        output_bias,
        inner_bias,
        outer_bias,
        first_gain,
        first_shift,
        second_gain,
        second_shift,
    ) = split_small(small_full)
    queries = (product(tokens, attention_full[0:D]) + query_bias).astype(jnp.bfloat16)
    key_vectors = product(tokens, attention_full[D : 2 * D]).astype(jnp.bfloat16)
    values = (product(tokens, attention_full[2 * D : 3 * D]) + value_bias).astype(jnp.bfloat16)
    seq_shape = (sequence_count, SEQ, D)
    attended, log_total = lax.map(
        attend_forward,
        (
            queries.reshape(seq_shape),
            key_vectors.reshape(seq_shape),
            values.reshape(seq_shape),
            key_valid,
        ),
    )
    attended = attended.reshape(row_count, D)
    branch_attention = product(attended, attention_full[3 * D : 4 * D]) + output_bias
    first_sum = tokens.astype(jnp.float32) + branch_attention
    normed = layer_norm(first_sum, first_gain, first_shift)
    normed_low = normed.astype(jnp.bfloat16)
    inner_sum = product_cols(normed_low, feed_full[0:FF]) + inner_bias
    active = gelu_exact(inner_sum).astype(jnp.bfloat16)
    branch_feed = product(active, feed_full[FF : 2 * FF]) + outer_bias
    residual = normed + branch_feed
    layer_out = layer_norm(residual, second_gain, second_shift).astype(jnp.bfloat16)
    column = token_valid[:, None]
    partials = jnp.stack(
        [
            jnp.sum(residual * residual * column),
            jnp.sum(branch_attention * branch_attention * column),
            jnp.sum(branch_feed * branch_feed * column),
            jnp.sum(token_valid),
        ]
    )
    query_weight = attention_full[0:D]
    key_weight = attention_full[D : 2 * D]
    value_weight = attention_full[2 * D : 3 * D]
    output_weight = attention_full[3 * D : 4 * D]
    outer_weight = feed_full[FF : 2 * FF]
    inner_weight = feed_full[0:FF]
    second_pull = jax.vjp(layer_norm, residual, second_gain, second_shift)[1]
    residual_grad, second_gain_grad, second_shift_grad = second_pull(cotangent)
    feed_out_grad = residual_grad.astype(jnp.bfloat16)
    outer_bias_grad = column_total(feed_out_grad)
    outer_weight_grad = product_rows(active, feed_out_grad)
    active_grad = product_cols(feed_out_grad, outer_weight)
    inner_grad = jax.vjp(gelu_exact, inner_sum)[1](active_grad)[0].astype(jnp.bfloat16)
    inner_bias_grad = column_total(inner_grad)
    inner_weight_grad = product_rows(inner_grad, normed_low)
    normed_grad = residual_grad + product(inner_grad, inner_weight)
    first_pull = jax.vjp(layer_norm, first_sum, first_gain, first_shift)[1]
    first_sum_grad, first_gain_grad, first_shift_grad = first_pull(normed_grad)
    branch_grad_low = first_sum_grad.astype(jnp.bfloat16)
    output_bias_grad = column_total(branch_grad_low)
    output_weight_grad = product_rows(attended, branch_grad_low)
    attended_grad = product_cols(branch_grad_low, output_weight).astype(jnp.bfloat16)
    query_grad, key_grad, value_grad = lax.map(
        attend_backward,
        (
            queries.reshape(seq_shape),
            key_vectors.reshape(seq_shape),
            values.reshape(seq_shape),
            key_valid,
            log_total,
            attended_grad.reshape(seq_shape),
        ),
    )
    query_grad = query_grad.reshape(row_count, D)
    key_grad = key_grad.reshape(row_count, D)
    value_grad = value_grad.reshape(row_count, D)
    query_weight_grad = product_rows(tokens, query_grad)
    key_weight_grad = product_rows(tokens, key_grad)
    value_weight_grad = product_rows(tokens, value_grad)
    query_bias_grad = column_total(query_grad)
    value_bias_grad = column_total(value_grad)
    tokens_grad = (
        first_sum_grad
        + product_cols(query_grad, query_weight)
        + product_cols(key_grad, key_weight)
        + product_cols(value_grad, value_weight)
    )
    small_grad_all = jnp.concatenate(
        [
            query_bias_grad,
            value_bias_grad,
            output_bias_grad,
            inner_bias_grad,
            outer_bias_grad,
            first_gain_grad,
            first_shift_grad,
            second_gain_grad,
            second_shift_grad,
        ]
    )
    attention_owned, feed_owned, small_owned, totals = scatter_gradients(
        [query_weight_grad, key_weight_grad, value_weight_grad, output_weight_grad],
        [inner_weight_grad, outer_weight_grad],
        small_grad_all,
        partials,
        staged,
    )
    rms_values = jnp.sqrt(totals[:3] / (totals[3] * D))
    step_float = step_count[0].astype(jnp.float32)
    attention_new, attention_first_new, attention_second_new = adam_step(
        attention_master,
        attention_first,
        attention_second,
        attention_owned,
        rate_matrix,
        weight_decay,
        step_float,
    )
    feed_new, feed_first_new, feed_second_new = adam_step(
        feed_master, feed_first, feed_second, feed_owned, rate_matrix, weight_decay, step_float
    )
    small_new, small_first_new, small_second_new = adam_step(
        small_master, small_first, small_second, small_owned, rate_small, 0.0, step_float
    )
    return (
        layer_out,
        tokens_grad,
        attention_new,
        attention_first_new,
        attention_second_new,
        attention_new.astype(jnp.bfloat16),
        feed_new,
        feed_first_new,
        feed_second_new,
        feed_new.astype(jnp.bfloat16),
        small_new,
        small_first_new,
        small_second_new,
        small_new.astype(jnp.bfloat16),
        rms_values,
    )


def solution(mesh):
    placed = (
        P(("fsdp", "dp"), None),
        P(("fsdp", "dp"), None),
        P(("fsdp", "dp")),
        P(),
        P(("fsdp", "dp"), None),
        P(("fsdp", "dp"), None),
        P(("fsdp", "dp"), None),
        P(("fsdp", "dp"), None),
        P(("fsdp", "dp"), None),
        P(("fsdp", "dp"), None),
        P(("fsdp", "dp")),
        P(("fsdp", "dp")),
        P(("fsdp", "dp")),
    )
    staged = dict(mesh.shape) == {"fsdp": 16, "dp": 2}
    return jax.shard_map(
        functools.partial(on_device, staged),
        mesh=mesh,
        in_specs=placed,
        out_specs=(
            P(("fsdp", "dp"), None),
            P(("fsdp", "dp"), None),
            P(("fsdp", "dp"), None),
            P(("fsdp", "dp"), None),
            P(("fsdp", "dp"), None),
            P(("fsdp", "dp"), None),
            P(("fsdp", "dp"), None),
            P(("fsdp", "dp"), None),
            P(("fsdp", "dp"), None),
            P(("fsdp", "dp"), None),
            P(("fsdp", "dp")),
            P(("fsdp", "dp")),
            P(("fsdp", "dp")),
            P(("fsdp", "dp")),
            P(),
        ),
        check_vma=False,
    )
```

```python
import functools
import math

import jax
import jax.numpy as jnp
from jax import lax
from jax.sharding import PartitionSpec as P

D = 768
HEADS = 12
HDIM = 64
FF = 3072
SEQ = 512


ln_epsilon = 1e-12
beta_first = 0.5
beta_second = 0.55
adam_epsilon = 1e-06
rate_matrix = 0.04
rate_small = 0.25
weight_decay = 0.01


def product(left_side, right_side):
    return jnp.dot(left_side, right_side, preferred_element_type=jnp.float32)


def product_rows(left_side, right_side):
    return lax.dot_general(
        left_side, right_side, (((0,), (0,)), ((), ())), preferred_element_type=jnp.float32
    )


def product_cols(left_side, right_side):
    return lax.dot_general(
        left_side, right_side, (((1,), (1,)), ((), ())), preferred_element_type=jnp.float32
    )


def column_total(entries):
    return jnp.sum(entries, axis=0, dtype=jnp.float32)


def layer_norm(entries, norm_gain, norm_shift):
    center = jnp.mean(entries, axis=-1, keepdims=True)
    offset = entries - center
    spread = jnp.mean(offset * offset, axis=-1, keepdims=True)
    return offset * lax.rsqrt(spread + ln_epsilon) * norm_gain + norm_shift


def gelu_exact(entries):
    return jax.nn.gelu(entries, approximate=False)


def split_small(small_full):
    pieces = []
    position = 0
    for length in (D, D, D, FF, D, D, D, D, D):
        pieces.append(small_full[position : position + length].astype(jnp.float32))
        position = position + length
    return pieces


def head_view(entries):
    return entries.reshape(SEQ, HEADS, HDIM)


def masked_scores(queries, key_vectors, key_valid):
    scores = jnp.einsum(
        "qhd,khd->hqk",
        head_view(queries),
        head_view(key_vectors),
        preferred_element_type=jnp.float32,
    ) * (1.0 / math.sqrt(HDIM))
    return jnp.where(key_valid[None, None, :] > 0, scores, -1e30)


def attend_forward(pieces):
    queries, key_vectors, values, key_valid = pieces
    scores = masked_scores(queries, key_vectors, key_valid)
    row_max = jnp.max(scores, axis=-1, keepdims=True)
    exponent = jnp.exp(scores - row_max)
    row_total = jnp.sum(exponent, axis=-1, keepdims=True)
    probability = (exponent / row_total).astype(jnp.bfloat16)
    attended = jnp.einsum(
        "hqk,khd->qhd", probability, head_view(values), preferred_element_type=jnp.float32
    )
    return (attended.reshape(SEQ, D).astype(jnp.bfloat16), (row_max + jnp.log(row_total))[:, :, 0])


def attend_backward(pieces):
    queries, key_vectors, values, key_valid, log_total, attended_grad = pieces
    scores = masked_scores(queries, key_vectors, key_valid)
    probability = jnp.exp(scores - log_total[:, :, None])
    probability_low = probability.astype(jnp.bfloat16)
    grad_heads = head_view(attended_grad)
    value_grad = jnp.einsum(
        "hqk,qhd->khd", probability_low, grad_heads, preferred_element_type=jnp.float32
    )
    probability_grad = jnp.einsum(
        "qhd,khd->hqk", grad_heads, head_view(values), preferred_element_type=jnp.float32
    )
    inner_total = jnp.sum(probability * probability_grad, axis=-1, keepdims=True)
    score_grad = (probability * (probability_grad - inner_total)).astype(jnp.bfloat16)
    score_scale = 1.0 / math.sqrt(HDIM)
    query_grad = (
        jnp.einsum(
            "hqk,khd->qhd", score_grad, head_view(key_vectors), preferred_element_type=jnp.float32
        )
        * score_scale
    )
    key_grad = (
        jnp.einsum(
            "hqk,qhd->khd", score_grad, head_view(queries), preferred_element_type=jnp.float32
        )
        * score_scale
    )
    return (
        query_grad.reshape(SEQ, D).astype(jnp.bfloat16),
        key_grad.reshape(SEQ, D).astype(jnp.bfloat16),
        value_grad.reshape(SEQ, D).astype(jnp.bfloat16),
    )


def adam_step(master, first_moment, second, gradient, step_rate, decay_rate, step_float):
    first_new = beta_first * first_moment + (1.0 - beta_first) * gradient
    second_new = beta_second * second + (1.0 - beta_second) * gradient * gradient
    first_hat = first_new / (1.0 - beta_first**step_float)
    second_hat = second_new / (1.0 - beta_second**step_float)
    master_new = master - step_rate * (
        first_hat / (jnp.sqrt(second_hat) + adam_epsilon) + decay_rate * master
    )
    return (master_new, first_new, second_new)


def padded_rows(rows, multiple):
    return -(-rows // multiple) * multiple


def gather_working(attention_master, feed_master, small_master):
    attention_rows = attention_master.shape[0]
    feed_rows = feed_master.shape[0]
    small_count = small_master.shape[0]
    main_rows = attention_rows + feed_rows
    extra_rows = padded_rows(main_rows + padded_rows(small_count, D) // D, 16) - main_rows
    small_flat = jnp.zeros((extra_rows * D,), jnp.bfloat16)
    small_flat = small_flat.at[:small_count].set(small_master.astype(jnp.bfloat16))
    block = jnp.concatenate(
        [
            attention_master.astype(jnp.bfloat16),
            feed_master.astype(jnp.bfloat16),
            small_flat.reshape(extra_rows, D),
        ],
        axis=0,
    )
    gathered = lax.all_gather(block, ("fsdp", "dp"), axis=0, tiled=False)
    owners = gathered.shape[0]
    attention_full = gathered[:, :attention_rows].reshape(owners * attention_rows, D)
    feed_full = gathered[:, attention_rows:main_rows].reshape(owners * feed_rows, D)
    small_full = gathered[:, main_rows:].reshape(owners, extra_rows * D)[:, :small_count]
    return attention_full, feed_full, small_full.reshape(owners * small_count)


def exchange_half(arrays, own, axis_dim, axis_name, pairs):
    combined = []
    for entries in arrays:
        keep = lax.dynamic_index_in_dim(entries, own, axis=axis_dim, keepdims=False)
        send = lax.dynamic_index_in_dim(entries, 1 - own, axis=axis_dim, keepdims=False)
        received = lax.ppermute(send.astype(jnp.bfloat16), axis_name, pairs)
        combined.append(keep.astype(jnp.float32) + received.astype(jnp.float32))
    return combined


def line_reduce(entries, place, length, stride, size, axis_name):
    zero = jnp.zeros(entries.shape[1:], jnp.float32)
    from_left, from_right = zero, zero
    for step in range(1, length):
        rightward = [
            (f, f + stride) for f in range(size) if (f // stride) % length <= step - 1 and (f // stride) % length < length - 1
        ]
        leftward = [
            (f, f - stride) for f in range(size) if (f // stride) % length >= length - step and (f // stride) % length > 0
        ]
        right_target = jnp.minimum(place + length - step, length - 1)
        left_target = jnp.maximum(place - length + step, 0)
        right_value = lax.dynamic_index_in_dim(entries, right_target, axis=0, keepdims=False) + from_left
        left_value = lax.dynamic_index_in_dim(entries, left_target, axis=0, keepdims=False) + from_right
        from_left = lax.ppermute(right_value.astype(jnp.bfloat16), axis_name, rightward).astype(jnp.float32)
        from_right = lax.ppermute(left_value.astype(jnp.bfloat16), axis_name, leftward).astype(jnp.float32)
    return lax.dynamic_index_in_dim(entries, place, axis=0, keepdims=False) + from_left + from_right


def staged_reduce_scatter(arrays):
    fsdp = lax.axis_index("fsdp")
    dp = lax.axis_index("dp")
    core, x_place, z_place = fsdp % 2, (fsdp // 2) % 2, fsdp // 4
    x_pairs = [(f, f ^ 2) for f in range(16)]
    y_pairs = [(0, 1), (1, 0)]
    blocks = [entries.reshape((4, 2, 2, 2) + entries.shape[1:]) for entries in arrays]
    after_core = exchange_half(blocks, core, 2, "fsdp", [(f, f ^ 1) for f in range(16)])
    half = arrays[0].shape[-1] // 2
    first = [entries[..., :half] for entries in after_core]
    second = [entries[..., half:] for entries in after_core]
    first = exchange_half(first, x_place, 1, "fsdp", x_pairs)
    second = exchange_half(second, dp, 2, "dp", y_pairs)
    first = exchange_half(first, dp, 1, "dp", y_pairs)
    second = exchange_half(second, x_place, 1, "fsdp", x_pairs)
    along_z = jnp.concatenate(
        [jnp.concatenate([a, b], axis=-1) for a, b in zip(first, second)], axis=1
    )
    return line_reduce(along_z, z_place, 4, 4, 16, "fsdp")


def place_along(entries, received, own, axis):
    size = entries.shape[axis]
    shape = list(entries.shape)
    shape[axis] = 2 * size
    start = [0] * len(shape)
    other = [0] * len(shape)
    start[axis] = own * size
    other[axis] = (1 - own) * size
    grown = jnp.zeros(shape, entries.dtype)
    grown = lax.dynamic_update_slice(grown, entries, start)
    return lax.dynamic_update_slice(grown, received, other)


def exchange_grow(entries, own, axis, axis_name, pairs):
    return place_along(entries, lax.ppermute(entries, axis_name, pairs), own, axis)


def line_gather(entries, place, length, stride, size, axis_name):
    slot = lax.broadcasted_iota(jnp.int32, (length,) + (1,) * (entries.ndim - 1), 0)
    grown = jnp.where(slot == place, entries, jnp.zeros((length,) + entries.shape[1:], entries.dtype))
    send_right, send_left = entries, entries
    for step in range(1, length):
        rightward = [
            (f, f + stride) for f in range(size) if step - 1 <= (f // stride) % length < length - 1
        ]
        leftward = [
            (f, f - stride) for f in range(size) if 0 < (f // stride) % length <= length - step
        ]
        send_right = lax.ppermute(send_right, axis_name, rightward)
        send_left = lax.ppermute(send_left, axis_name, leftward)
        grown = jnp.where(slot == place - step, send_right, grown)
        grown = jnp.where(slot == place + step, send_left, grown)
    return grown


def staged_all_gather(block):
    fsdp = lax.axis_index("fsdp")
    dp = lax.axis_index("dp")
    core, x_place, z_place = fsdp % 2, (fsdp // 2) % 2, fsdp // 4
    rows, columns = block.shape
    x_pairs = [(f, f ^ 2) for f in range(16)]
    y_pairs = [(0, 1), (1, 0)]
    grown = line_gather(block.reshape(1, 1, 1, 1, rows, columns), z_place, 4, 4, 16, "fsdp")
    half = columns // 2
    first, second = grown[..., :half], grown[..., half:]
    first = exchange_grow(first, dp, 3, "dp", y_pairs)
    second = exchange_grow(second, x_place, 1, "fsdp", x_pairs)
    first = exchange_grow(first, x_place, 1, "fsdp", x_pairs)
    second = exchange_grow(second, dp, 3, "dp", y_pairs)
    grown = jnp.concatenate([first, second], axis=-1)
    grown = exchange_grow(grown, core, 2, "fsdp", [(f, f ^ 1) for f in range(16)])
    return grown.reshape(32 * rows, columns)


def staged_working(attention_master, feed_master, small_master):
    small_count = small_master.shape[0]
    small_row = jnp.zeros((1, D), jnp.bfloat16).at[0, :small_count].set(small_master.astype(jnp.bfloat16))
    attention_full = staged_all_gather(attention_master.astype(jnp.bfloat16))
    small_full = staged_all_gather(small_row)[:, :small_count].reshape(32 * small_count)
    feed_full = lax.all_gather(feed_master.astype(jnp.bfloat16), ("fsdp", "dp"), axis=0, tiled=True)
    return attention_full, feed_full, small_full


def scatter_gradients(attention_pieces, feed_pieces, small_grad_all, partials, staged):
    owners = lax.psum(1, ("fsdp", "dp"))
    me = lax.axis_index(("fsdp", "dp"))
    attention_rows = sum(piece.shape[0] for piece in attention_pieces) // owners
    feed_rows = sum(piece.shape[0] for piece in feed_pieces) // owners
    small_count = small_grad_all.shape[0] // owners
    feed_grad_all = jnp.zeros((owners * feed_rows, D), jnp.bfloat16)
    start = 0
    for piece in feed_pieces:
        feed_grad_all = lax.dynamic_update_slice(feed_grad_all, piece.astype(jnp.bfloat16), (start, 0))
        start = start + piece.shape[0]
    feed_owned = lax.psum_scatter(feed_grad_all, ("fsdp", "dp"), scatter_dimension=0, tiled=True)
    partials_high = partials.astype(jnp.bfloat16)
    partials_low = (partials - partials_high.astype(jnp.float32)).astype(jnp.bfloat16)
    split_partials = jnp.concatenate([partials_high, partials_low])
    slots = split_partials.shape[0]
    extra_count = small_count + owners * slots
    extra_rows = padded_rows(attention_rows + padded_rows(extra_count, D) // D, 16) - attention_rows
    slot_row = jnp.zeros((owners * slots,), jnp.bfloat16)
    slot_row = lax.dynamic_update_slice(slot_row, split_partials, (me * slots,))
    extra = jnp.concatenate(
        [
            small_grad_all.astype(jnp.bfloat16).reshape(owners, small_count),
            jnp.broadcast_to(slot_row[None], (owners, owners * slots)),
            jnp.zeros((owners, extra_rows * D - extra_count), jnp.bfloat16),
        ],
        axis=1,
    ).reshape(owners, extra_rows, D)
    block_rows = attention_rows + extra_rows
    if staged:
        attention_grad_all = jnp.concatenate(attention_pieces, axis=0).astype(jnp.bfloat16)
        owned = staged_reduce_scatter(
            [attention_grad_all.reshape(owners, attention_rows, D), extra]
        )
    else:
        packed = jnp.zeros((owners, block_rows, D), jnp.bfloat16)
        packed = lax.dynamic_update_slice(packed, extra, (0, attention_rows, 0))
        owner = 0
        for piece in attention_pieces:
            piece_owners = piece.shape[0] // attention_rows
            packed = lax.dynamic_update_slice(
                packed, piece.astype(jnp.bfloat16).reshape(piece_owners, attention_rows, D), (owner, 0, 0)
            )
            owner = owner + piece_owners
        owned = lax.psum_scatter(
            packed.reshape(owners * block_rows, D), ("fsdp", "dp"), scatter_dimension=0, tiled=True
        ).astype(jnp.float32)
    attention_owned = owned[:attention_rows]
    extra_owned = owned[attention_rows:].reshape(extra_rows * D)
    small_owned = extra_owned[:small_count]
    gathered_partials = extra_owned[small_count:extra_count].reshape(owners, slots)
    half = slots // 2
    totals = gathered_partials[0, :half] + gathered_partials[0, half:]
    for index in range(1, owners):
        totals = totals + (gathered_partials[index, :half] + gathered_partials[index, half:])
    return attention_owned, feed_owned.astype(jnp.float32), small_owned, totals


def on_device(
    staged,
    tokens,
    cotangent,
    lengths,
    step_count,
    attention_master,
    attention_first,
    attention_second,
    feed_master,
    feed_first,
    feed_second,
    small_master,
    small_first,
    small_second,
):
    row_count = tokens.shape[0]
    sequence_count = row_count // SEQ
    if staged:
        attention_full, feed_full, small_full = staged_working(attention_master, feed_master, small_master)
    else:
        attention_full, feed_full, small_full = gather_working(attention_master, feed_master, small_master)
    key_valid = (
        lax.broadcasted_iota(jnp.int32, (sequence_count, SEQ), 1) < lengths[:, None]
    ).astype(jnp.float32)
    token_valid = key_valid.reshape(row_count)
    (
        query_bias,
        value_bias,
        output_bias,
        inner_bias,
        outer_bias,
        first_gain,
        first_shift,
        second_gain,
        second_shift,
    ) = split_small(small_full)
    queries = (product(tokens, attention_full[0:D]) + query_bias).astype(jnp.bfloat16)
    key_vectors = product(tokens, attention_full[D : 2 * D]).astype(jnp.bfloat16)
    values = (product(tokens, attention_full[2 * D : 3 * D]) + value_bias).astype(jnp.bfloat16)
    seq_shape = (sequence_count, SEQ, D)
    attended, log_total = lax.map(
        attend_forward,
        (
            queries.reshape(seq_shape),
            key_vectors.reshape(seq_shape),
            values.reshape(seq_shape),
            key_valid,
        ),
    )
    attended = attended.reshape(row_count, D)
    branch_attention = product(attended, attention_full[3 * D : 4 * D]) + output_bias
    first_sum = tokens.astype(jnp.float32) + branch_attention
    normed = layer_norm(first_sum, first_gain, first_shift)
    normed_low = normed.astype(jnp.bfloat16)
    inner_sum = product_cols(normed_low, feed_full[0:FF]) + inner_bias
    active = gelu_exact(inner_sum).astype(jnp.bfloat16)
    branch_feed = product(active, feed_full[FF : 2 * FF]) + outer_bias
    residual = normed + branch_feed
    layer_out = layer_norm(residual, second_gain, second_shift).astype(jnp.bfloat16)
    column = token_valid[:, None]
    partials = jnp.stack(
        [
            jnp.sum(residual * residual * column),
            jnp.sum(branch_attention * branch_attention * column),
            jnp.sum(branch_feed * branch_feed * column),
            jnp.sum(token_valid),
        ]
    )
    query_weight = attention_full[0:D]
    key_weight = attention_full[D : 2 * D]
    value_weight = attention_full[2 * D : 3 * D]
    output_weight = attention_full[3 * D : 4 * D]
    outer_weight = feed_full[FF : 2 * FF]
    inner_weight = feed_full[0:FF]
    second_pull = jax.vjp(layer_norm, residual, second_gain, second_shift)[1]
    residual_grad, second_gain_grad, second_shift_grad = second_pull(cotangent)
    feed_out_grad = residual_grad.astype(jnp.bfloat16)
    outer_bias_grad = column_total(feed_out_grad)
    outer_weight_grad = product_rows(active, feed_out_grad)
    active_grad = product_cols(feed_out_grad, outer_weight)
    inner_grad = jax.vjp(gelu_exact, inner_sum)[1](active_grad)[0].astype(jnp.bfloat16)
    inner_bias_grad = column_total(inner_grad)
    inner_weight_grad = product_rows(inner_grad, normed_low)
    normed_grad = residual_grad + product(inner_grad, inner_weight)
    first_pull = jax.vjp(layer_norm, first_sum, first_gain, first_shift)[1]
    first_sum_grad, first_gain_grad, first_shift_grad = first_pull(normed_grad)
    branch_grad_low = first_sum_grad.astype(jnp.bfloat16)
    output_bias_grad = column_total(branch_grad_low)
    output_weight_grad = product_rows(attended, branch_grad_low)
    attended_grad = product_cols(branch_grad_low, output_weight).astype(jnp.bfloat16)
    query_grad, key_grad, value_grad = lax.map(
        attend_backward,
        (
            queries.reshape(seq_shape),
            key_vectors.reshape(seq_shape),
            values.reshape(seq_shape),
            key_valid,
            log_total,
            attended_grad.reshape(seq_shape),
        ),
    )
    query_grad = query_grad.reshape(row_count, D)
    key_grad = key_grad.reshape(row_count, D)
    value_grad = value_grad.reshape(row_count, D)
    query_weight_grad = product_rows(tokens, query_grad)
    key_weight_grad = product_rows(tokens, key_grad)
    value_weight_grad = product_rows(tokens, value_grad)
    query_bias_grad = column_total(query_grad)
    value_bias_grad = column_total(value_grad)
    tokens_grad = (
        first_sum_grad
        + product_cols(query_grad, query_weight)
        + product_cols(key_grad, key_weight)
        + product_cols(value_grad, value_weight)
    )
    small_grad_all = jnp.concatenate(
        [
            query_bias_grad,
            value_bias_grad,
            output_bias_grad,
            inner_bias_grad,
            outer_bias_grad,
            first_gain_grad,
            first_shift_grad,
            second_gain_grad,
            second_shift_grad,
        ]
    )
    attention_owned, feed_owned, small_owned, totals = scatter_gradients(
        [query_weight_grad, key_weight_grad, value_weight_grad, output_weight_grad],
        [inner_weight_grad, outer_weight_grad],
        small_grad_all,
        partials,
        staged,
    )
    rms_values = jnp.sqrt(totals[:3] / (totals[3] * D))
    step_float = step_count[0].astype(jnp.float32)
    attention_new, attention_first_new, attention_second_new = adam_step(
        attention_master,
        attention_first,
        attention_second,
        attention_owned,
        rate_matrix,
        weight_decay,
        step_float,
    )
    feed_new, feed_first_new, feed_second_new = adam_step(
        feed_master, feed_first, feed_second, feed_owned, rate_matrix, weight_decay, step_float
    )
    small_new, small_first_new, small_second_new = adam_step(
        small_master, small_first, small_second, small_owned, rate_small, 0.0, step_float
    )
    return (
        layer_out,
        tokens_grad,
        attention_new,
        attention_first_new,
        attention_second_new,
        attention_new.astype(jnp.bfloat16),
        feed_new,
        feed_first_new,
        feed_second_new,
        feed_new.astype(jnp.bfloat16),
        small_new,
        small_first_new,
        small_second_new,
        small_new.astype(jnp.bfloat16),
        rms_values,
    )


def solution(mesh):
    placed = (
        P(("fsdp", "dp"), None),
        P(("fsdp", "dp"), None),
        P(("fsdp", "dp")),
        P(),
        P(("fsdp", "dp"), None),
        P(("fsdp", "dp"), None),
        P(("fsdp", "dp"), None),
        P(("fsdp", "dp"), None),
        P(("fsdp", "dp"), None),
        P(("fsdp", "dp"), None),
        P(("fsdp", "dp")),
        P(("fsdp", "dp")),
        P(("fsdp", "dp")),
    )
    staged = dict(mesh.shape) == {"fsdp": 16, "dp": 2}
    return jax.shard_map(
        functools.partial(on_device, staged),
        mesh=mesh,
        in_specs=placed,
        out_specs=(
            P(("fsdp", "dp"), None),
            P(("fsdp", "dp"), None),
            P(("fsdp", "dp"), None),
            P(("fsdp", "dp"), None),
            P(("fsdp", "dp"), None),
            P(("fsdp", "dp"), None),
            P(("fsdp", "dp"), None),
            P(("fsdp", "dp"), None),
            P(("fsdp", "dp"), None),
            P(("fsdp", "dp"), None),
            P(("fsdp", "dp")),
            P(("fsdp", "dp")),
            P(("fsdp", "dp")),
            P(("fsdp", "dp")),
            P(),
        ),
        check_vma=False,
    )
```

```python
import functools
import math

import jax
import jax.numpy as jnp
from jax import lax
from jax.sharding import PartitionSpec as P

D = 768
HEADS = 12
HDIM = 64
FF = 3072
SEQ = 512


ln_epsilon = 1e-12
beta_first = 0.5
beta_second = 0.55
adam_epsilon = 1e-06
rate_matrix = 0.04
rate_small = 0.25
weight_decay = 0.01


def product(left_side, right_side):
    return jnp.dot(left_side, right_side, preferred_element_type=jnp.float32)


def product_rows(left_side, right_side):
    return lax.dot_general(
        left_side, right_side, (((0,), (0,)), ((), ())), preferred_element_type=jnp.float32
    )


def product_cols(left_side, right_side):
    return lax.dot_general(
        left_side, right_side, (((1,), (1,)), ((), ())), preferred_element_type=jnp.float32
    )


def column_total(entries):
    return jnp.sum(entries, axis=0, dtype=jnp.float32)


def layer_norm(entries, norm_gain, norm_shift):
    center = jnp.mean(entries, axis=-1, keepdims=True)
    offset = entries - center
    spread = jnp.mean(offset * offset, axis=-1, keepdims=True)
    return offset * lax.rsqrt(spread + ln_epsilon) * norm_gain + norm_shift


def gelu_exact(entries):
    return jax.nn.gelu(entries, approximate=False)


def split_small(small_full):
    pieces = []
    position = 0
    for length in (D, D, D, FF, D, D, D, D, D):
        pieces.append(small_full[position : position + length].astype(jnp.float32))
        position = position + length
    return pieces


def head_view(entries):
    return entries.reshape(SEQ, HEADS, HDIM)


def masked_scores(queries, key_vectors, key_valid):
    scores = jnp.einsum(
        "qhd,khd->hqk",
        head_view(queries),
        head_view(key_vectors),
        preferred_element_type=jnp.float32,
    ) * (1.0 / math.sqrt(HDIM))
    return jnp.where(key_valid[None, None, :] > 0, scores, -1e30)


def attend_forward(pieces):
    queries, key_vectors, values, key_valid = pieces
    scores = masked_scores(queries, key_vectors, key_valid)
    row_max = jnp.max(scores, axis=-1, keepdims=True)
    exponent = jnp.exp(scores - row_max)
    row_total = jnp.sum(exponent, axis=-1, keepdims=True)
    probability = (exponent / row_total).astype(jnp.bfloat16)
    attended = jnp.einsum(
        "hqk,khd->qhd", probability, head_view(values), preferred_element_type=jnp.float32
    )
    return (attended.reshape(SEQ, D).astype(jnp.bfloat16), (row_max + jnp.log(row_total))[:, :, 0])


def attend_backward(pieces):
    queries, key_vectors, values, key_valid, log_total, attended_grad = pieces
    scores = masked_scores(queries, key_vectors, key_valid)
    probability = jnp.exp(scores - log_total[:, :, None])
    probability_low = probability.astype(jnp.bfloat16)
    grad_heads = head_view(attended_grad)
    value_grad = jnp.einsum(
        "hqk,qhd->khd", probability_low, grad_heads, preferred_element_type=jnp.float32
    )
    probability_grad = jnp.einsum(
        "qhd,khd->hqk", grad_heads, head_view(values), preferred_element_type=jnp.float32
    )
    inner_total = jnp.sum(probability * probability_grad, axis=-1, keepdims=True)
    score_grad = (probability * (probability_grad - inner_total)).astype(jnp.bfloat16)
    score_scale = 1.0 / math.sqrt(HDIM)
    query_grad = (
        jnp.einsum(
            "hqk,khd->qhd", score_grad, head_view(key_vectors), preferred_element_type=jnp.float32
        )
        * score_scale
    )
    key_grad = (
        jnp.einsum(
            "hqk,qhd->khd", score_grad, head_view(queries), preferred_element_type=jnp.float32
        )
        * score_scale
    )
    return (
        query_grad.reshape(SEQ, D).astype(jnp.bfloat16),
        key_grad.reshape(SEQ, D).astype(jnp.bfloat16),
        value_grad.reshape(SEQ, D).astype(jnp.bfloat16),
    )


def adam_step(master, first_moment, second, gradient, step_rate, decay_rate, step_float):
    first_new = beta_first * first_moment + (1.0 - beta_first) * gradient
    second_new = beta_second * second + (1.0 - beta_second) * gradient * gradient
    first_hat = first_new / (1.0 - beta_first**step_float)
    second_hat = second_new / (1.0 - beta_second**step_float)
    master_new = master - step_rate * (
        first_hat / (jnp.sqrt(second_hat) + adam_epsilon) + decay_rate * master
    )
    return (master_new, first_new, second_new)


def padded_rows(rows, multiple):
    return -(-rows // multiple) * multiple


def gather_working(attention_master, feed_master, small_master):
    attention_rows = attention_master.shape[0]
    feed_rows = feed_master.shape[0]
    small_count = small_master.shape[0]
    main_rows = attention_rows + feed_rows
    extra_rows = padded_rows(main_rows + padded_rows(small_count, D) // D, 16) - main_rows
    small_flat = jnp.zeros((extra_rows * D,), jnp.bfloat16)
    small_flat = small_flat.at[:small_count].set(small_master.astype(jnp.bfloat16))
    block = jnp.concatenate(
        [
            attention_master.astype(jnp.bfloat16),
            feed_master.astype(jnp.bfloat16),
            small_flat.reshape(extra_rows, D),
        ],
        axis=0,
    )
    gathered = lax.all_gather(block, ("fsdp", "dp"), axis=0, tiled=False)
    owners = gathered.shape[0]
    attention_full = gathered[:, :attention_rows].reshape(owners * attention_rows, D)
    feed_full = gathered[:, attention_rows:main_rows].reshape(owners * feed_rows, D)
    small_full = gathered[:, main_rows:].reshape(owners, extra_rows * D)[:, :small_count]
    return attention_full, feed_full, small_full.reshape(owners * small_count)


def flat_coordinates():
    me = lax.axis_index(("fsdp", "dp"))
    return me, me % 2, (me // 2) % 2, (me // 4) % 2, me // 8


def shifted(distance, count=32):
    return [(d, d + distance) for d in range(count) if 0 <= d + distance < count]


def flipped(mask, count=32):
    return [(d, d ^ mask) for d in range(count)]


def permute(arrays, pairs):
    return lax.ppermute(tuple(arrays), ("fsdp", "dp"), pairs)


def staged_reduce_scatter(arrays):
    me, y_place, core, x_place, z_place = flat_coordinates()
    blocks = [entries.reshape((4, 2, 2, 2) + entries.shape[1:]) for entries in arrays]
    keep = [lax.dynamic_index_in_dim(b, core, axis=2, keepdims=False) for b in blocks]
    send = [lax.dynamic_index_in_dim(b, 1 - core, axis=2, keepdims=False).astype(jnp.bfloat16) for b in blocks]
    received = permute(send, flipped(2))
    plane = [k.astype(jnp.float32) + r.astype(jnp.float32) for k, r in zip(keep, received)]

    def pick(entries, x_index, y_index):
        picked = lax.dynamic_index_in_dim(entries, x_index, axis=1, keepdims=False)
        return lax.dynamic_index_in_dim(picked, y_index, axis=1, keepdims=False)

    along_z = [pick(p, x_place, y_place) for p in plane]
    for mask, x_index, y_index in ((4, 1 - x_place, y_place), (1, x_place, 1 - y_place), (5, 1 - x_place, 1 - y_place)):
        got = permute([pick(p, x_index, y_index).astype(jnp.bfloat16) for p in plane], flipped(mask))
        along_z = [a + g.astype(jnp.float32) for a, g in zip(along_z, got)]
    owned = [lax.dynamic_index_in_dim(a, z_place, axis=0, keepdims=False) for a in along_z]
    for distance in (1, 2, 3):
        up = permute(
            [lax.dynamic_index_in_dim(a, jnp.minimum(z_place + distance, 3), axis=0, keepdims=False).astype(jnp.bfloat16) for a in along_z],
            shifted(8 * distance),
        )
        down = permute(
            [lax.dynamic_index_in_dim(a, jnp.maximum(z_place - distance, 0), axis=0, keepdims=False).astype(jnp.bfloat16) for a in along_z],
            shifted(-8 * distance),
        )
        owned = [o + u.astype(jnp.float32) + w.astype(jnp.float32) for o, u, w in zip(owned, up, down)]
    return owned


def staged_all_gather(arrays):
    me, y_place, core, x_place, z_place = flat_coordinates()
    slot = [lax.broadcasted_iota(jnp.int32, (4,) + (1,) * a.ndim, 0) for a in arrays]
    grown = [jnp.where(s == z_place, a[None], jnp.zeros((4,) + a.shape, a.dtype)) for s, a in zip(slot, arrays)]
    for distance in (1, 2, 3):
        from_below = permute(arrays, shifted(8 * distance))
        from_above = permute(arrays, shifted(-8 * distance))
        grown = [jnp.where(s == z_place - distance, b[None], g) for s, b, g in zip(slot, from_below, grown)]
        grown = [jnp.where(s == z_place + distance, b[None], g) for s, b, g in zip(slot, from_above, grown)]
    got_x = permute(grown, flipped(4))
    got_y = permute(grown, flipped(1))
    got_xy = permute(grown, flipped(5))
    planes = []
    for own, gx, gy, gxy in zip(grown, got_x, got_y, got_xy):
        shape = (own.shape[0], 2, 2) + own.shape[1:]
        xs = lax.broadcasted_iota(jnp.int32, (1, 2, 1) + (1,) * (own.ndim - 1), 1)
        ys = lax.broadcasted_iota(jnp.int32, (1, 1, 2) + (1,) * (own.ndim - 1), 2)
        same_x, same_y = xs == x_place, ys == y_place
        plane = jnp.where(
            same_x,
            jnp.where(same_y, own[:, None, None], gy[:, None, None]),
            jnp.where(same_y, gx[:, None, None], gxy[:, None, None]),
        )
        planes.append(jnp.broadcast_to(plane, shape))
    got_core = permute(planes, flipped(2))
    gathered = []
    for own, other in zip(planes, got_core):
        own = own[:, :, None]
        other = other[:, :, None]
        size = own.shape[2]
        shape = own.shape[:2] + (2,) + own.shape[3:]
        start = [0] * len(shape)
        start_other = [0] * len(shape)
        start[2] = core * size
        start_other[2] = (1 - core) * size
        full = jnp.zeros(shape, own.dtype)
        full = lax.dynamic_update_slice(full, own, start)
        full = lax.dynamic_update_slice(full, other, start_other)
        gathered.append(full.reshape((32 * full.shape[4],) + full.shape[5:]))
    return gathered


def staged_working(attention_master, feed_master, small_master):
    small_count = small_master.shape[0]
    small_row = jnp.zeros((1, D), jnp.bfloat16).at[0, :small_count].set(small_master.astype(jnp.bfloat16))
    attention_full, small_rows = staged_all_gather([attention_master.astype(jnp.bfloat16), small_row])
    small_full = small_rows[:, :small_count].reshape(32 * small_count)
    feed_full = lax.all_gather(feed_master.astype(jnp.bfloat16), ("fsdp", "dp"), axis=0, tiled=True)
    return attention_full, feed_full, small_full


def scatter_gradients(attention_pieces, feed_pieces, small_grad_all, partials, staged):
    owners = lax.psum(1, ("fsdp", "dp"))
    me = lax.axis_index(("fsdp", "dp"))
    attention_rows = sum(piece.shape[0] for piece in attention_pieces) // owners
    small_count = small_grad_all.shape[0] // owners
    feed_owned = lax.psum_scatter(feed_pieces, ("fsdp", "dp"), scatter_dimension=0, tiled=True)
    partials_high = partials.astype(jnp.bfloat16)
    partials_low = (partials - partials_high.astype(jnp.float32)).astype(jnp.bfloat16)
    split_partials = jnp.concatenate([partials_high, partials_low])
    slots = split_partials.shape[0]
    extra_count = small_count + owners * slots
    extra_rows = padded_rows(attention_rows + padded_rows(extra_count, D) // D, 16) - attention_rows
    slot_row = jnp.zeros((owners * slots,), jnp.bfloat16)
    slot_row = lax.dynamic_update_slice(slot_row, split_partials, (me * slots,))
    extra = jnp.concatenate(
        [
            small_grad_all.astype(jnp.bfloat16).reshape(owners, small_count),
            jnp.broadcast_to(slot_row[None], (owners, owners * slots)),
            jnp.zeros((owners, extra_rows * D - extra_count), jnp.bfloat16),
        ],
        axis=1,
    ).reshape(owners, extra_rows, D)
    block_rows = attention_rows + extra_rows
    if staged:
        attention_grad_all = jnp.concatenate(attention_pieces, axis=0).astype(jnp.bfloat16)
        owned = jnp.concatenate(
            staged_reduce_scatter([attention_grad_all.reshape(owners, attention_rows, D), extra]), axis=0
        )
    else:
        packed = jnp.zeros((owners, block_rows, D), jnp.bfloat16)
        packed = lax.dynamic_update_slice(packed, extra, (0, attention_rows, 0))
        owner = 0
        for piece in attention_pieces:
            piece_owners = piece.shape[0] // attention_rows
            packed = lax.dynamic_update_slice(
                packed, piece.astype(jnp.bfloat16).reshape(piece_owners, attention_rows, D), (owner, 0, 0)
            )
            owner = owner + piece_owners
        owned = lax.psum_scatter(
            packed.reshape(owners * block_rows, D), ("fsdp", "dp"), scatter_dimension=0, tiled=True
        ).astype(jnp.float32)
    attention_owned = owned[:attention_rows]
    extra_owned = owned[attention_rows:].reshape(extra_rows * D)
    small_owned = extra_owned[:small_count]
    gathered_partials = extra_owned[small_count:extra_count].reshape(owners, slots)
    half = slots // 2
    totals = gathered_partials[0, :half] + gathered_partials[0, half:]
    for index in range(1, owners):
        totals = totals + (gathered_partials[index, :half] + gathered_partials[index, half:])
    return attention_owned, feed_owned.astype(jnp.float32), small_owned, totals


def on_device(
    staged,
    tokens,
    cotangent,
    lengths,
    step_count,
    attention_master,
    attention_first,
    attention_second,
    feed_master,
    feed_first,
    feed_second,
    small_master,
    small_first,
    small_second,
):
    row_count = tokens.shape[0]
    sequence_count = row_count // SEQ
    if staged:
        attention_full, feed_full, small_full = staged_working(attention_master, feed_master, small_master)
    else:
        attention_full, feed_full, small_full = gather_working(attention_master, feed_master, small_master)
    key_valid = (
        lax.broadcasted_iota(jnp.int32, (sequence_count, SEQ), 1) < lengths[:, None]
    ).astype(jnp.float32)
    token_valid = key_valid.reshape(row_count)
    (
        query_bias,
        value_bias,
        output_bias,
        inner_bias,
        outer_bias,
        first_gain,
        first_shift,
        second_gain,
        second_shift,
    ) = split_small(small_full)
    queries = (product(tokens, attention_full[0:D]) + query_bias).astype(jnp.bfloat16)
    key_vectors = product(tokens, attention_full[D : 2 * D]).astype(jnp.bfloat16)
    values = (product(tokens, attention_full[2 * D : 3 * D]) + value_bias).astype(jnp.bfloat16)
    seq_shape = (sequence_count, SEQ, D)
    attended, log_total = lax.map(
        attend_forward,
        (
            queries.reshape(seq_shape),
            key_vectors.reshape(seq_shape),
            values.reshape(seq_shape),
            key_valid,
        ),
    )
    attended = attended.reshape(row_count, D)
    branch_attention = product(attended, attention_full[3 * D : 4 * D]) + output_bias
    first_sum = tokens.astype(jnp.float32) + branch_attention
    normed = layer_norm(first_sum, first_gain, first_shift)
    normed_low = normed.astype(jnp.bfloat16)
    inner_sum = product_cols(normed_low, feed_full[0:FF]) + inner_bias
    active = gelu_exact(inner_sum).astype(jnp.bfloat16)
    branch_feed = product(active, feed_full[FF : 2 * FF]) + outer_bias
    residual = normed + branch_feed
    layer_out = layer_norm(residual, second_gain, second_shift).astype(jnp.bfloat16)
    column = token_valid[:, None]
    partials = jnp.stack(
        [
            jnp.sum(residual * residual * column),
            jnp.sum(branch_attention * branch_attention * column),
            jnp.sum(branch_feed * branch_feed * column),
            jnp.sum(token_valid),
        ]
    )
    query_weight = attention_full[0:D]
    key_weight = attention_full[D : 2 * D]
    value_weight = attention_full[2 * D : 3 * D]
    output_weight = attention_full[3 * D : 4 * D]
    outer_weight = feed_full[FF : 2 * FF]
    inner_weight = feed_full[0:FF]
    second_pull = jax.vjp(layer_norm, residual, second_gain, second_shift)[1]
    residual_grad, second_gain_grad, second_shift_grad = second_pull(cotangent)
    feed_out_grad = residual_grad.astype(jnp.bfloat16)
    outer_bias_grad = column_total(feed_out_grad)
    active_grad = product_cols(feed_out_grad, outer_weight)
    inner_grad = jax.vjp(gelu_exact, inner_sum)[1](active_grad)[0].astype(jnp.bfloat16)
    inner_bias_grad = column_total(inner_grad)
    feed_grad_all = (
        lax.dot_general(
            jnp.stack([inner_grad, active]),
            jnp.stack([normed_low, feed_out_grad]),
            (((1,), (1,)), ((0,), (0,))),
            preferred_element_type=jnp.float32,
        )
        .astype(jnp.bfloat16)
        .reshape(2 * FF, D)
    )
    normed_grad = residual_grad + product(inner_grad, inner_weight)
    first_pull = jax.vjp(layer_norm, first_sum, first_gain, first_shift)[1]
    first_sum_grad, first_gain_grad, first_shift_grad = first_pull(normed_grad)
    branch_grad_low = first_sum_grad.astype(jnp.bfloat16)
    output_bias_grad = column_total(branch_grad_low)
    output_weight_grad = product_rows(attended, branch_grad_low)
    attended_grad = product_cols(branch_grad_low, output_weight).astype(jnp.bfloat16)
    feed_grad_all, attended_grad = lax.optimization_barrier((feed_grad_all, attended_grad))
    query_grad, key_grad, value_grad = lax.map(
        attend_backward,
        (
            queries.reshape(seq_shape),
            key_vectors.reshape(seq_shape),
            values.reshape(seq_shape),
            key_valid,
            log_total,
            attended_grad.reshape(seq_shape),
        ),
    )
    query_grad = query_grad.reshape(row_count, D)
    key_grad = key_grad.reshape(row_count, D)
    value_grad = value_grad.reshape(row_count, D)
    query_weight_grad = product_rows(tokens, query_grad)
    key_weight_grad = product_rows(tokens, key_grad)
    value_weight_grad = product_rows(tokens, value_grad)
    query_bias_grad = column_total(query_grad)
    value_bias_grad = column_total(value_grad)
    tokens_grad = (
        first_sum_grad
        + product_cols(query_grad, query_weight)
        + product_cols(key_grad, key_weight)
        + product_cols(value_grad, value_weight)
    )
    small_grad_all = jnp.concatenate(
        [
            query_bias_grad,
            value_bias_grad,
            output_bias_grad,
            inner_bias_grad,
            outer_bias_grad,
            first_gain_grad,
            first_shift_grad,
            second_gain_grad,
            second_shift_grad,
        ]
    )
    attention_owned, feed_owned, small_owned, totals = scatter_gradients(
        [query_weight_grad, key_weight_grad, value_weight_grad, output_weight_grad],
        feed_grad_all,
        small_grad_all,
        partials,
        staged,
    )
    rms_values = jnp.sqrt(totals[:3] / (totals[3] * D))
    step_float = step_count[0].astype(jnp.float32)
    attention_new, attention_first_new, attention_second_new = adam_step(
        attention_master,
        attention_first,
        attention_second,
        attention_owned,
        rate_matrix,
        weight_decay,
        step_float,
    )
    feed_new, feed_first_new, feed_second_new = adam_step(
        feed_master, feed_first, feed_second, feed_owned, rate_matrix, weight_decay, step_float
    )
    small_new, small_first_new, small_second_new = adam_step(
        small_master, small_first, small_second, small_owned, rate_small, 0.0, step_float
    )
    return (
        layer_out,
        tokens_grad,
        attention_new,
        attention_first_new,
        attention_second_new,
        attention_new.astype(jnp.bfloat16),
        feed_new,
        feed_first_new,
        feed_second_new,
        feed_new.astype(jnp.bfloat16),
        small_new,
        small_first_new,
        small_second_new,
        small_new.astype(jnp.bfloat16),
        rms_values,
    )


def solution(mesh):
    placed = (
        P(("fsdp", "dp"), None),
        P(("fsdp", "dp"), None),
        P(("fsdp", "dp")),
        P(),
        P(("fsdp", "dp"), None),
        P(("fsdp", "dp"), None),
        P(("fsdp", "dp"), None),
        P(("fsdp", "dp"), None),
        P(("fsdp", "dp"), None),
        P(("fsdp", "dp"), None),
        P(("fsdp", "dp")),
        P(("fsdp", "dp")),
        P(("fsdp", "dp")),
    )
    staged = dict(mesh.shape) == {"fsdp": 16, "dp": 2}
    return jax.shard_map(
        functools.partial(on_device, staged),
        mesh=mesh,
        in_specs=placed,
        out_specs=(
            P(("fsdp", "dp"), None),
            P(("fsdp", "dp"), None),
            P(("fsdp", "dp"), None),
            P(("fsdp", "dp"), None),
            P(("fsdp", "dp"), None),
            P(("fsdp", "dp"), None),
            P(("fsdp", "dp"), None),
            P(("fsdp", "dp"), None),
            P(("fsdp", "dp"), None),
            P(("fsdp", "dp"), None),
            P(("fsdp", "dp")),
            P(("fsdp", "dp")),
            P(("fsdp", "dp")),
            P(("fsdp", "dp")),
            P(),
        ),
        check_vma=False,
    )
```

```python
import functools
import math

import jax
import jax.numpy as jnp
from jax import lax
from jax.sharding import PartitionSpec as P

D = 768
HEADS = 12
HDIM = 64
FF = 3072
SEQ = 512


ln_epsilon = 1e-12
beta_first = 0.5
beta_second = 0.55
adam_epsilon = 1e-06
rate_matrix = 0.04
rate_small = 0.25
weight_decay = 0.01


def product(left_side, right_side):
    return jnp.dot(left_side, right_side, preferred_element_type=jnp.float32)


def product_rows(left_side, right_side):
    return lax.dot_general(
        left_side, right_side, (((0,), (0,)), ((), ())), preferred_element_type=jnp.float32
    )


def product_cols(left_side, right_side):
    return lax.dot_general(
        left_side, right_side, (((1,), (1,)), ((), ())), preferred_element_type=jnp.float32
    )


def column_total(entries):
    return jnp.sum(entries, axis=0, dtype=jnp.float32)


def layer_norm(entries, norm_gain, norm_shift):
    center = jnp.mean(entries, axis=-1, keepdims=True)
    offset = entries - center
    spread = jnp.mean(offset * offset, axis=-1, keepdims=True)
    return offset * lax.rsqrt(spread + ln_epsilon) * norm_gain + norm_shift


def gelu_exact(entries):
    return jax.nn.gelu(entries, approximate=False)


def split_small(small_full):
    pieces = []
    position = 0
    for length in (D, D, D, FF, D, D, D, D, D):
        pieces.append(small_full[position : position + length].astype(jnp.float32))
        position = position + length
    return pieces


def head_view(entries):
    return entries.reshape(SEQ, HEADS, HDIM)


def masked_scores(queries, key_vectors, key_valid):
    scores = jnp.einsum(
        "qhd,khd->hqk",
        head_view(queries),
        head_view(key_vectors),
        preferred_element_type=jnp.float32,
    ) * (1.0 / math.sqrt(HDIM))
    return jnp.where(key_valid[None, None, :] > 0, scores, -1e30)


def attend_forward(pieces):
    queries, key_vectors, values, key_valid = pieces
    scores = masked_scores(queries, key_vectors, key_valid)
    row_max = jnp.max(scores, axis=-1, keepdims=True)
    exponent = jnp.exp(scores - row_max)
    row_total = jnp.sum(exponent, axis=-1, keepdims=True)
    probability = (exponent / row_total).astype(jnp.bfloat16)
    attended = jnp.einsum(
        "hqk,khd->qhd", probability, head_view(values), preferred_element_type=jnp.float32
    )
    return (attended.reshape(SEQ, D).astype(jnp.bfloat16), (row_max + jnp.log(row_total))[:, :, 0])


def attend_backward(pieces):
    queries, key_vectors, values, key_valid, log_total, attended_grad = pieces
    scores = masked_scores(queries, key_vectors, key_valid)
    probability = jnp.exp(scores - log_total[:, :, None])
    probability_low = probability.astype(jnp.bfloat16)
    grad_heads = head_view(attended_grad)
    value_grad = jnp.einsum(
        "hqk,qhd->khd", probability_low, grad_heads, preferred_element_type=jnp.float32
    )
    probability_grad = jnp.einsum(
        "qhd,khd->hqk", grad_heads, head_view(values), preferred_element_type=jnp.float32
    )
    inner_total = jnp.sum(probability * probability_grad, axis=-1, keepdims=True)
    score_grad = (probability * (probability_grad - inner_total)).astype(jnp.bfloat16)
    score_scale = 1.0 / math.sqrt(HDIM)
    query_grad = (
        jnp.einsum(
            "hqk,khd->qhd", score_grad, head_view(key_vectors), preferred_element_type=jnp.float32
        )
        * score_scale
    )
    key_grad = (
        jnp.einsum(
            "hqk,qhd->khd", score_grad, head_view(queries), preferred_element_type=jnp.float32
        )
        * score_scale
    )
    return (
        query_grad.reshape(SEQ, D).astype(jnp.bfloat16),
        key_grad.reshape(SEQ, D).astype(jnp.bfloat16),
        value_grad.reshape(SEQ, D).astype(jnp.bfloat16),
    )


def adam_step(master, first_moment, second, gradient, step_rate, decay_rate, step_float):
    first_new = beta_first * first_moment + (1.0 - beta_first) * gradient
    second_new = beta_second * second + (1.0 - beta_second) * gradient * gradient
    first_hat = first_new / (1.0 - beta_first**step_float)
    second_hat = second_new / (1.0 - beta_second**step_float)
    master_new = master - step_rate * (
        first_hat / (jnp.sqrt(second_hat) + adam_epsilon) + decay_rate * master
    )
    return (master_new, first_new, second_new)


def padded_rows(rows, multiple):
    return -(-rows // multiple) * multiple


def gather_working(attention_master, feed_master, small_master):
    attention_rows = attention_master.shape[0]
    feed_rows = feed_master.shape[0]
    small_count = small_master.shape[0]
    main_rows = attention_rows + feed_rows
    extra_rows = padded_rows(main_rows + padded_rows(small_count, D) // D, 16) - main_rows
    small_flat = jnp.zeros((extra_rows * D,), jnp.bfloat16)
    small_flat = small_flat.at[:small_count].set(small_master.astype(jnp.bfloat16))
    block = jnp.concatenate(
        [
            attention_master.astype(jnp.bfloat16),
            feed_master.astype(jnp.bfloat16),
            small_flat.reshape(extra_rows, D),
        ],
        axis=0,
    )
    gathered = lax.all_gather(block, ("fsdp", "dp"), axis=0, tiled=False)
    owners = gathered.shape[0]
    attention_full = gathered[:, :attention_rows].reshape(owners * attention_rows, D)
    feed_full = gathered[:, attention_rows:main_rows].reshape(owners * feed_rows, D)
    small_full = gathered[:, main_rows:].reshape(owners, extra_rows * D)[:, :small_count]
    return attention_full, feed_full, small_full.reshape(owners * small_count)


def flat_coordinates():
    me = lax.axis_index(("fsdp", "dp"))
    return me, me % 2, (me // 2) % 2, (me // 4) % 2, me // 8


def shifted(distance, count=32):
    return [(d, d + distance) for d in range(count) if 0 <= d + distance < count]


def flipped(mask, count=32):
    return [(d, d ^ mask) for d in range(count)]


def permute(arrays, pairs):
    return lax.ppermute(tuple(arrays), ("fsdp", "dp"), pairs)


def staged_reduce_scatter(arrays):
    me, y_place, core, x_place, z_place = flat_coordinates()
    blocks = [entries.reshape((4, 2, 2, 2) + entries.shape[1:]) for entries in arrays]
    keep = [lax.dynamic_index_in_dim(b, core, axis=2, keepdims=False) for b in blocks]
    send = [lax.dynamic_index_in_dim(b, 1 - core, axis=2, keepdims=False).astype(jnp.bfloat16) for b in blocks]
    received = permute(send, flipped(2))
    plane = [k.astype(jnp.float32) + r.astype(jnp.float32) for k, r in zip(keep, received)]

    def pick(entries, x_index, y_index):
        picked = lax.dynamic_index_in_dim(entries, x_index, axis=1, keepdims=False)
        return lax.dynamic_index_in_dim(picked, y_index, axis=1, keepdims=False)

    along_z = [pick(p, x_place, y_place) for p in plane]
    for mask, x_index, y_index in ((4, 1 - x_place, y_place), (1, x_place, 1 - y_place), (5, 1 - x_place, 1 - y_place)):
        got = permute([pick(p, x_index, y_index).astype(jnp.bfloat16) for p in plane], flipped(mask))
        along_z = [a + g.astype(jnp.float32) for a, g in zip(along_z, got)]
    owned = [lax.dynamic_index_in_dim(a, z_place, axis=0, keepdims=False) for a in along_z]
    for distance in (1, 2, 3):
        up = permute(
            [lax.dynamic_index_in_dim(a, jnp.minimum(z_place + distance, 3), axis=0, keepdims=False).astype(jnp.bfloat16) for a in along_z],
            shifted(8 * distance),
        )
        down = permute(
            [lax.dynamic_index_in_dim(a, jnp.maximum(z_place - distance, 0), axis=0, keepdims=False).astype(jnp.bfloat16) for a in along_z],
            shifted(-8 * distance),
        )
        owned = [o + u.astype(jnp.float32) + w.astype(jnp.float32) for o, u, w in zip(owned, up, down)]
    return owned


def staged_all_gather(arrays):
    me, y_place, core, x_place, z_place = flat_coordinates()
    slot = [lax.broadcasted_iota(jnp.int32, (4,) + (1,) * a.ndim, 0) for a in arrays]
    grown = [jnp.where(s == z_place, a[None], jnp.zeros((4,) + a.shape, a.dtype)) for s, a in zip(slot, arrays)]
    for distance in (1, 2, 3):
        from_below = permute(arrays, shifted(8 * distance))
        from_above = permute(arrays, shifted(-8 * distance))
        grown = [jnp.where(s == z_place - distance, b[None], g) for s, b, g in zip(slot, from_below, grown)]
        grown = [jnp.where(s == z_place + distance, b[None], g) for s, b, g in zip(slot, from_above, grown)]
    got_x = permute(grown, flipped(4))
    got_y = permute(grown, flipped(1))
    got_xy = permute(grown, flipped(5))
    planes = []
    for own, gx, gy, gxy in zip(grown, got_x, got_y, got_xy):
        shape = (own.shape[0], 2, 2) + own.shape[1:]
        xs = lax.broadcasted_iota(jnp.int32, (1, 2, 1) + (1,) * (own.ndim - 1), 1)
        ys = lax.broadcasted_iota(jnp.int32, (1, 1, 2) + (1,) * (own.ndim - 1), 2)
        same_x, same_y = xs == x_place, ys == y_place
        plane = jnp.where(
            same_x,
            jnp.where(same_y, own[:, None, None], gy[:, None, None]),
            jnp.where(same_y, gx[:, None, None], gxy[:, None, None]),
        )
        planes.append(jnp.broadcast_to(plane, shape))
    got_core = permute(planes, flipped(2))
    gathered = []
    for own, other in zip(planes, got_core):
        own = own[:, :, None]
        other = other[:, :, None]
        size = own.shape[2]
        shape = own.shape[:2] + (2,) + own.shape[3:]
        start = [0] * len(shape)
        start_other = [0] * len(shape)
        start[2] = core * size
        start_other[2] = (1 - core) * size
        full = jnp.zeros(shape, own.dtype)
        full = lax.dynamic_update_slice(full, own, start)
        full = lax.dynamic_update_slice(full, other, start_other)
        gathered.append(full.reshape((32 * full.shape[4],) + full.shape[5:]))
    return gathered


def staged_working(attention_master, feed_master, small_master):
    attention_rows = attention_master.shape[0]
    small_count = small_master.shape[0]
    small_rows = jnp.zeros((16, D), jnp.bfloat16).at[0, :small_count].set(small_master.astype(jnp.bfloat16))
    block = jnp.concatenate([attention_master.astype(jnp.bfloat16), small_rows], axis=0)
    (gathered,) = staged_all_gather([block])
    gathered = gathered.reshape(32, attention_rows + 16, D)
    attention_full = gathered[:, :attention_rows].reshape(32 * attention_rows, D)
    small_full = gathered[:, attention_rows, :small_count].reshape(32 * small_count)
    feed_full = lax.all_gather(feed_master.astype(jnp.bfloat16), ("fsdp", "dp"), axis=0, tiled=True)
    return attention_full, feed_full, small_full


def scatter_gradients(attention_pieces, feed_pieces, small_grad_all, partials, staged):
    owners = lax.psum(1, ("fsdp", "dp"))
    me = lax.axis_index(("fsdp", "dp"))
    attention_rows = sum(piece.shape[0] for piece in attention_pieces) // owners
    small_count = small_grad_all.shape[0] // owners
    feed_owned = lax.psum_scatter(feed_pieces, ("fsdp", "dp"), scatter_dimension=0, tiled=True)
    partials_high = partials.astype(jnp.bfloat16)
    partials_low = (partials - partials_high.astype(jnp.float32)).astype(jnp.bfloat16)
    split_partials = jnp.concatenate([partials_high, partials_low])
    slots = split_partials.shape[0]
    extra_count = small_count + owners * slots
    extra_rows = padded_rows(attention_rows + padded_rows(extra_count, D) // D, 16) - attention_rows
    slot_row = jnp.zeros((owners * slots,), jnp.bfloat16)
    slot_row = lax.dynamic_update_slice(slot_row, split_partials, (me * slots,))
    extra = jnp.concatenate(
        [
            small_grad_all.astype(jnp.bfloat16).reshape(owners, small_count),
            jnp.broadcast_to(slot_row[None], (owners, owners * slots)),
            jnp.zeros((owners, extra_rows * D - extra_count), jnp.bfloat16),
        ],
        axis=1,
    ).reshape(owners, extra_rows, D)
    block_rows = attention_rows + extra_rows
    if staged:
        attention_grad_all = jnp.concatenate(attention_pieces, axis=0).astype(jnp.bfloat16)
        packed = jnp.concatenate([attention_grad_all.reshape(owners, attention_rows, D), extra], axis=1)
        (owned,) = staged_reduce_scatter([packed])
    else:
        packed = jnp.zeros((owners, block_rows, D), jnp.bfloat16)
        packed = lax.dynamic_update_slice(packed, extra, (0, attention_rows, 0))
        owner = 0
        for piece in attention_pieces:
            piece_owners = piece.shape[0] // attention_rows
            packed = lax.dynamic_update_slice(
                packed, piece.astype(jnp.bfloat16).reshape(piece_owners, attention_rows, D), (owner, 0, 0)
            )
            owner = owner + piece_owners
        owned = lax.psum_scatter(
            packed.reshape(owners * block_rows, D), ("fsdp", "dp"), scatter_dimension=0, tiled=True
        ).astype(jnp.float32)
    attention_owned = owned[:attention_rows]
    extra_owned = owned[attention_rows:].reshape(extra_rows * D)
    small_owned = extra_owned[:small_count]
    gathered_partials = extra_owned[small_count:extra_count].reshape(owners, slots)
    half = slots // 2
    totals = gathered_partials[0, :half] + gathered_partials[0, half:]
    for index in range(1, owners):
        totals = totals + (gathered_partials[index, :half] + gathered_partials[index, half:])
    return attention_owned, feed_owned.astype(jnp.float32), small_owned, totals


def on_device(
    staged,
    tokens,
    cotangent,
    lengths,
    step_count,
    attention_master,
    attention_first,
    attention_second,
    feed_master,
    feed_first,
    feed_second,
    small_master,
    small_first,
    small_second,
):
    row_count = tokens.shape[0]
    sequence_count = row_count // SEQ
    if staged:
        attention_full, feed_full, small_full = staged_working(attention_master, feed_master, small_master)
    else:
        attention_full, feed_full, small_full = gather_working(attention_master, feed_master, small_master)
    key_valid = (
        lax.broadcasted_iota(jnp.int32, (sequence_count, SEQ), 1) < lengths[:, None]
    ).astype(jnp.float32)
    token_valid = key_valid.reshape(row_count)
    (
        query_bias,
        value_bias,
        output_bias,
        inner_bias,
        outer_bias,
        first_gain,
        first_shift,
        second_gain,
        second_shift,
    ) = split_small(small_full)
    queries = (product(tokens, attention_full[0:D]) + query_bias).astype(jnp.bfloat16)
    key_vectors = product(tokens, attention_full[D : 2 * D]).astype(jnp.bfloat16)
    values = (product(tokens, attention_full[2 * D : 3 * D]) + value_bias).astype(jnp.bfloat16)
    seq_shape = (sequence_count, SEQ, D)
    attended, log_total = lax.map(
        attend_forward,
        (
            queries.reshape(seq_shape),
            key_vectors.reshape(seq_shape),
            values.reshape(seq_shape),
            key_valid,
        ),
    )
    attended = attended.reshape(row_count, D)
    branch_attention = product(attended, attention_full[3 * D : 4 * D]) + output_bias
    first_sum = tokens.astype(jnp.float32) + branch_attention
    normed = layer_norm(first_sum, first_gain, first_shift)
    normed_low = normed.astype(jnp.bfloat16)
    inner_sum = product_cols(normed_low, feed_full[0:FF]) + inner_bias
    active = gelu_exact(inner_sum).astype(jnp.bfloat16)
    branch_feed = product(active, feed_full[FF : 2 * FF]) + outer_bias
    residual = normed + branch_feed
    layer_out = layer_norm(residual, second_gain, second_shift).astype(jnp.bfloat16)
    column = token_valid[:, None]
    partials = jnp.stack(
        [
            jnp.sum(residual * residual * column),
            jnp.sum(branch_attention * branch_attention * column),
            jnp.sum(branch_feed * branch_feed * column),
            jnp.sum(token_valid),
        ]
    )
    query_weight = attention_full[0:D]
    key_weight = attention_full[D : 2 * D]
    value_weight = attention_full[2 * D : 3 * D]
    output_weight = attention_full[3 * D : 4 * D]
    outer_weight = feed_full[FF : 2 * FF]
    inner_weight = feed_full[0:FF]
    second_pull = jax.vjp(layer_norm, residual, second_gain, second_shift)[1]
    residual_grad, second_gain_grad, second_shift_grad = second_pull(cotangent)
    feed_out_grad = residual_grad.astype(jnp.bfloat16)
    outer_bias_grad = column_total(feed_out_grad)
    active_grad = product_cols(feed_out_grad, outer_weight)
    inner_grad = jax.vjp(gelu_exact, inner_sum)[1](active_grad)[0].astype(jnp.bfloat16)
    inner_bias_grad = column_total(inner_grad)
    feed_grad_all = (
        lax.dot_general(
            jnp.stack([inner_grad, active]),
            jnp.stack([normed_low, feed_out_grad]),
            (((1,), (1,)), ((0,), (0,))),
            preferred_element_type=jnp.float32,
        )
        .astype(jnp.bfloat16)
        .reshape(2 * FF, D)
    )
    normed_grad = residual_grad + product(inner_grad, inner_weight)
    first_pull = jax.vjp(layer_norm, first_sum, first_gain, first_shift)[1]
    first_sum_grad, first_gain_grad, first_shift_grad = first_pull(normed_grad)
    branch_grad_low = first_sum_grad.astype(jnp.bfloat16)
    output_bias_grad = column_total(branch_grad_low)
    output_weight_grad = product_rows(attended, branch_grad_low)
    attended_grad = product_cols(branch_grad_low, output_weight).astype(jnp.bfloat16)
    feed_grad_all, attended_grad = lax.optimization_barrier((feed_grad_all, attended_grad))
    query_grad, key_grad, value_grad = lax.map(
        attend_backward,
        (
            queries.reshape(seq_shape),
            key_vectors.reshape(seq_shape),
            values.reshape(seq_shape),
            key_valid,
            log_total,
            attended_grad.reshape(seq_shape),
        ),
    )
    query_grad = query_grad.reshape(row_count, D)
    key_grad = key_grad.reshape(row_count, D)
    value_grad = value_grad.reshape(row_count, D)
    query_weight_grad = product_rows(tokens, query_grad)
    key_weight_grad = product_rows(tokens, key_grad)
    value_weight_grad = product_rows(tokens, value_grad)
    query_bias_grad = column_total(query_grad)
    value_bias_grad = column_total(value_grad)
    tokens_grad = (
        first_sum_grad
        + product_cols(query_grad, query_weight)
        + product_cols(key_grad, key_weight)
        + product_cols(value_grad, value_weight)
    )
    small_grad_all = jnp.concatenate(
        [
            query_bias_grad,
            value_bias_grad,
            output_bias_grad,
            inner_bias_grad,
            outer_bias_grad,
            first_gain_grad,
            first_shift_grad,
            second_gain_grad,
            second_shift_grad,
        ]
    )
    attention_owned, feed_owned, small_owned, totals = scatter_gradients(
        [query_weight_grad, key_weight_grad, value_weight_grad, output_weight_grad],
        feed_grad_all,
        small_grad_all,
        partials,
        staged,
    )
    rms_values = jnp.sqrt(totals[:3] / (totals[3] * D))
    step_float = step_count[0].astype(jnp.float32)
    attention_new, attention_first_new, attention_second_new = adam_step(
        attention_master,
        attention_first,
        attention_second,
        attention_owned,
        rate_matrix,
        weight_decay,
        step_float,
    )
    feed_new, feed_first_new, feed_second_new = adam_step(
        feed_master, feed_first, feed_second, feed_owned, rate_matrix, weight_decay, step_float
    )
    small_new, small_first_new, small_second_new = adam_step(
        small_master, small_first, small_second, small_owned, rate_small, 0.0, step_float
    )
    return (
        layer_out,
        tokens_grad,
        attention_new,
        attention_first_new,
        attention_second_new,
        attention_new.astype(jnp.bfloat16),
        feed_new,
        feed_first_new,
        feed_second_new,
        feed_new.astype(jnp.bfloat16),
        small_new,
        small_first_new,
        small_second_new,
        small_new.astype(jnp.bfloat16),
        rms_values,
    )


def solution(mesh):
    placed = (
        P(("fsdp", "dp"), None),
        P(("fsdp", "dp"), None),
        P(("fsdp", "dp")),
        P(),
        P(("fsdp", "dp"), None),
        P(("fsdp", "dp"), None),
        P(("fsdp", "dp"), None),
        P(("fsdp", "dp"), None),
        P(("fsdp", "dp"), None),
        P(("fsdp", "dp"), None),
        P(("fsdp", "dp")),
        P(("fsdp", "dp")),
        P(("fsdp", "dp")),
    )
    staged = dict(mesh.shape) == {"fsdp": 16, "dp": 2}
    return jax.shard_map(
        functools.partial(on_device, staged),
        mesh=mesh,
        in_specs=placed,
        out_specs=(
            P(("fsdp", "dp"), None),
            P(("fsdp", "dp"), None),
            P(("fsdp", "dp"), None),
            P(("fsdp", "dp"), None),
            P(("fsdp", "dp"), None),
            P(("fsdp", "dp"), None),
            P(("fsdp", "dp"), None),
            P(("fsdp", "dp"), None),
            P(("fsdp", "dp"), None),
            P(("fsdp", "dp"), None),
            P(("fsdp", "dp")),
            P(("fsdp", "dp")),
            P(("fsdp", "dp")),
            P(("fsdp", "dp")),
            P(),
        ),
        check_vma=False,
    )
```

```python
import functools
import math

import jax
import numpy as np
import jax.numpy as jnp
from jax import lax
from jax.sharding import PartitionSpec as P

D = 768
HEADS = 12
HDIM = 64
FF = 3072
SEQ = 512


ln_epsilon = 1e-12
beta_first = 0.5
beta_second = 0.55
adam_epsilon = 1e-06
rate_matrix = 0.04
rate_small = 0.25
weight_decay = 0.01


def product(left_side, right_side):
    return jnp.dot(left_side, right_side, preferred_element_type=jnp.float32)


def product_rows(left_side, right_side):
    return lax.dot_general(
        left_side, right_side, (((0,), (0,)), ((), ())), preferred_element_type=jnp.float32
    )


def product_cols(left_side, right_side):
    return lax.dot_general(
        left_side, right_side, (((1,), (1,)), ((), ())), preferred_element_type=jnp.float32
    )


def column_total(entries):
    return jnp.sum(entries, axis=0, dtype=jnp.float32)


def layer_norm(entries, norm_gain, norm_shift):
    center = jnp.mean(entries, axis=-1, keepdims=True)
    offset = entries - center
    spread = jnp.mean(offset * offset, axis=-1, keepdims=True)
    return offset * lax.rsqrt(spread + ln_epsilon) * norm_gain + norm_shift


def gelu_exact(entries):
    return jax.nn.gelu(entries, approximate=False)


def gelu_derivative(entries):
    sqrt_half = np.sqrt(0.5).astype(np.float32)
    shifted_entries = -entries * sqrt_half
    return 0.5 * lax.erfc(shifted_entries) + entries * (
        jnp.exp(-(shifted_entries * shifted_entries)) * np.float32(sqrt_half / np.sqrt(np.pi))
    )


def split_small(small_full):
    pieces = []
    position = 0
    for length in (D, D, D, FF, D, D, D, D, D):
        pieces.append(small_full[position : position + length].astype(jnp.float32))
        position = position + length
    return pieces


def head_view(entries):
    return entries.reshape(SEQ, HEADS, HDIM)


def masked_scores(queries, key_vectors, key_valid):
    scores = jnp.einsum(
        "qhd,khd->hqk",
        head_view(queries),
        head_view(key_vectors),
        preferred_element_type=jnp.float32,
    ) * (1.0 / math.sqrt(HDIM))
    return jnp.where(key_valid[None, None, :] > 0, scores, -1e30)


def attend_forward(pieces):
    queries, key_vectors, values, key_valid = pieces
    scores = masked_scores(queries, key_vectors, key_valid)
    row_max = jnp.max(scores, axis=-1, keepdims=True)
    exponent = jnp.exp(scores - row_max)
    row_total = jnp.sum(exponent, axis=-1, keepdims=True)
    probability = (exponent / row_total).astype(jnp.bfloat16)
    attended = jnp.einsum(
        "hqk,khd->qhd", probability, head_view(values), preferred_element_type=jnp.float32
    )
    return (attended.reshape(SEQ, D).astype(jnp.bfloat16), (row_max + jnp.log(row_total))[:, :, 0])


def attend_backward(pieces):
    queries, key_vectors, values, key_valid, log_total, attended_grad = pieces
    scores = masked_scores(queries, key_vectors, key_valid)
    probability = jnp.exp(scores - log_total[:, :, None])
    probability_low = probability.astype(jnp.bfloat16)
    grad_heads = head_view(attended_grad)
    value_grad = jnp.einsum(
        "hqk,qhd->khd", probability_low, grad_heads, preferred_element_type=jnp.float32
    )
    probability_grad = jnp.einsum(
        "qhd,khd->hqk", grad_heads, head_view(values), preferred_element_type=jnp.float32
    )
    inner_total = jnp.sum(probability * probability_grad, axis=-1, keepdims=True)
    score_grad = (probability * (probability_grad - inner_total)).astype(jnp.bfloat16)
    score_scale = 1.0 / math.sqrt(HDIM)
    query_grad = (
        jnp.einsum(
            "hqk,khd->qhd", score_grad, head_view(key_vectors), preferred_element_type=jnp.float32
        )
        * score_scale
    )
    key_grad = (
        jnp.einsum(
            "hqk,qhd->khd", score_grad, head_view(queries), preferred_element_type=jnp.float32
        )
        * score_scale
    )
    return (
        query_grad.reshape(SEQ, D).astype(jnp.bfloat16),
        key_grad.reshape(SEQ, D).astype(jnp.bfloat16),
        value_grad.reshape(SEQ, D).astype(jnp.bfloat16),
    )


def adam_step(master, first_moment, second, gradient, step_rate, decay_rate, step_float):
    first_new = beta_first * first_moment + (1.0 - beta_first) * gradient
    second_new = beta_second * second + (1.0 - beta_second) * gradient * gradient
    first_hat = first_new / (1.0 - beta_first**step_float)
    second_hat = second_new / (1.0 - beta_second**step_float)
    master_new = master - step_rate * (
        first_hat / (jnp.sqrt(second_hat) + adam_epsilon) + decay_rate * master
    )
    return (master_new, first_new, second_new)


def padded_rows(rows, multiple):
    return -(-rows // multiple) * multiple


def gather_working(attention_master, feed_master, small_master):
    attention_rows = attention_master.shape[0]
    feed_rows = feed_master.shape[0]
    small_count = small_master.shape[0]
    main_rows = attention_rows + feed_rows
    extra_rows = padded_rows(main_rows + padded_rows(small_count, D) // D, 16) - main_rows
    small_flat = jnp.zeros((extra_rows * D,), jnp.bfloat16)
    small_flat = small_flat.at[:small_count].set(small_master.astype(jnp.bfloat16))
    block = jnp.concatenate(
        [
            attention_master.astype(jnp.bfloat16),
            feed_master.astype(jnp.bfloat16),
            small_flat.reshape(extra_rows, D),
        ],
        axis=0,
    )
    gathered = lax.all_gather(block, ("fsdp", "dp"), axis=0, tiled=False)
    owners = gathered.shape[0]
    attention_full = gathered[:, :attention_rows].reshape(owners * attention_rows, D)
    feed_full = gathered[:, attention_rows:main_rows].reshape(owners * feed_rows, D)
    small_full = gathered[:, main_rows:].reshape(owners, extra_rows * D)[:, :small_count]
    return attention_full, feed_full, small_full.reshape(owners * small_count)


def flat_coordinates():
    me = lax.axis_index(("fsdp", "dp"))
    return me, me % 2, (me // 2) % 2, (me // 4) % 2, me // 8


def shifted(distance, count=32):
    return [(d, d + distance) for d in range(count) if 0 <= d + distance < count]


def flipped(mask, count=32):
    return [(d, d ^ mask) for d in range(count)]


def permute(arrays, pairs):
    return lax.ppermute(tuple(arrays), ("fsdp", "dp"), pairs)


def staged_reduce_scatter(arrays):
    me, y_place, core, x_place, z_place = flat_coordinates()
    blocks = [entries.reshape((4, 2, 2, 2) + entries.shape[1:]) for entries in arrays]
    keep = [lax.dynamic_index_in_dim(b, core, axis=2, keepdims=False) for b in blocks]
    send = [lax.dynamic_index_in_dim(b, 1 - core, axis=2, keepdims=False).astype(jnp.bfloat16) for b in blocks]
    received = permute(send, flipped(2))
    plane = [k.astype(jnp.float32) + r.astype(jnp.float32) for k, r in zip(keep, received)]

    def pick(entries, x_index, y_index):
        picked = lax.dynamic_index_in_dim(entries, x_index, axis=1, keepdims=False)
        return lax.dynamic_index_in_dim(picked, y_index, axis=1, keepdims=False)

    along_z = [pick(p, x_place, y_place) for p in plane]
    for mask, x_index, y_index in ((4, 1 - x_place, y_place), (1, x_place, 1 - y_place), (5, 1 - x_place, 1 - y_place)):
        got = permute([pick(p, x_index, y_index).astype(jnp.bfloat16) for p in plane], flipped(mask))
        along_z = [a + g.astype(jnp.float32) for a, g in zip(along_z, got)]
    owned = [lax.dynamic_index_in_dim(a, z_place, axis=0, keepdims=False) for a in along_z]
    for distance in (1, 2, 3):
        up = permute(
            [lax.dynamic_index_in_dim(a, jnp.minimum(z_place + distance, 3), axis=0, keepdims=False).astype(jnp.bfloat16) for a in along_z],
            shifted(8 * distance),
        )
        down = permute(
            [lax.dynamic_index_in_dim(a, jnp.maximum(z_place - distance, 0), axis=0, keepdims=False).astype(jnp.bfloat16) for a in along_z],
            shifted(-8 * distance),
        )
        owned = [o + u.astype(jnp.float32) + w.astype(jnp.float32) for o, u, w in zip(owned, up, down)]
    return owned


def staged_all_gather(arrays):
    me, y_place, core, x_place, z_place = flat_coordinates()
    slot = [lax.broadcasted_iota(jnp.int32, (4,) + (1,) * a.ndim, 0) for a in arrays]
    grown = [jnp.where(s == z_place, a[None], jnp.zeros((4,) + a.shape, a.dtype)) for s, a in zip(slot, arrays)]
    for distance in (1, 2, 3):
        from_below = permute(arrays, shifted(8 * distance))
        from_above = permute(arrays, shifted(-8 * distance))
        grown = [jnp.where(s == z_place - distance, b[None], g) for s, b, g in zip(slot, from_below, grown)]
        grown = [jnp.where(s == z_place + distance, b[None], g) for s, b, g in zip(slot, from_above, grown)]
    got_x = permute(grown, flipped(4))
    got_y = permute(grown, flipped(1))
    got_xy = permute(grown, flipped(5))
    planes = []
    for own, gx, gy, gxy in zip(grown, got_x, got_y, got_xy):
        shape = (own.shape[0], 2, 2) + own.shape[1:]
        xs = lax.broadcasted_iota(jnp.int32, (1, 2, 1) + (1,) * (own.ndim - 1), 1)
        ys = lax.broadcasted_iota(jnp.int32, (1, 1, 2) + (1,) * (own.ndim - 1), 2)
        same_x, same_y = xs == x_place, ys == y_place
        plane = jnp.where(
            same_x,
            jnp.where(same_y, own[:, None, None], gy[:, None, None]),
            jnp.where(same_y, gx[:, None, None], gxy[:, None, None]),
        )
        planes.append(jnp.broadcast_to(plane, shape))
    got_core = permute(planes, flipped(2))
    gathered = []
    for own, other in zip(planes, got_core):
        own = own[:, :, None]
        other = other[:, :, None]
        size = own.shape[2]
        shape = own.shape[:2] + (2,) + own.shape[3:]
        start = [0] * len(shape)
        start_other = [0] * len(shape)
        start[2] = core * size
        start_other[2] = (1 - core) * size
        full = jnp.zeros(shape, own.dtype)
        full = lax.dynamic_update_slice(full, own, start)
        full = lax.dynamic_update_slice(full, other, start_other)
        gathered.append(full.reshape((32 * full.shape[4],) + full.shape[5:]))
    return gathered


def staged_working(attention_master, feed_master, small_master):
    small_count = small_master.shape[0]
    small_row = jnp.zeros((1, D), jnp.bfloat16).at[0, :small_count].set(small_master.astype(jnp.bfloat16))
    attention_full, small_rows = staged_all_gather([attention_master.astype(jnp.bfloat16), small_row])
    small_full = small_rows[:, :small_count].reshape(32 * small_count)
    feed_full = lax.all_gather(feed_master.astype(jnp.bfloat16), ("fsdp", "dp"), axis=0, tiled=True)
    return attention_full, feed_full, small_full


def scatter_gradients(attention_pieces, feed_pieces, small_grad_all, partials, staged):
    owners = lax.psum(1, ("fsdp", "dp"))
    me = lax.axis_index(("fsdp", "dp"))
    attention_rows = sum(piece.shape[0] for piece in attention_pieces) // owners
    small_count = small_grad_all.shape[0] // owners
    feed_owned = lax.psum_scatter(feed_pieces, ("fsdp", "dp"), scatter_dimension=0, tiled=True)
    partials_high = partials.astype(jnp.bfloat16)
    partials_low = (partials - partials_high.astype(jnp.float32)).astype(jnp.bfloat16)
    split_partials = jnp.concatenate([partials_high, partials_low])
    slots = split_partials.shape[0]
    extra_count = small_count + owners * slots
    extra_rows = padded_rows(attention_rows + padded_rows(extra_count, D) // D, 16) - attention_rows
    slot_row = jnp.zeros((owners * slots,), jnp.bfloat16)
    slot_row = lax.dynamic_update_slice(slot_row, split_partials, (me * slots,))
    extra = jnp.concatenate(
        [
            small_grad_all.astype(jnp.bfloat16).reshape(owners, small_count),
            jnp.broadcast_to(slot_row[None], (owners, owners * slots)),
            jnp.zeros((owners, extra_rows * D - extra_count), jnp.bfloat16),
        ],
        axis=1,
    ).reshape(owners, extra_rows, D)
    block_rows = attention_rows + extra_rows
    if staged:
        attention_grad_all = jnp.concatenate(attention_pieces, axis=0).astype(jnp.bfloat16)
        owned = jnp.concatenate(
            staged_reduce_scatter([attention_grad_all.reshape(owners, attention_rows, D), extra]), axis=0
        )
    else:
        packed = jnp.zeros((owners, block_rows, D), jnp.bfloat16)
        packed = lax.dynamic_update_slice(packed, extra, (0, attention_rows, 0))
        owner = 0
        for piece in attention_pieces:
            piece_owners = piece.shape[0] // attention_rows
            packed = lax.dynamic_update_slice(
                packed, piece.astype(jnp.bfloat16).reshape(piece_owners, attention_rows, D), (owner, 0, 0)
            )
            owner = owner + piece_owners
        owned = lax.psum_scatter(
            packed.reshape(owners * block_rows, D), ("fsdp", "dp"), scatter_dimension=0, tiled=True
        ).astype(jnp.float32)
    attention_owned = owned[:attention_rows]
    extra_owned = owned[attention_rows:].reshape(extra_rows * D)
    small_owned = extra_owned[:small_count]
    gathered_partials = extra_owned[small_count:extra_count].reshape(owners, slots)
    half = slots // 2
    totals = gathered_partials[0, :half] + gathered_partials[0, half:]
    for index in range(1, owners):
        totals = totals + (gathered_partials[index, :half] + gathered_partials[index, half:])
    return attention_owned, feed_owned.astype(jnp.float32), small_owned, totals


def on_device(
    staged,
    tokens,
    cotangent,
    lengths,
    step_count,
    attention_master,
    attention_first,
    attention_second,
    feed_master,
    feed_first,
    feed_second,
    small_master,
    small_first,
    small_second,
):
    row_count = tokens.shape[0]
    sequence_count = row_count // SEQ
    if staged:
        attention_full, feed_full, small_full = staged_working(attention_master, feed_master, small_master)
    else:
        attention_full, feed_full, small_full = gather_working(attention_master, feed_master, small_master)
    key_valid = (
        lax.broadcasted_iota(jnp.int32, (sequence_count, SEQ), 1) < lengths[:, None]
    ).astype(jnp.float32)
    token_valid = key_valid.reshape(row_count)
    (
        query_bias,
        value_bias,
        output_bias,
        inner_bias,
        outer_bias,
        first_gain,
        first_shift,
        second_gain,
        second_shift,
    ) = split_small(small_full)
    queries = (product(tokens, attention_full[0:D]) + query_bias).astype(jnp.bfloat16)
    key_vectors = product(tokens, attention_full[D : 2 * D]).astype(jnp.bfloat16)
    values = (product(tokens, attention_full[2 * D : 3 * D]) + value_bias).astype(jnp.bfloat16)
    seq_shape = (sequence_count, SEQ, D)
    attended, log_total = lax.map(
        attend_forward,
        (
            queries.reshape(seq_shape),
            key_vectors.reshape(seq_shape),
            values.reshape(seq_shape),
            key_valid,
        ),
    )
    attended = attended.reshape(row_count, D)
    branch_attention = product(attended, attention_full[3 * D : 4 * D]) + output_bias
    first_sum = tokens.astype(jnp.float32) + branch_attention
    normed = layer_norm(first_sum, first_gain, first_shift)
    normed_low = normed.astype(jnp.bfloat16)
    inner_sum = product_cols(normed_low, feed_full[0:FF]) + inner_bias
    active = gelu_exact(inner_sum).astype(jnp.bfloat16)
    gelu_slope = gelu_derivative(inner_sum)
    branch_feed = product(active, feed_full[FF : 2 * FF]) + outer_bias
    residual = normed + branch_feed
    layer_out = layer_norm(residual, second_gain, second_shift).astype(jnp.bfloat16)
    column = token_valid[:, None]
    partials = jnp.stack(
        [
            jnp.sum(residual * residual * column),
            jnp.sum(branch_attention * branch_attention * column),
            jnp.sum(branch_feed * branch_feed * column),
            jnp.sum(token_valid),
        ]
    )
    query_weight = attention_full[0:D]
    key_weight = attention_full[D : 2 * D]
    value_weight = attention_full[2 * D : 3 * D]
    output_weight = attention_full[3 * D : 4 * D]
    outer_weight = feed_full[FF : 2 * FF]
    inner_weight = feed_full[0:FF]
    second_pull = jax.vjp(layer_norm, residual, second_gain, second_shift)[1]
    residual_grad, second_gain_grad, second_shift_grad = second_pull(cotangent)
    feed_out_grad = residual_grad.astype(jnp.bfloat16)
    outer_bias_grad = column_total(feed_out_grad)
    active_grad = product_cols(feed_out_grad, outer_weight)
    inner_grad = (active_grad * gelu_slope).astype(jnp.bfloat16)
    inner_bias_grad = column_total(inner_grad)
    feed_grad_all = (
        lax.dot_general(
            jnp.stack([inner_grad, active]),
            jnp.stack([normed_low, feed_out_grad]),
            (((1,), (1,)), ((0,), (0,))),
            preferred_element_type=jnp.float32,
        )
        .astype(jnp.bfloat16)
        .reshape(2 * FF, D)
    )
    feed_grad_all, inner_grad_late = lax.optimization_barrier((feed_grad_all, inner_grad))
    normed_grad = residual_grad + product(inner_grad_late, inner_weight)
    first_pull = jax.vjp(layer_norm, first_sum, first_gain, first_shift)[1]
    first_sum_grad, first_gain_grad, first_shift_grad = first_pull(normed_grad)
    branch_grad_low = first_sum_grad.astype(jnp.bfloat16)
    output_bias_grad = column_total(branch_grad_low)
    output_weight_grad = product_rows(attended, branch_grad_low)
    attended_grad = product_cols(branch_grad_low, output_weight).astype(jnp.bfloat16)
    query_grad, key_grad, value_grad = lax.map(
        attend_backward,
        (
            queries.reshape(seq_shape),
            key_vectors.reshape(seq_shape),
            values.reshape(seq_shape),
            key_valid,
            log_total,
            attended_grad.reshape(seq_shape),
        ),
    )
    query_grad = query_grad.reshape(row_count, D)
    key_grad = key_grad.reshape(row_count, D)
    value_grad = value_grad.reshape(row_count, D)
    query_weight_grad = product_rows(tokens, query_grad)
    key_weight_grad = product_rows(tokens, key_grad)
    value_weight_grad = product_rows(tokens, value_grad)
    query_bias_grad = column_total(query_grad)
    value_bias_grad = column_total(value_grad)
    tokens_grad = (
        first_sum_grad
        + product_cols(query_grad, query_weight)
        + product_cols(key_grad, key_weight)
        + product_cols(value_grad, value_weight)
    )
    small_grad_all = jnp.concatenate(
        [
            query_bias_grad,
            value_bias_grad,
            output_bias_grad,
            inner_bias_grad,
            outer_bias_grad,
            first_gain_grad,
            first_shift_grad,
            second_gain_grad,
            second_shift_grad,
        ]
    )
    attention_owned, feed_owned, small_owned, totals = scatter_gradients(
        [query_weight_grad, key_weight_grad, value_weight_grad, output_weight_grad],
        feed_grad_all,
        small_grad_all,
        partials,
        staged,
    )
    rms_values = jnp.sqrt(totals[:3] / (totals[3] * D))
    step_float = step_count[0].astype(jnp.float32)
    attention_new, attention_first_new, attention_second_new = adam_step(
        attention_master,
        attention_first,
        attention_second,
        attention_owned,
        rate_matrix,
        weight_decay,
        step_float,
    )
    feed_new, feed_first_new, feed_second_new = adam_step(
        feed_master, feed_first, feed_second, feed_owned, rate_matrix, weight_decay, step_float
    )
    small_new, small_first_new, small_second_new = adam_step(
        small_master, small_first, small_second, small_owned, rate_small, 0.0, step_float
    )
    return (
        layer_out,
        tokens_grad,
        attention_new,
        attention_first_new,
        attention_second_new,
        attention_new.astype(jnp.bfloat16),
        feed_new,
        feed_first_new,
        feed_second_new,
        feed_new.astype(jnp.bfloat16),
        small_new,
        small_first_new,
        small_second_new,
        small_new.astype(jnp.bfloat16),
        rms_values,
    )


def solution(mesh):
    placed = (
        P(("fsdp", "dp"), None),
        P(("fsdp", "dp"), None),
        P(("fsdp", "dp")),
        P(),
        P(("fsdp", "dp"), None),
        P(("fsdp", "dp"), None),
        P(("fsdp", "dp"), None),
        P(("fsdp", "dp"), None),
        P(("fsdp", "dp"), None),
        P(("fsdp", "dp"), None),
        P(("fsdp", "dp")),
        P(("fsdp", "dp")),
        P(("fsdp", "dp")),
    )
    staged = dict(mesh.shape) == {"fsdp": 16, "dp": 2}
    return jax.shard_map(
        functools.partial(on_device, staged),
        mesh=mesh,
        in_specs=placed,
        out_specs=(
            P(("fsdp", "dp"), None),
            P(("fsdp", "dp"), None),
            P(("fsdp", "dp"), None),
            P(("fsdp", "dp"), None),
            P(("fsdp", "dp"), None),
            P(("fsdp", "dp"), None),
            P(("fsdp", "dp"), None),
            P(("fsdp", "dp"), None),
            P(("fsdp", "dp"), None),
            P(("fsdp", "dp"), None),
            P(("fsdp", "dp")),
            P(("fsdp", "dp")),
            P(("fsdp", "dp")),
            P(("fsdp", "dp")),
            P(),
        ),
        check_vma=False,
    )
```

```python
import functools
import math

import jax
import numpy as np
import jax.numpy as jnp
from jax import lax
from jax.experimental import pallas as pl
from jax.sharding import PartitionSpec as P

D = 768
HEADS = 12
HDIM = 64
FF = 3072
SEQ = 512


ln_epsilon = 1e-12
beta_first = 0.5
beta_second = 0.55
adam_epsilon = 1e-06
rate_matrix = 0.04
rate_small = 0.25
weight_decay = 0.01


def product(left_side, right_side):
    return jnp.dot(left_side, right_side, preferred_element_type=jnp.float32)


def product_rows(left_side, right_side):
    return lax.dot_general(
        left_side, right_side, (((0,), (0,)), ((), ())), preferred_element_type=jnp.float32
    )


def product_cols(left_side, right_side):
    return lax.dot_general(
        left_side, right_side, (((1,), (1,)), ((), ())), preferred_element_type=jnp.float32
    )


def column_total(entries):
    return jnp.sum(entries, axis=0, dtype=jnp.float32)


def layer_norm(entries, norm_gain, norm_shift):
    center = jnp.mean(entries, axis=-1, keepdims=True)
    offset = entries - center
    spread = jnp.mean(offset * offset, axis=-1, keepdims=True)
    return offset * lax.rsqrt(spread + ln_epsilon) * norm_gain + norm_shift


def gelu_exact(entries):
    return jax.nn.gelu(entries, approximate=False)


def gelu_derivative(entries):
    sqrt_half = np.sqrt(0.5).astype(np.float32)
    shifted_entries = -entries * sqrt_half
    return 0.5 * lax.erfc(shifted_entries) + entries * (
        jnp.exp(-(shifted_entries * shifted_entries)) * np.float32(sqrt_half / np.sqrt(np.pi))
    )


def split_small(small_full):
    pieces = []
    position = 0
    for length in (D, D, D, FF, D, D, D, D, D):
        pieces.append(small_full[position : position + length].astype(jnp.float32))
        position = position + length
    return pieces


def head_view(entries):
    return entries.reshape(SEQ, HEADS, HDIM)


def masked_scores(queries, key_vectors, key_valid):
    scores = jnp.einsum(
        "qhd,khd->hqk",
        head_view(queries),
        head_view(key_vectors),
        preferred_element_type=jnp.float32,
    ) * (1.0 / math.sqrt(HDIM))
    return jnp.where(key_valid[None, None, :] > 0, scores, -1e30)


def attention_kernel(valid_ref, query_ref, key_ref, value_ref, out_ref, log_total_ref):
    valid = valid_ref[...] > 0
    heads_here = out_ref.shape[1] // HDIM
    outs = []
    for head in range(heads_here):
        columns = slice(head * HDIM, (head + 1) * HDIM)
        scores = lax.dot_general(
            query_ref[:, columns],
            key_ref[:, columns],
            (((1,), (1,)), ((), ())),
            preferred_element_type=jnp.float32,
        ) * (1.0 / math.sqrt(HDIM))
        scores = jnp.where(valid, scores, -1e30)
        row_max = jnp.max(scores, axis=1, keepdims=True)
        exponent = jnp.exp(scores - row_max)
        row_total = jnp.sum(exponent, axis=1, keepdims=True)
        probability = (exponent / row_total).astype(jnp.bfloat16)
        attended = jnp.dot(probability, value_ref[:, columns], preferred_element_type=jnp.float32)
        outs.append(attended.astype(jnp.bfloat16))
        log_total_ref[0, head : head + 1, :] = (row_max + jnp.log(row_total)).reshape(1, SEQ)
    out_ref[...] = jnp.concatenate(outs, axis=1)


def attend_forward(pieces):
    queries, key_vectors, values, key_valid = pieces
    groups = HEADS // 2
    cost = pl.CostEstimate(
        flops=4 * SEQ * SEQ * D,
        transcendentals=HEADS * SEQ * SEQ,
        bytes_accessed=4 * SEQ * D * 2 + HEADS * SEQ * 4,
    )
    attended, log_total = pl.pallas_call(
        attention_kernel,
        grid=(groups,),
        in_specs=[
            pl.BlockSpec((1, SEQ), lambda h: (0, 0)),
            pl.BlockSpec((SEQ, 2 * HDIM), lambda h: (0, h)),
            pl.BlockSpec((SEQ, 2 * HDIM), lambda h: (0, h)),
            pl.BlockSpec((SEQ, 2 * HDIM), lambda h: (0, h)),
        ],
        out_specs=[
            pl.BlockSpec((SEQ, 2 * HDIM), lambda h: (0, h)),
            pl.BlockSpec((1, 2, SEQ), lambda h: (h, 0, 0)),
        ],
        out_shape=[
            jax.ShapeDtypeStruct((SEQ, D), jnp.bfloat16),
            jax.ShapeDtypeStruct((groups, 2, SEQ), jnp.float32),
        ],
        cost_estimate=cost,
    )(key_valid.reshape(1, SEQ), queries, key_vectors, values)
    return attended, log_total.reshape(HEADS, SEQ)


def attend_backward(pieces):
    queries, key_vectors, values, key_valid, log_total, attended_grad = pieces
    scores = masked_scores(queries, key_vectors, key_valid)
    probability = jnp.exp(scores - log_total[:, :, None])
    probability_low = probability.astype(jnp.bfloat16)
    grad_heads = head_view(attended_grad)
    value_grad = jnp.einsum(
        "hqk,qhd->khd", probability_low, grad_heads, preferred_element_type=jnp.float32
    )
    probability_grad = jnp.einsum(
        "qhd,khd->hqk", grad_heads, head_view(values), preferred_element_type=jnp.float32
    )
    inner_total = jnp.sum(probability * probability_grad, axis=-1, keepdims=True)
    score_grad = (probability * (probability_grad - inner_total)).astype(jnp.bfloat16)
    score_scale = 1.0 / math.sqrt(HDIM)
    query_grad = (
        jnp.einsum(
            "hqk,khd->qhd", score_grad, head_view(key_vectors), preferred_element_type=jnp.float32
        )
        * score_scale
    )
    key_grad = (
        jnp.einsum(
            "hqk,qhd->khd", score_grad, head_view(queries), preferred_element_type=jnp.float32
        )
        * score_scale
    )
    return (
        query_grad.reshape(SEQ, D).astype(jnp.bfloat16),
        key_grad.reshape(SEQ, D).astype(jnp.bfloat16),
        value_grad.reshape(SEQ, D).astype(jnp.bfloat16),
    )


def adam_step(master, first_moment, second, gradient, step_rate, decay_rate, step_float):
    first_new = beta_first * first_moment + (1.0 - beta_first) * gradient
    second_new = beta_second * second + (1.0 - beta_second) * gradient * gradient
    first_hat = first_new / (1.0 - beta_first**step_float)
    second_hat = second_new / (1.0 - beta_second**step_float)
    master_new = master - step_rate * (
        first_hat / (jnp.sqrt(second_hat) + adam_epsilon) + decay_rate * master
    )
    return (master_new, first_new, second_new)


def padded_rows(rows, multiple):
    return -(-rows // multiple) * multiple


def gather_working(attention_master, feed_master, small_master):
    attention_rows = attention_master.shape[0]
    feed_rows = feed_master.shape[0]
    small_count = small_master.shape[0]
    main_rows = attention_rows + feed_rows
    extra_rows = padded_rows(main_rows + padded_rows(small_count, D) // D, 16) - main_rows
    small_flat = jnp.zeros((extra_rows * D,), jnp.bfloat16)
    small_flat = small_flat.at[:small_count].set(small_master.astype(jnp.bfloat16))
    block = jnp.concatenate(
        [
            attention_master.astype(jnp.bfloat16),
            feed_master.astype(jnp.bfloat16),
            small_flat.reshape(extra_rows, D),
        ],
        axis=0,
    )
    gathered = lax.all_gather(block, ("fsdp", "dp"), axis=0, tiled=False)
    owners = gathered.shape[0]
    attention_full = gathered[:, :attention_rows].reshape(owners * attention_rows, D)
    feed_full = gathered[:, attention_rows:main_rows].reshape(owners * feed_rows, D)
    small_full = gathered[:, main_rows:].reshape(owners, extra_rows * D)[:, :small_count]
    return attention_full, feed_full, small_full.reshape(owners * small_count)


def flat_coordinates():
    me = lax.axis_index(("fsdp", "dp"))
    return me, me % 2, (me // 2) % 2, (me // 4) % 2, me // 8


def shifted(distance, count=32):
    return [(d, d + distance) for d in range(count) if 0 <= d + distance < count]


def flipped(mask, count=32):
    return [(d, d ^ mask) for d in range(count)]


def permute(arrays, pairs):
    return lax.ppermute(tuple(arrays), ("fsdp", "dp"), pairs)


def staged_reduce_scatter(arrays):
    me, y_place, core, x_place, z_place = flat_coordinates()
    blocks = [entries.reshape((4, 2, 2, 2) + entries.shape[1:]) for entries in arrays]
    keep = [lax.dynamic_index_in_dim(b, core, axis=2, keepdims=False) for b in blocks]
    send = [lax.dynamic_index_in_dim(b, 1 - core, axis=2, keepdims=False).astype(jnp.bfloat16) for b in blocks]
    received = permute(send, flipped(2))
    plane = [k.astype(jnp.float32) + r.astype(jnp.float32) for k, r in zip(keep, received)]

    def pick(entries, x_index, y_index):
        picked = lax.dynamic_index_in_dim(entries, x_index, axis=1, keepdims=False)
        return lax.dynamic_index_in_dim(picked, y_index, axis=1, keepdims=False)

    along_z = [pick(p, x_place, y_place) for p in plane]
    for mask, x_index, y_index in ((4, 1 - x_place, y_place), (1, x_place, 1 - y_place), (5, 1 - x_place, 1 - y_place)):
        got = permute([pick(p, x_index, y_index).astype(jnp.bfloat16) for p in plane], flipped(mask))
        along_z = [a + g.astype(jnp.float32) for a, g in zip(along_z, got)]
    owned = [lax.dynamic_index_in_dim(a, z_place, axis=0, keepdims=False) for a in along_z]
    for distance in (1, 2, 3):
        up = permute(
            [lax.dynamic_index_in_dim(a, jnp.minimum(z_place + distance, 3), axis=0, keepdims=False).astype(jnp.bfloat16) for a in along_z],
            shifted(8 * distance),
        )
        down = permute(
            [lax.dynamic_index_in_dim(a, jnp.maximum(z_place - distance, 0), axis=0, keepdims=False).astype(jnp.bfloat16) for a in along_z],
            shifted(-8 * distance),
        )
        owned = [o + u.astype(jnp.float32) + w.astype(jnp.float32) for o, u, w in zip(owned, up, down)]
    return owned


def staged_all_gather(arrays):
    me, y_place, core, x_place, z_place = flat_coordinates()
    slot = [lax.broadcasted_iota(jnp.int32, (4,) + (1,) * a.ndim, 0) for a in arrays]
    grown = [jnp.where(s == z_place, a[None], jnp.zeros((4,) + a.shape, a.dtype)) for s, a in zip(slot, arrays)]
    for distance in (1, 2, 3):
        from_below = permute(arrays, shifted(8 * distance))
        from_above = permute(arrays, shifted(-8 * distance))
        grown = [jnp.where(s == z_place - distance, b[None], g) for s, b, g in zip(slot, from_below, grown)]
        grown = [jnp.where(s == z_place + distance, b[None], g) for s, b, g in zip(slot, from_above, grown)]
    got_x = permute(grown, flipped(4))
    got_y = permute(grown, flipped(1))
    got_xy = permute(grown, flipped(5))
    planes = []
    for own, gx, gy, gxy in zip(grown, got_x, got_y, got_xy):
        shape = (own.shape[0], 2, 2) + own.shape[1:]
        xs = lax.broadcasted_iota(jnp.int32, (1, 2, 1) + (1,) * (own.ndim - 1), 1)
        ys = lax.broadcasted_iota(jnp.int32, (1, 1, 2) + (1,) * (own.ndim - 1), 2)
        same_x, same_y = xs == x_place, ys == y_place
        plane = jnp.where(
            same_x,
            jnp.where(same_y, own[:, None, None], gy[:, None, None]),
            jnp.where(same_y, gx[:, None, None], gxy[:, None, None]),
        )
        planes.append(jnp.broadcast_to(plane, shape))
    got_core = permute(planes, flipped(2))
    gathered = []
    for own, other in zip(planes, got_core):
        own = own[:, :, None]
        other = other[:, :, None]
        size = own.shape[2]
        shape = own.shape[:2] + (2,) + own.shape[3:]
        start = [0] * len(shape)
        start_other = [0] * len(shape)
        start[2] = core * size
        start_other[2] = (1 - core) * size
        full = jnp.zeros(shape, own.dtype)
        full = lax.dynamic_update_slice(full, own, start)
        full = lax.dynamic_update_slice(full, other, start_other)
        gathered.append(full.reshape((32 * full.shape[4],) + full.shape[5:]))
    return gathered


def staged_working(attention_master, feed_master, small_master):
    small_count = small_master.shape[0]
    small_row = jnp.zeros((1, D), jnp.bfloat16).at[0, :small_count].set(small_master.astype(jnp.bfloat16))
    attention_full, small_rows = staged_all_gather([attention_master.astype(jnp.bfloat16), small_row])
    small_full = small_rows[:, :small_count].reshape(32 * small_count)
    feed_full = lax.all_gather(feed_master.astype(jnp.bfloat16), ("fsdp", "dp"), axis=0, tiled=True)
    return attention_full, feed_full, small_full


def scatter_gradients(attention_pieces, feed_pieces, small_grad_all, partials, staged):
    owners = lax.psum(1, ("fsdp", "dp"))
    me = lax.axis_index(("fsdp", "dp"))
    attention_rows = sum(piece.shape[0] for piece in attention_pieces) // owners
    small_count = small_grad_all.shape[0] // owners
    feed_owned = lax.psum_scatter(feed_pieces, ("fsdp", "dp"), scatter_dimension=0, tiled=True)
    partials_high = partials.astype(jnp.bfloat16)
    partials_low = (partials - partials_high.astype(jnp.float32)).astype(jnp.bfloat16)
    split_partials = jnp.concatenate([partials_high, partials_low])
    slots = split_partials.shape[0]
    extra_count = small_count + owners * slots
    extra_rows = padded_rows(attention_rows + padded_rows(extra_count, D) // D, 16) - attention_rows
    slot_row = jnp.zeros((owners * slots,), jnp.bfloat16)
    slot_row = lax.dynamic_update_slice(slot_row, split_partials, (me * slots,))
    extra = jnp.concatenate(
        [
            small_grad_all.astype(jnp.bfloat16).reshape(owners, small_count),
            jnp.broadcast_to(slot_row[None], (owners, owners * slots)),
            jnp.zeros((owners, extra_rows * D - extra_count), jnp.bfloat16),
        ],
        axis=1,
    ).reshape(owners, extra_rows, D)
    block_rows = attention_rows + extra_rows
    if staged:
        attention_grad_all = jnp.concatenate(attention_pieces, axis=0).astype(jnp.bfloat16)
        owned = jnp.concatenate(
            staged_reduce_scatter([attention_grad_all.reshape(owners, attention_rows, D), extra]), axis=0
        )
    else:
        packed = jnp.zeros((owners, block_rows, D), jnp.bfloat16)
        packed = lax.dynamic_update_slice(packed, extra, (0, attention_rows, 0))
        owner = 0
        for piece in attention_pieces:
            piece_owners = piece.shape[0] // attention_rows
            packed = lax.dynamic_update_slice(
                packed, piece.astype(jnp.bfloat16).reshape(piece_owners, attention_rows, D), (owner, 0, 0)
            )
            owner = owner + piece_owners
        owned = lax.psum_scatter(
            packed.reshape(owners * block_rows, D), ("fsdp", "dp"), scatter_dimension=0, tiled=True
        ).astype(jnp.float32)
    attention_owned = owned[:attention_rows]
    extra_owned = owned[attention_rows:].reshape(extra_rows * D)
    small_owned = extra_owned[:small_count]
    gathered_partials = extra_owned[small_count:extra_count].reshape(owners, slots)
    half = slots // 2
    totals = gathered_partials[0, :half] + gathered_partials[0, half:]
    for index in range(1, owners):
        totals = totals + (gathered_partials[index, :half] + gathered_partials[index, half:])
    return attention_owned, feed_owned.astype(jnp.float32), small_owned, totals


def on_device(
    staged,
    tokens,
    cotangent,
    lengths,
    step_count,
    attention_master,
    attention_first,
    attention_second,
    feed_master,
    feed_first,
    feed_second,
    small_master,
    small_first,
    small_second,
):
    row_count = tokens.shape[0]
    sequence_count = row_count // SEQ
    if staged:
        attention_full, feed_full, small_full = staged_working(attention_master, feed_master, small_master)
    else:
        attention_full, feed_full, small_full = gather_working(attention_master, feed_master, small_master)
    key_valid = (
        lax.broadcasted_iota(jnp.int32, (sequence_count, SEQ), 1) < lengths[:, None]
    ).astype(jnp.float32)
    token_valid = key_valid.reshape(row_count)
    (
        query_bias,
        value_bias,
        output_bias,
        inner_bias,
        outer_bias,
        first_gain,
        first_shift,
        second_gain,
        second_shift,
    ) = split_small(small_full)
    queries = (product(tokens, attention_full[0:D]) + query_bias).astype(jnp.bfloat16)
    key_vectors = product(tokens, attention_full[D : 2 * D]).astype(jnp.bfloat16)
    values = (product(tokens, attention_full[2 * D : 3 * D]) + value_bias).astype(jnp.bfloat16)
    seq_shape = (sequence_count, SEQ, D)
    attended, log_total = lax.map(
        attend_forward,
        (
            queries.reshape(seq_shape),
            key_vectors.reshape(seq_shape),
            values.reshape(seq_shape),
            key_valid,
        ),
    )
    attended = attended.reshape(row_count, D)
    branch_attention = product(attended, attention_full[3 * D : 4 * D]) + output_bias
    first_sum = tokens.astype(jnp.float32) + branch_attention
    normed = layer_norm(first_sum, first_gain, first_shift)
    normed_low = normed.astype(jnp.bfloat16)
    inner_sum = product_cols(normed_low, feed_full[0:FF]) + inner_bias
    active = gelu_exact(inner_sum).astype(jnp.bfloat16)
    gelu_slope = gelu_derivative(inner_sum)
    branch_feed = product(active, feed_full[FF : 2 * FF]) + outer_bias
    residual = normed + branch_feed
    layer_out = layer_norm(residual, second_gain, second_shift).astype(jnp.bfloat16)
    column = token_valid[:, None]
    partials = jnp.stack(
        [
            jnp.sum(residual * residual * column),
            jnp.sum(branch_attention * branch_attention * column),
            jnp.sum(branch_feed * branch_feed * column),
            jnp.sum(token_valid),
        ]
    )
    query_weight = attention_full[0:D]
    key_weight = attention_full[D : 2 * D]
    value_weight = attention_full[2 * D : 3 * D]
    output_weight = attention_full[3 * D : 4 * D]
    outer_weight = feed_full[FF : 2 * FF]
    inner_weight = feed_full[0:FF]
    second_pull = jax.vjp(layer_norm, residual, second_gain, second_shift)[1]
    residual_grad, second_gain_grad, second_shift_grad = second_pull(cotangent)
    feed_out_grad = residual_grad.astype(jnp.bfloat16)
    outer_bias_grad = column_total(feed_out_grad)
    active_grad = product_cols(feed_out_grad, outer_weight)
    inner_grad = (active_grad * gelu_slope).astype(jnp.bfloat16)
    inner_bias_grad = column_total(inner_grad)
    feed_grad_all = (
        lax.dot_general(
            jnp.stack([inner_grad, active]),
            jnp.stack([normed_low, feed_out_grad]),
            (((1,), (1,)), ((0,), (0,))),
            preferred_element_type=jnp.float32,
        )
        .astype(jnp.bfloat16)
        .reshape(2 * FF, D)
    )
    feed_grad_all, inner_grad_late = lax.optimization_barrier((feed_grad_all, inner_grad))
    normed_grad = residual_grad + product(inner_grad_late, inner_weight)
    first_pull = jax.vjp(layer_norm, first_sum, first_gain, first_shift)[1]
    first_sum_grad, first_gain_grad, first_shift_grad = first_pull(normed_grad)
    branch_grad_low = first_sum_grad.astype(jnp.bfloat16)
    output_bias_grad = column_total(branch_grad_low)
    output_weight_grad = product_rows(attended, branch_grad_low)
    attended_grad = product_cols(branch_grad_low, output_weight).astype(jnp.bfloat16)
    query_grad, key_grad, value_grad = lax.map(
        attend_backward,
        (
            queries.reshape(seq_shape),
            key_vectors.reshape(seq_shape),
            values.reshape(seq_shape),
            key_valid,
            log_total,
            attended_grad.reshape(seq_shape),
        ),
    )
    query_grad = query_grad.reshape(row_count, D)
    key_grad = key_grad.reshape(row_count, D)
    value_grad = value_grad.reshape(row_count, D)
    query_weight_grad = product_rows(tokens, query_grad)
    key_weight_grad = product_rows(tokens, key_grad)
    value_weight_grad = product_rows(tokens, value_grad)
    query_bias_grad = column_total(query_grad)
    value_bias_grad = column_total(value_grad)
    tokens_grad = (
        first_sum_grad
        + product_cols(query_grad, query_weight)
        + product_cols(key_grad, key_weight)
        + product_cols(value_grad, value_weight)
    )
    small_grad_all = jnp.concatenate(
        [
            query_bias_grad,
            value_bias_grad,
            output_bias_grad,
            inner_bias_grad,
            outer_bias_grad,
            first_gain_grad,
            first_shift_grad,
            second_gain_grad,
            second_shift_grad,
        ]
    )
    attention_owned, feed_owned, small_owned, totals = scatter_gradients(
        [query_weight_grad, key_weight_grad, value_weight_grad, output_weight_grad],
        feed_grad_all,
        small_grad_all,
        partials,
        staged,
    )
    rms_values = jnp.sqrt(totals[:3] / (totals[3] * D))
    step_float = step_count[0].astype(jnp.float32)
    attention_new, attention_first_new, attention_second_new = adam_step(
        attention_master,
        attention_first,
        attention_second,
        attention_owned,
        rate_matrix,
        weight_decay,
        step_float,
    )
    feed_new, feed_first_new, feed_second_new = adam_step(
        feed_master, feed_first, feed_second, feed_owned, rate_matrix, weight_decay, step_float
    )
    small_new, small_first_new, small_second_new = adam_step(
        small_master, small_first, small_second, small_owned, rate_small, 0.0, step_float
    )
    return (
        layer_out,
        tokens_grad,
        attention_new,
        attention_first_new,
        attention_second_new,
        attention_new.astype(jnp.bfloat16),
        feed_new,
        feed_first_new,
        feed_second_new,
        feed_new.astype(jnp.bfloat16),
        small_new,
        small_first_new,
        small_second_new,
        small_new.astype(jnp.bfloat16),
        rms_values,
    )


def solution(mesh):
    placed = (
        P(("fsdp", "dp"), None),
        P(("fsdp", "dp"), None),
        P(("fsdp", "dp")),
        P(),
        P(("fsdp", "dp"), None),
        P(("fsdp", "dp"), None),
        P(("fsdp", "dp"), None),
        P(("fsdp", "dp"), None),
        P(("fsdp", "dp"), None),
        P(("fsdp", "dp"), None),
        P(("fsdp", "dp")),
        P(("fsdp", "dp")),
        P(("fsdp", "dp")),
    )
    staged = dict(mesh.shape) == {"fsdp": 16, "dp": 2}
    return jax.shard_map(
        functools.partial(on_device, staged),
        mesh=mesh,
        in_specs=placed,
        out_specs=(
            P(("fsdp", "dp"), None),
            P(("fsdp", "dp"), None),
            P(("fsdp", "dp"), None),
            P(("fsdp", "dp"), None),
            P(("fsdp", "dp"), None),
            P(("fsdp", "dp"), None),
            P(("fsdp", "dp"), None),
            P(("fsdp", "dp"), None),
            P(("fsdp", "dp"), None),
            P(("fsdp", "dp"), None),
            P(("fsdp", "dp")),
            P(("fsdp", "dp")),
            P(("fsdp", "dp")),
            P(("fsdp", "dp")),
            P(),
        ),
        check_vma=False,
    )
```

```python
import functools
import math

import jax
import numpy as np
import jax.numpy as jnp
from jax import lax
from jax.sharding import PartitionSpec as P

D = 768
HEADS = 12
HDIM = 64
FF = 3072
SEQ = 512


ln_epsilon = 1e-12
beta_first = 0.5
beta_second = 0.55
adam_epsilon = 1e-06
rate_matrix = 0.04
rate_small = 0.25
weight_decay = 0.01


def product(left_side, right_side):
    return jnp.dot(left_side, right_side, preferred_element_type=jnp.float32)


def product_rows(left_side, right_side):
    return lax.dot_general(
        left_side, right_side, (((0,), (0,)), ((), ())), preferred_element_type=jnp.float32
    )


def product_cols(left_side, right_side):
    return lax.dot_general(
        left_side, right_side, (((1,), (1,)), ((), ())), preferred_element_type=jnp.float32
    )


def column_total(entries):
    return jnp.sum(entries, axis=0, dtype=jnp.float32)


def layer_norm(entries, norm_gain, norm_shift):
    center = jnp.mean(entries, axis=-1, keepdims=True)
    offset = entries - center
    spread = jnp.mean(offset * offset, axis=-1, keepdims=True)
    return offset * lax.rsqrt(spread + ln_epsilon) * norm_gain + norm_shift


def gelu_exact(entries):
    return jax.nn.gelu(entries, approximate=False)


def gelu_derivative(entries):
    sqrt_half = np.sqrt(0.5).astype(np.float32)
    shifted_entries = -entries * sqrt_half
    return 0.5 * lax.erfc(shifted_entries) + entries * (
        jnp.exp(-(shifted_entries * shifted_entries)) * np.float32(sqrt_half / np.sqrt(np.pi))
    )


def split_small(small_full):
    pieces = []
    position = 0
    for length in (D, D, D, FF, D, D, D, D, D):
        pieces.append(small_full[position : position + length].astype(jnp.float32))
        position = position + length
    return pieces


def head_view(entries):
    return entries.reshape(SEQ, HEADS, HDIM)


def masked_scores(queries, key_vectors, key_valid):
    scores = jnp.einsum(
        "qhd,khd->hqk",
        head_view(queries),
        head_view(key_vectors),
        preferred_element_type=jnp.float32,
    ) * (1.0 / math.sqrt(HDIM))
    return jnp.where(key_valid[None, None, :] > 0, scores, -1e30)


def attend_forward(pieces):
    queries, key_vectors, values, key_valid = pieces
    scores = masked_scores(queries, key_vectors, key_valid)
    row_max = jnp.max(scores, axis=-1, keepdims=True)
    exponent = jnp.exp(scores - row_max)
    row_total = jnp.sum(exponent, axis=-1, keepdims=True)
    probability = (exponent / row_total).astype(jnp.bfloat16)
    attended = jnp.einsum(
        "hqk,khd->qhd", probability, head_view(values), preferred_element_type=jnp.float32
    )
    return (attended.reshape(SEQ, D).astype(jnp.bfloat16), (row_max + jnp.log(row_total))[:, :, 0])


def attend_backward(pieces):
    queries, key_vectors, values, key_valid, log_total, attended_grad = pieces
    scores = masked_scores(queries, key_vectors, key_valid)
    probability = jnp.exp(scores - log_total[:, :, None])
    probability_low = probability.astype(jnp.bfloat16)
    grad_heads = head_view(attended_grad)
    value_grad = jnp.einsum(
        "hqk,qhd->khd", probability_low, grad_heads, preferred_element_type=jnp.float32
    )
    probability_grad = jnp.einsum(
        "qhd,khd->hqk", grad_heads, head_view(values), preferred_element_type=jnp.float32
    )
    inner_total = jnp.sum(probability * probability_grad, axis=-1, keepdims=True)
    score_grad = (probability * (probability_grad - inner_total)).astype(jnp.bfloat16)
    score_scale = 1.0 / math.sqrt(HDIM)
    query_grad = (
        jnp.einsum(
            "hqk,khd->qhd", score_grad, head_view(key_vectors), preferred_element_type=jnp.float32
        )
        * score_scale
    )
    key_grad = (
        jnp.einsum(
            "hqk,qhd->khd", score_grad, head_view(queries), preferred_element_type=jnp.float32
        )
        * score_scale
    )
    return (
        query_grad.reshape(SEQ, D).astype(jnp.bfloat16),
        key_grad.reshape(SEQ, D).astype(jnp.bfloat16),
        value_grad.reshape(SEQ, D).astype(jnp.bfloat16),
    )


def adam_step(master, first_moment, second, gradient, step_rate, decay_rate, step_float):
    first_new = beta_first * first_moment + (1.0 - beta_first) * gradient
    second_new = beta_second * second + (1.0 - beta_second) * gradient * gradient
    first_hat = first_new / (1.0 - beta_first**step_float)
    second_hat = second_new / (1.0 - beta_second**step_float)
    master_new = master - step_rate * (
        first_hat / (jnp.sqrt(second_hat) + adam_epsilon) + decay_rate * master
    )
    return (master_new, first_new, second_new)


def padded_rows(rows, multiple):
    return -(-rows // multiple) * multiple


def gather_working(attention_master, feed_master, small_master):
    attention_rows = attention_master.shape[0]
    feed_rows = feed_master.shape[0]
    small_count = small_master.shape[0]
    main_rows = attention_rows + feed_rows
    extra_rows = padded_rows(main_rows + padded_rows(small_count, D) // D, 16) - main_rows
    small_flat = jnp.zeros((extra_rows * D,), jnp.bfloat16)
    small_flat = small_flat.at[:small_count].set(small_master.astype(jnp.bfloat16))
    block = jnp.concatenate(
        [
            attention_master.astype(jnp.bfloat16),
            feed_master.astype(jnp.bfloat16),
            small_flat.reshape(extra_rows, D),
        ],
        axis=0,
    )
    gathered = lax.all_gather(block, ("fsdp", "dp"), axis=0, tiled=False)
    owners = gathered.shape[0]
    attention_full = gathered[:, :attention_rows].reshape(owners * attention_rows, D)
    feed_full = gathered[:, attention_rows:main_rows].reshape(owners * feed_rows, D)
    small_full = gathered[:, main_rows:].reshape(owners, extra_rows * D)[:, :small_count]
    return attention_full, feed_full, small_full.reshape(owners * small_count)


def flat_coordinates():
    me = lax.axis_index(("fsdp", "dp"))
    return me, me % 2, (me // 2) % 2, (me // 4) % 2, me // 8


def shifted(distance, count=32):
    return [(d, d + distance) for d in range(count) if 0 <= d + distance < count]


def flipped(mask, count=32):
    return [(d, d ^ mask) for d in range(count)]


def permute(arrays, pairs):
    return lax.ppermute(tuple(arrays), ("fsdp", "dp"), pairs)


def staged_reduce_scatter(arrays):
    me, y_place, core, x_place, z_place = flat_coordinates()
    blocks = [entries.reshape((4, 2, 2, 2) + entries.shape[1:]) for entries in arrays]
    keep = [lax.dynamic_index_in_dim(b, core, axis=2, keepdims=False) for b in blocks]
    send = [lax.dynamic_index_in_dim(b, 1 - core, axis=2, keepdims=False).astype(jnp.bfloat16) for b in blocks]
    received = permute(send, flipped(2))
    plane = [k.astype(jnp.float32) + r.astype(jnp.float32) for k, r in zip(keep, received)]

    def pick(entries, x_index, y_index):
        picked = lax.dynamic_index_in_dim(entries, x_index, axis=1, keepdims=False)
        return lax.dynamic_index_in_dim(picked, y_index, axis=1, keepdims=False)

    along_z = [pick(p, x_place, y_place) for p in plane]
    for mask, x_index, y_index in ((4, 1 - x_place, y_place), (1, x_place, 1 - y_place), (5, 1 - x_place, 1 - y_place)):
        got = permute([pick(p, x_index, y_index).astype(jnp.bfloat16) for p in plane], flipped(mask))
        along_z = [a + g.astype(jnp.float32) for a, g in zip(along_z, got)]
    owned = [lax.dynamic_index_in_dim(a, z_place, axis=0, keepdims=False) for a in along_z]
    for distance in (1, 2, 3):
        up = permute(
            [lax.dynamic_index_in_dim(a, jnp.minimum(z_place + distance, 3), axis=0, keepdims=False).astype(jnp.bfloat16) for a in along_z],
            shifted(8 * distance),
        )
        down = permute(
            [lax.dynamic_index_in_dim(a, jnp.maximum(z_place - distance, 0), axis=0, keepdims=False).astype(jnp.bfloat16) for a in along_z],
            shifted(-8 * distance),
        )
        owned = [o + u.astype(jnp.float32) + w.astype(jnp.float32) for o, u, w in zip(owned, up, down)]
    return owned


def staged_all_gather(arrays):
    me, y_place, core, x_place, z_place = flat_coordinates()
    slot = [lax.broadcasted_iota(jnp.int32, (4,) + (1,) * a.ndim, 0) for a in arrays]
    grown = [jnp.where(s == z_place, a[None], jnp.zeros((4,) + a.shape, a.dtype)) for s, a in zip(slot, arrays)]
    for distance in (1, 2, 3):
        from_below = permute(arrays, shifted(8 * distance))
        from_above = permute(arrays, shifted(-8 * distance))
        grown = [jnp.where(s == z_place - distance, b[None], g) for s, b, g in zip(slot, from_below, grown)]
        grown = [jnp.where(s == z_place + distance, b[None], g) for s, b, g in zip(slot, from_above, grown)]
    got_x = permute(grown, flipped(4))
    got_y = permute(grown, flipped(1))
    got_xy = permute(grown, flipped(5))
    planes = []
    for own, gx, gy, gxy in zip(grown, got_x, got_y, got_xy):
        shape = (own.shape[0], 2, 2) + own.shape[1:]
        xs = lax.broadcasted_iota(jnp.int32, (1, 2, 1) + (1,) * (own.ndim - 1), 1)
        ys = lax.broadcasted_iota(jnp.int32, (1, 1, 2) + (1,) * (own.ndim - 1), 2)
        same_x, same_y = xs == x_place, ys == y_place
        plane = jnp.where(
            same_x,
            jnp.where(same_y, own[:, None, None], gy[:, None, None]),
            jnp.where(same_y, gx[:, None, None], gxy[:, None, None]),
        )
        planes.append(jnp.broadcast_to(plane, shape))
    got_core = permute(planes, flipped(2))
    gathered = []
    for own, other in zip(planes, got_core):
        own = own[:, :, None]
        other = other[:, :, None]
        size = own.shape[2]
        shape = own.shape[:2] + (2,) + own.shape[3:]
        start = [0] * len(shape)
        start_other = [0] * len(shape)
        start[2] = core * size
        start_other[2] = (1 - core) * size
        full = jnp.zeros(shape, own.dtype)
        full = lax.dynamic_update_slice(full, own, start)
        full = lax.dynamic_update_slice(full, other, start_other)
        gathered.append(full.reshape((32 * full.shape[4],) + full.shape[5:]))
    return gathered


def staged_working(attention_master, feed_master, small_master):
    small_count = small_master.shape[0]
    small_row = jnp.zeros((1, D), jnp.bfloat16).at[0, :small_count].set(small_master.astype(jnp.bfloat16))
    attention_full, small_rows = staged_all_gather([attention_master.astype(jnp.bfloat16), small_row])
    small_full = small_rows[:, :small_count].reshape(32 * small_count)
    feed_full = lax.all_gather(feed_master.astype(jnp.bfloat16), ("fsdp", "dp"), axis=0, tiled=True)
    return attention_full, feed_full, small_full


def scatter_gradients(attention_pieces, feed_pieces, small_grad_all, partials, staged):
    owners = lax.psum(1, ("fsdp", "dp"))
    me = lax.axis_index(("fsdp", "dp"))
    attention_rows = sum(piece.shape[0] for piece in attention_pieces) // owners
    small_count = small_grad_all.shape[0] // owners
    if staged:
        feed_rows = feed_pieces.shape[0] // owners
        dp = lax.axis_index("dp")
        within = lax.psum_scatter(
            feed_pieces.reshape(owners // 2, 2 * feed_rows, D), "fsdp", scatter_dimension=0, tiled=True
        ).reshape(2, feed_rows, D)
        keep = lax.dynamic_index_in_dim(within, dp, axis=0, keepdims=False)
        send = lax.dynamic_index_in_dim(within, 1 - dp, axis=0, keepdims=False)
        feed_owned = keep.astype(jnp.float32) + lax.ppermute(send, "dp", [(0, 1), (1, 0)]).astype(jnp.float32)
    else:
        feed_owned = lax.psum_scatter(feed_pieces, ("fsdp", "dp"), scatter_dimension=0, tiled=True)
    partials_high = partials.astype(jnp.bfloat16)
    partials_low = (partials - partials_high.astype(jnp.float32)).astype(jnp.bfloat16)
    split_partials = jnp.concatenate([partials_high, partials_low])
    slots = split_partials.shape[0]
    extra_count = small_count + owners * slots
    extra_rows = padded_rows(attention_rows + padded_rows(extra_count, D) // D, 16) - attention_rows
    slot_row = jnp.zeros((owners * slots,), jnp.bfloat16)
    slot_row = lax.dynamic_update_slice(slot_row, split_partials, (me * slots,))
    extra = jnp.concatenate(
        [
            small_grad_all.astype(jnp.bfloat16).reshape(owners, small_count),
            jnp.broadcast_to(slot_row[None], (owners, owners * slots)),
            jnp.zeros((owners, extra_rows * D - extra_count), jnp.bfloat16),
        ],
        axis=1,
    ).reshape(owners, extra_rows, D)
    block_rows = attention_rows + extra_rows
    if staged:
        attention_grad_all = jnp.concatenate(attention_pieces, axis=0).astype(jnp.bfloat16)
        owned = jnp.concatenate(
            staged_reduce_scatter([attention_grad_all.reshape(owners, attention_rows, D), extra]), axis=0
        )
    else:
        packed = jnp.zeros((owners, block_rows, D), jnp.bfloat16)
        packed = lax.dynamic_update_slice(packed, extra, (0, attention_rows, 0))
        owner = 0
        for piece in attention_pieces:
            piece_owners = piece.shape[0] // attention_rows
            packed = lax.dynamic_update_slice(
                packed, piece.astype(jnp.bfloat16).reshape(piece_owners, attention_rows, D), (owner, 0, 0)
            )
            owner = owner + piece_owners
        owned = lax.psum_scatter(
            packed.reshape(owners * block_rows, D), ("fsdp", "dp"), scatter_dimension=0, tiled=True
        ).astype(jnp.float32)
    attention_owned = owned[:attention_rows]
    extra_owned = owned[attention_rows:].reshape(extra_rows * D)
    small_owned = extra_owned[:small_count]
    gathered_partials = extra_owned[small_count:extra_count].reshape(owners, slots)
    half = slots // 2
    totals = gathered_partials[0, :half] + gathered_partials[0, half:]
    for index in range(1, owners):
        totals = totals + (gathered_partials[index, :half] + gathered_partials[index, half:])
    return attention_owned, feed_owned.astype(jnp.float32), small_owned, totals


def on_device(
    staged,
    tokens,
    cotangent,
    lengths,
    step_count,
    attention_master,
    attention_first,
    attention_second,
    feed_master,
    feed_first,
    feed_second,
    small_master,
    small_first,
    small_second,
):
    row_count = tokens.shape[0]
    sequence_count = row_count // SEQ
    if staged:
        attention_full, feed_full, small_full = staged_working(attention_master, feed_master, small_master)
    else:
        attention_full, feed_full, small_full = gather_working(attention_master, feed_master, small_master)
    key_valid = (
        lax.broadcasted_iota(jnp.int32, (sequence_count, SEQ), 1) < lengths[:, None]
    ).astype(jnp.float32)
    token_valid = key_valid.reshape(row_count)
    (
        query_bias,
        value_bias,
        output_bias,
        inner_bias,
        outer_bias,
        first_gain,
        first_shift,
        second_gain,
        second_shift,
    ) = split_small(small_full)
    queries = (product(tokens, attention_full[0:D]) + query_bias).astype(jnp.bfloat16)
    key_vectors = product(tokens, attention_full[D : 2 * D]).astype(jnp.bfloat16)
    values = (product(tokens, attention_full[2 * D : 3 * D]) + value_bias).astype(jnp.bfloat16)
    seq_shape = (sequence_count, SEQ, D)
    attended, log_total = lax.map(
        attend_forward,
        (
            queries.reshape(seq_shape),
            key_vectors.reshape(seq_shape),
            values.reshape(seq_shape),
            key_valid,
        ),
    )
    attended = attended.reshape(row_count, D)
    branch_attention = product(attended, attention_full[3 * D : 4 * D]) + output_bias
    first_sum = tokens.astype(jnp.float32) + branch_attention
    normed = layer_norm(first_sum, first_gain, first_shift)
    normed_low = normed.astype(jnp.bfloat16)
    inner_sum = product_cols(normed_low, feed_full[0:FF]) + inner_bias
    active = gelu_exact(inner_sum).astype(jnp.bfloat16)
    gelu_slope = gelu_derivative(inner_sum)
    branch_feed = product(active, feed_full[FF : 2 * FF]) + outer_bias
    residual = normed + branch_feed
    layer_out = layer_norm(residual, second_gain, second_shift).astype(jnp.bfloat16)
    column = token_valid[:, None]
    partials = jnp.stack(
        [
            jnp.sum(residual * residual * column),
            jnp.sum(branch_attention * branch_attention * column),
            jnp.sum(branch_feed * branch_feed * column),
            jnp.sum(token_valid),
        ]
    )
    query_weight = attention_full[0:D]
    key_weight = attention_full[D : 2 * D]
    value_weight = attention_full[2 * D : 3 * D]
    output_weight = attention_full[3 * D : 4 * D]
    outer_weight = feed_full[FF : 2 * FF]
    inner_weight = feed_full[0:FF]
    second_pull = jax.vjp(layer_norm, residual, second_gain, second_shift)[1]
    residual_grad, second_gain_grad, second_shift_grad = second_pull(cotangent)
    feed_out_grad = residual_grad.astype(jnp.bfloat16)
    outer_bias_grad = column_total(feed_out_grad)
    active_grad = product_cols(feed_out_grad, outer_weight)
    inner_grad = (active_grad * gelu_slope).astype(jnp.bfloat16)
    inner_bias_grad = column_total(inner_grad)
    feed_grad_all = (
        lax.dot_general(
            jnp.stack([inner_grad, active]),
            jnp.stack([normed_low, feed_out_grad]),
            (((1,), (1,)), ((0,), (0,))),
            preferred_element_type=jnp.float32,
        )
        .astype(jnp.bfloat16)
        .reshape(2 * FF, D)
    )
    feed_grad_all, inner_grad_late = lax.optimization_barrier((feed_grad_all, inner_grad))
    normed_grad = residual_grad + product(inner_grad_late, inner_weight)
    first_pull = jax.vjp(layer_norm, first_sum, first_gain, first_shift)[1]
    first_sum_grad, first_gain_grad, first_shift_grad = first_pull(normed_grad)
    branch_grad_low = first_sum_grad.astype(jnp.bfloat16)
    output_bias_grad = column_total(branch_grad_low)
    output_weight_grad = product_rows(attended, branch_grad_low)
    attended_grad = product_cols(branch_grad_low, output_weight).astype(jnp.bfloat16)
    query_grad, key_grad, value_grad = lax.map(
        attend_backward,
        (
            queries.reshape(seq_shape),
            key_vectors.reshape(seq_shape),
            values.reshape(seq_shape),
            key_valid,
            log_total,
            attended_grad.reshape(seq_shape),
        ),
    )
    query_grad = query_grad.reshape(row_count, D)
    key_grad = key_grad.reshape(row_count, D)
    value_grad = value_grad.reshape(row_count, D)
    query_weight_grad = product_rows(tokens, query_grad)
    key_weight_grad = product_rows(tokens, key_grad)
    value_weight_grad = product_rows(tokens, value_grad)
    query_bias_grad = column_total(query_grad)
    value_bias_grad = column_total(value_grad)
    tokens_grad = (
        first_sum_grad
        + product_cols(query_grad, query_weight)
        + product_cols(key_grad, key_weight)
        + product_cols(value_grad, value_weight)
    )
    small_grad_all = jnp.concatenate(
        [
            query_bias_grad,
            value_bias_grad,
            output_bias_grad,
            inner_bias_grad,
            outer_bias_grad,
            first_gain_grad,
            first_shift_grad,
            second_gain_grad,
            second_shift_grad,
        ]
    )
    attention_owned, feed_owned, small_owned, totals = scatter_gradients(
        [query_weight_grad, key_weight_grad, value_weight_grad, output_weight_grad],
        feed_grad_all,
        small_grad_all,
        partials,
        staged,
    )
    rms_values = jnp.sqrt(totals[:3] / (totals[3] * D))
    step_float = step_count[0].astype(jnp.float32)
    attention_new, attention_first_new, attention_second_new = adam_step(
        attention_master,
        attention_first,
        attention_second,
        attention_owned,
        rate_matrix,
        weight_decay,
        step_float,
    )
    feed_new, feed_first_new, feed_second_new = adam_step(
        feed_master, feed_first, feed_second, feed_owned, rate_matrix, weight_decay, step_float
    )
    small_new, small_first_new, small_second_new = adam_step(
        small_master, small_first, small_second, small_owned, rate_small, 0.0, step_float
    )
    return (
        layer_out,
        tokens_grad,
        attention_new,
        attention_first_new,
        attention_second_new,
        attention_new.astype(jnp.bfloat16),
        feed_new,
        feed_first_new,
        feed_second_new,
        feed_new.astype(jnp.bfloat16),
        small_new,
        small_first_new,
        small_second_new,
        small_new.astype(jnp.bfloat16),
        rms_values,
    )


def solution(mesh):
    placed = (
        P(("fsdp", "dp"), None),
        P(("fsdp", "dp"), None),
        P(("fsdp", "dp")),
        P(),
        P(("fsdp", "dp"), None),
        P(("fsdp", "dp"), None),
        P(("fsdp", "dp"), None),
        P(("fsdp", "dp"), None),
        P(("fsdp", "dp"), None),
        P(("fsdp", "dp"), None),
        P(("fsdp", "dp")),
        P(("fsdp", "dp")),
        P(("fsdp", "dp")),
    )
    staged = dict(mesh.shape) == {"fsdp": 16, "dp": 2}
    return jax.shard_map(
        functools.partial(on_device, staged),
        mesh=mesh,
        in_specs=placed,
        out_specs=(
            P(("fsdp", "dp"), None),
            P(("fsdp", "dp"), None),
            P(("fsdp", "dp"), None),
            P(("fsdp", "dp"), None),
            P(("fsdp", "dp"), None),
            P(("fsdp", "dp"), None),
            P(("fsdp", "dp"), None),
            P(("fsdp", "dp"), None),
            P(("fsdp", "dp"), None),
            P(("fsdp", "dp"), None),
            P(("fsdp", "dp")),
            P(("fsdp", "dp")),
            P(("fsdp", "dp")),
            P(("fsdp", "dp")),
            P(),
        ),
        check_vma=False,
    )
```

```python
import functools
import math

import jax
import numpy as np
import jax.numpy as jnp
from jax import lax
from jax.sharding import PartitionSpec as P

D = 768
HEADS = 12
HDIM = 64
FF = 3072
SEQ = 512


ln_epsilon = 1e-12
beta_first = 0.5
beta_second = 0.55
adam_epsilon = 1e-06
rate_matrix = 0.04
rate_small = 0.25
weight_decay = 0.01


def product(left_side, right_side):
    return jnp.dot(left_side, right_side, preferred_element_type=jnp.float32)


def product_rows(left_side, right_side):
    return lax.dot_general(
        left_side, right_side, (((0,), (0,)), ((), ())), preferred_element_type=jnp.float32
    )


def product_cols(left_side, right_side):
    return lax.dot_general(
        left_side, right_side, (((1,), (1,)), ((), ())), preferred_element_type=jnp.float32
    )


def column_total(entries):
    return jnp.sum(entries, axis=0, dtype=jnp.float32)


def layer_norm(entries, norm_gain, norm_shift):
    center = jnp.mean(entries, axis=-1, keepdims=True)
    offset = entries - center
    spread = jnp.mean(offset * offset, axis=-1, keepdims=True)
    return offset * lax.rsqrt(spread + ln_epsilon) * norm_gain + norm_shift


def gelu_exact(entries):
    return jax.nn.gelu(entries, approximate=False)


def gelu_derivative(entries):
    sqrt_half = np.sqrt(0.5).astype(np.float32)
    shifted_entries = -entries * sqrt_half
    return 0.5 * lax.erfc(shifted_entries) + entries * (
        jnp.exp(-(shifted_entries * shifted_entries)) * np.float32(sqrt_half / np.sqrt(np.pi))
    )


def split_small(small_full):
    pieces = []
    position = 0
    for length in (D, D, D, FF, D, D, D, D, D):
        pieces.append(small_full[position : position + length].astype(jnp.float32))
        position = position + length
    return pieces


def head_view(entries):
    return entries.reshape(SEQ, -1, HDIM)


def masked_scores(queries, key_vectors, key_valid):
    scores = jnp.einsum(
        "qhd,khd->hqk",
        head_view(queries),
        head_view(key_vectors),
        preferred_element_type=jnp.float32,
    ) * (1.0 / math.sqrt(HDIM))
    return jnp.where(key_valid[None, None, :] > 0, scores, -1e30)


def attend_forward(pieces):
    queries, key_vectors, values, key_valid = pieces
    scores = masked_scores(queries, key_vectors, key_valid)
    row_max = jnp.max(scores, axis=-1, keepdims=True)
    exponent = jnp.exp(scores - row_max)
    row_total = jnp.sum(exponent, axis=-1, keepdims=True)
    probability = (exponent / row_total).astype(jnp.bfloat16)
    attended = jnp.einsum(
        "hqk,khd->qhd", probability, head_view(values), preferred_element_type=jnp.float32
    )
    return (attended.reshape(SEQ, D).astype(jnp.bfloat16), (row_max + jnp.log(row_total))[:, :, 0])


def attend_backward(pieces):
    queries, key_vectors, values, key_valid, log_total, attended_grad = pieces
    scores = masked_scores(queries, key_vectors, key_valid)
    probability = jnp.exp(scores - log_total[:, :, None])
    probability_low = probability.astype(jnp.bfloat16)
    grad_heads = head_view(attended_grad)
    value_grad = jnp.einsum(
        "hqk,qhd->khd", probability_low, grad_heads, preferred_element_type=jnp.float32
    )
    probability_grad = jnp.einsum(
        "qhd,khd->hqk", grad_heads, head_view(values), preferred_element_type=jnp.float32
    )
    inner_total = jnp.sum(probability * probability_grad, axis=-1, keepdims=True)
    score_grad = (probability * (probability_grad - inner_total)).astype(jnp.bfloat16)
    score_scale = 1.0 / math.sqrt(HDIM)
    query_grad = (
        jnp.einsum(
            "hqk,khd->qhd", score_grad, head_view(key_vectors), preferred_element_type=jnp.float32
        )
        * score_scale
    )
    key_grad = (
        jnp.einsum(
            "hqk,qhd->khd", score_grad, head_view(queries), preferred_element_type=jnp.float32
        )
        * score_scale
    )
    return (
        query_grad.reshape(SEQ, -1).astype(jnp.bfloat16),
        key_grad.reshape(SEQ, -1).astype(jnp.bfloat16),
        value_grad.reshape(SEQ, -1).astype(jnp.bfloat16),
    )


def adam_step(master, first_moment, second, gradient, step_rate, decay_rate, step_float):
    first_new = beta_first * first_moment + (1.0 - beta_first) * gradient
    second_new = beta_second * second + (1.0 - beta_second) * gradient * gradient
    first_hat = first_new / (1.0 - beta_first**step_float)
    second_hat = second_new / (1.0 - beta_second**step_float)
    master_new = master - step_rate * (
        first_hat / (jnp.sqrt(second_hat) + adam_epsilon) + decay_rate * master
    )
    return (master_new, first_new, second_new)


def padded_rows(rows, multiple):
    return -(-rows // multiple) * multiple


def gather_working(attention_master, feed_master, small_master):
    attention_rows = attention_master.shape[0]
    feed_rows = feed_master.shape[0]
    small_count = small_master.shape[0]
    main_rows = attention_rows + feed_rows
    extra_rows = padded_rows(main_rows + padded_rows(small_count, D) // D, 16) - main_rows
    small_flat = jnp.zeros((extra_rows * D,), jnp.bfloat16)
    small_flat = small_flat.at[:small_count].set(small_master.astype(jnp.bfloat16))
    block = jnp.concatenate(
        [
            attention_master.astype(jnp.bfloat16),
            feed_master.astype(jnp.bfloat16),
            small_flat.reshape(extra_rows, D),
        ],
        axis=0,
    )
    gathered = lax.all_gather(block, ("fsdp", "dp"), axis=0, tiled=False)
    owners = gathered.shape[0]
    attention_full = gathered[:, :attention_rows].reshape(owners * attention_rows, D)
    feed_full = gathered[:, attention_rows:main_rows].reshape(owners * feed_rows, D)
    small_full = gathered[:, main_rows:].reshape(owners, extra_rows * D)[:, :small_count]
    return attention_full, feed_full, small_full.reshape(owners * small_count)


def flat_coordinates():
    me = lax.axis_index(("fsdp", "dp"))
    return me, me % 2, (me // 2) % 2, (me // 4) % 2, me // 8


def shifted(distance, count=32):
    return [(d, d + distance) for d in range(count) if 0 <= d + distance < count]


def flipped(mask, count=32):
    return [(d, d ^ mask) for d in range(count)]


def permute(arrays, pairs):
    return lax.ppermute(tuple(arrays), ("fsdp", "dp"), pairs)


def staged_reduce_scatter(arrays):
    me, y_place, core, x_place, z_place = flat_coordinates()
    blocks = [entries.reshape((4, 2, 2, 2) + entries.shape[1:]) for entries in arrays]
    keep = [lax.dynamic_index_in_dim(b, core, axis=2, keepdims=False) for b in blocks]
    send = [lax.dynamic_index_in_dim(b, 1 - core, axis=2, keepdims=False).astype(jnp.bfloat16) for b in blocks]
    received = permute(send, flipped(2))
    plane = [k.astype(jnp.float32) + r.astype(jnp.float32) for k, r in zip(keep, received)]

    def pick(entries, x_index, y_index):
        picked = lax.dynamic_index_in_dim(entries, x_index, axis=1, keepdims=False)
        return lax.dynamic_index_in_dim(picked, y_index, axis=1, keepdims=False)

    along_z = [pick(p, x_place, y_place) for p in plane]
    for mask, x_index, y_index in ((4, 1 - x_place, y_place), (1, x_place, 1 - y_place), (5, 1 - x_place, 1 - y_place)):
        got = permute([pick(p, x_index, y_index).astype(jnp.bfloat16) for p in plane], flipped(mask))
        along_z = [a + g.astype(jnp.float32) for a, g in zip(along_z, got)]
    owned = [lax.dynamic_index_in_dim(a, z_place, axis=0, keepdims=False) for a in along_z]
    for distance in (1, 2, 3):
        up = permute(
            [lax.dynamic_index_in_dim(a, jnp.minimum(z_place + distance, 3), axis=0, keepdims=False).astype(jnp.bfloat16) for a in along_z],
            shifted(8 * distance),
        )
        down = permute(
            [lax.dynamic_index_in_dim(a, jnp.maximum(z_place - distance, 0), axis=0, keepdims=False).astype(jnp.bfloat16) for a in along_z],
            shifted(-8 * distance),
        )
        owned = [o + u.astype(jnp.float32) + w.astype(jnp.float32) for o, u, w in zip(owned, up, down)]
    return owned


def staged_all_gather(arrays):
    me, y_place, core, x_place, z_place = flat_coordinates()
    slot = [lax.broadcasted_iota(jnp.int32, (4,) + (1,) * a.ndim, 0) for a in arrays]
    grown = [jnp.where(s == z_place, a[None], jnp.zeros((4,) + a.shape, a.dtype)) for s, a in zip(slot, arrays)]
    for distance in (1, 2, 3):
        from_below = permute(arrays, shifted(8 * distance))
        from_above = permute(arrays, shifted(-8 * distance))
        grown = [jnp.where(s == z_place - distance, b[None], g) for s, b, g in zip(slot, from_below, grown)]
        grown = [jnp.where(s == z_place + distance, b[None], g) for s, b, g in zip(slot, from_above, grown)]
    got_x = permute(grown, flipped(4))
    got_y = permute(grown, flipped(1))
    got_xy = permute(grown, flipped(5))
    planes = []
    for own, gx, gy, gxy in zip(grown, got_x, got_y, got_xy):
        shape = (own.shape[0], 2, 2) + own.shape[1:]
        xs = lax.broadcasted_iota(jnp.int32, (1, 2, 1) + (1,) * (own.ndim - 1), 1)
        ys = lax.broadcasted_iota(jnp.int32, (1, 1, 2) + (1,) * (own.ndim - 1), 2)
        same_x, same_y = xs == x_place, ys == y_place
        plane = jnp.where(
            same_x,
            jnp.where(same_y, own[:, None, None], gy[:, None, None]),
            jnp.where(same_y, gx[:, None, None], gxy[:, None, None]),
        )
        planes.append(jnp.broadcast_to(plane, shape))
    got_core = permute(planes, flipped(2))
    gathered = []
    for own, other in zip(planes, got_core):
        own = own[:, :, None]
        other = other[:, :, None]
        size = own.shape[2]
        shape = own.shape[:2] + (2,) + own.shape[3:]
        start = [0] * len(shape)
        start_other = [0] * len(shape)
        start[2] = core * size
        start_other[2] = (1 - core) * size
        full = jnp.zeros(shape, own.dtype)
        full = lax.dynamic_update_slice(full, own, start)
        full = lax.dynamic_update_slice(full, other, start_other)
        gathered.append(full.reshape((32 * full.shape[4],) + full.shape[5:]))
    return gathered


def staged_working(attention_master, feed_master, small_master):
    small_count = small_master.shape[0]
    small_row = jnp.zeros((1, D), jnp.bfloat16).at[0, :small_count].set(small_master.astype(jnp.bfloat16))
    attention_full, small_rows = staged_all_gather([attention_master.astype(jnp.bfloat16), small_row])
    small_full = small_rows[:, :small_count].reshape(32 * small_count)
    feed_full = lax.all_gather(feed_master.astype(jnp.bfloat16), ("fsdp", "dp"), axis=0, tiled=True)
    return attention_full, feed_full, small_full


def scatter_gradients(attention_parts, feed_pieces, small_grad_all, partials, staged):
    owners = lax.psum(1, ("fsdp", "dp"))
    me = lax.axis_index(("fsdp", "dp"))
    attention_rows = sum(piece.shape[0] for piece in attention_parts[0]) // owners
    small_count = small_grad_all.shape[0] // owners
    if staged:
        feed_rows = feed_pieces.shape[0] // owners
        dp = lax.axis_index("dp")
        within = lax.psum_scatter(
            feed_pieces.reshape(owners // 2, 2 * feed_rows, D), "fsdp", scatter_dimension=0, tiled=True
        ).reshape(2, feed_rows, D)
        keep = lax.dynamic_index_in_dim(within, dp, axis=0, keepdims=False)
        send = lax.dynamic_index_in_dim(within, 1 - dp, axis=0, keepdims=False)
        feed_owned = keep.astype(jnp.float32) + lax.ppermute(send, "dp", [(0, 1), (1, 0)]).astype(jnp.float32)
    else:
        feed_owned = lax.psum_scatter(feed_pieces, ("fsdp", "dp"), scatter_dimension=0, tiled=True)
    partials_high = partials.astype(jnp.bfloat16)
    partials_low = (partials - partials_high.astype(jnp.float32)).astype(jnp.bfloat16)
    split_partials = jnp.concatenate([partials_high, partials_low])
    slots = split_partials.shape[0]
    extra_count = small_count + owners * slots
    extra_rows = padded_rows(attention_rows + padded_rows(extra_count, D) // D, 16) - attention_rows
    slot_row = jnp.zeros((owners * slots,), jnp.bfloat16)
    slot_row = lax.dynamic_update_slice(slot_row, split_partials, (me * slots,))
    extra = jnp.concatenate(
        [
            small_grad_all.astype(jnp.bfloat16).reshape(owners, small_count),
            jnp.broadcast_to(slot_row[None], (owners, owners * slots)),
            jnp.zeros((owners, extra_rows * D - extra_count), jnp.bfloat16),
        ],
        axis=1,
    ).reshape(owners, extra_rows, D)
    block_rows = attention_rows + extra_rows
    if staged:
        owned_parts = []
        for index, pieces in enumerate(attention_parts):
            part_all = jnp.concatenate(pieces, axis=0).astype(jnp.bfloat16)
            arrays = [part_all.reshape(owners, attention_rows, part_all.shape[1])]
            if index == len(attention_parts) - 1:
                arrays.append(extra)
            owned_parts.append(staged_reduce_scatter(arrays))
        owned = jnp.concatenate(
            [jnp.concatenate([part[0] for part in owned_parts], axis=1), owned_parts[-1][1]], axis=0
        )
    else:
        attention_pieces = [
            jnp.concatenate([pieces[index] for pieces in attention_parts], axis=1) for index in range(4)
        ]
        packed = jnp.zeros((owners, block_rows, D), jnp.bfloat16)
        packed = lax.dynamic_update_slice(packed, extra, (0, attention_rows, 0))
        owner = 0
        for piece in attention_pieces:
            piece_owners = piece.shape[0] // attention_rows
            packed = lax.dynamic_update_slice(
                packed, piece.astype(jnp.bfloat16).reshape(piece_owners, attention_rows, D), (owner, 0, 0)
            )
            owner = owner + piece_owners
        owned = lax.psum_scatter(
            packed.reshape(owners * block_rows, D), ("fsdp", "dp"), scatter_dimension=0, tiled=True
        ).astype(jnp.float32)
    attention_owned = owned[:attention_rows]
    extra_owned = owned[attention_rows:].reshape(extra_rows * D)
    small_owned = extra_owned[:small_count]
    gathered_partials = extra_owned[small_count:extra_count].reshape(owners, slots)
    half = slots // 2
    totals = gathered_partials[0, :half] + gathered_partials[0, half:]
    for index in range(1, owners):
        totals = totals + (gathered_partials[index, :half] + gathered_partials[index, half:])
    return attention_owned, feed_owned.astype(jnp.float32), small_owned, totals


def on_device(
    staged,
    tokens,
    cotangent,
    lengths,
    step_count,
    attention_master,
    attention_first,
    attention_second,
    feed_master,
    feed_first,
    feed_second,
    small_master,
    small_first,
    small_second,
):
    row_count = tokens.shape[0]
    sequence_count = row_count // SEQ
    if staged:
        attention_full, feed_full, small_full = staged_working(attention_master, feed_master, small_master)
    else:
        attention_full, feed_full, small_full = gather_working(attention_master, feed_master, small_master)
    key_valid = (
        lax.broadcasted_iota(jnp.int32, (sequence_count, SEQ), 1) < lengths[:, None]
    ).astype(jnp.float32)
    token_valid = key_valid.reshape(row_count)
    (
        query_bias,
        value_bias,
        output_bias,
        inner_bias,
        outer_bias,
        first_gain,
        first_shift,
        second_gain,
        second_shift,
    ) = split_small(small_full)
    queries = (product(tokens, attention_full[0:D]) + query_bias).astype(jnp.bfloat16)
    key_vectors = product(tokens, attention_full[D : 2 * D]).astype(jnp.bfloat16)
    values = (product(tokens, attention_full[2 * D : 3 * D]) + value_bias).astype(jnp.bfloat16)
    seq_shape = (sequence_count, SEQ, D)
    attended, log_total = lax.map(
        attend_forward,
        (
            queries.reshape(seq_shape),
            key_vectors.reshape(seq_shape),
            values.reshape(seq_shape),
            key_valid,
        ),
    )
    attended = attended.reshape(row_count, D)
    branch_attention = product(attended, attention_full[3 * D : 4 * D]) + output_bias
    first_sum = tokens.astype(jnp.float32) + branch_attention
    normed = layer_norm(first_sum, first_gain, first_shift)
    normed_low = normed.astype(jnp.bfloat16)
    inner_sum = product_cols(normed_low, feed_full[0:FF]) + inner_bias
    active = gelu_exact(inner_sum).astype(jnp.bfloat16)
    gelu_slope = gelu_derivative(inner_sum)
    branch_feed = product(active, feed_full[FF : 2 * FF]) + outer_bias
    residual = normed + branch_feed
    layer_out = layer_norm(residual, second_gain, second_shift).astype(jnp.bfloat16)
    column = token_valid[:, None]
    partials = jnp.stack(
        [
            jnp.sum(residual * residual * column),
            jnp.sum(branch_attention * branch_attention * column),
            jnp.sum(branch_feed * branch_feed * column),
            jnp.sum(token_valid),
        ]
    )
    query_weight = attention_full[0:D]
    key_weight = attention_full[D : 2 * D]
    value_weight = attention_full[2 * D : 3 * D]
    output_weight = attention_full[3 * D : 4 * D]
    outer_weight = feed_full[FF : 2 * FF]
    inner_weight = feed_full[0:FF]
    second_pull = jax.vjp(layer_norm, residual, second_gain, second_shift)[1]
    residual_grad, second_gain_grad, second_shift_grad = second_pull(cotangent)
    feed_out_grad = residual_grad.astype(jnp.bfloat16)
    outer_bias_grad = column_total(feed_out_grad)
    active_grad = product_cols(feed_out_grad, outer_weight)
    inner_grad = (active_grad * gelu_slope).astype(jnp.bfloat16)
    inner_bias_grad = column_total(inner_grad)
    feed_grad_all = (
        lax.dot_general(
            jnp.stack([inner_grad, active]),
            jnp.stack([normed_low, feed_out_grad]),
            (((1,), (1,)), ((0,), (0,))),
            preferred_element_type=jnp.float32,
        )
        .astype(jnp.bfloat16)
        .reshape(2 * FF, D)
    )
    feed_grad_all, inner_grad_late = lax.optimization_barrier((feed_grad_all, inner_grad))
    normed_grad = residual_grad + product(inner_grad_late, inner_weight)
    first_pull = jax.vjp(layer_norm, first_sum, first_gain, first_shift)[1]
    first_sum_grad, first_gain_grad, first_shift_grad = first_pull(normed_grad)
    branch_grad_low = first_sum_grad.astype(jnp.bfloat16)
    output_bias_grad = column_total(branch_grad_low)
    attended_grad = product_cols(branch_grad_low, output_weight).astype(jnp.bfloat16)
    parts = 2
    width = D // parts
    head_count = HEADS // parts
    part_grads = []
    attention_parts = []
    for part in range(parts):
        columns = slice(part * width, (part + 1) * width)
        part_shape = (sequence_count, SEQ, width)
        query_part, key_part, value_part = lax.map(
            attend_backward,
            (
                queries[:, columns].reshape(part_shape),
                key_vectors[:, columns].reshape(part_shape),
                values[:, columns].reshape(part_shape),
                key_valid,
                log_total[:, part * head_count : (part + 1) * head_count],
                attended_grad[:, columns].reshape(part_shape),
            ),
        )
        query_part = query_part.reshape(row_count, width)
        key_part = key_part.reshape(row_count, width)
        value_part = value_part.reshape(row_count, width)
        part_grads.append((query_part, key_part, value_part))
        attention_parts.append(
            [
                product_rows(tokens, query_part),
                product_rows(tokens, key_part),
                product_rows(tokens, value_part),
                product_rows(attended, branch_grad_low[:, columns]),
            ]
        )
    query_grad = jnp.concatenate([grads[0] for grads in part_grads], axis=1)
    key_grad = jnp.concatenate([grads[1] for grads in part_grads], axis=1)
    value_grad = jnp.concatenate([grads[2] for grads in part_grads], axis=1)
    query_bias_grad = column_total(query_grad)
    value_bias_grad = column_total(value_grad)
    tokens_grad = (
        first_sum_grad
        + product_cols(query_grad, query_weight)
        + product_cols(key_grad, key_weight)
        + product_cols(value_grad, value_weight)
    )
    small_grad_all = jnp.concatenate(
        [
            query_bias_grad,
            value_bias_grad,
            output_bias_grad,
            inner_bias_grad,
            outer_bias_grad,
            first_gain_grad,
            first_shift_grad,
            second_gain_grad,
            second_shift_grad,
        ]
    )
    attention_owned, feed_owned, small_owned, totals = scatter_gradients(
        attention_parts,
        feed_grad_all,
        small_grad_all,
        partials,
        staged,
    )
    rms_values = jnp.sqrt(totals[:3] / (totals[3] * D))
    step_float = step_count[0].astype(jnp.float32)
    attention_new, attention_first_new, attention_second_new = adam_step(
        attention_master,
        attention_first,
        attention_second,
        attention_owned,
        rate_matrix,
        weight_decay,
        step_float,
    )
    feed_new, feed_first_new, feed_second_new = adam_step(
        feed_master, feed_first, feed_second, feed_owned, rate_matrix, weight_decay, step_float
    )
    small_new, small_first_new, small_second_new = adam_step(
        small_master, small_first, small_second, small_owned, rate_small, 0.0, step_float
    )
    return (
        layer_out,
        tokens_grad,
        attention_new,
        attention_first_new,
        attention_second_new,
        attention_new.astype(jnp.bfloat16),
        feed_new,
        feed_first_new,
        feed_second_new,
        feed_new.astype(jnp.bfloat16),
        small_new,
        small_first_new,
        small_second_new,
        small_new.astype(jnp.bfloat16),
        rms_values,
    )


def solution(mesh):
    placed = (
        P(("fsdp", "dp"), None),
        P(("fsdp", "dp"), None),
        P(("fsdp", "dp")),
        P(),
        P(("fsdp", "dp"), None),
        P(("fsdp", "dp"), None),
        P(("fsdp", "dp"), None),
        P(("fsdp", "dp"), None),
        P(("fsdp", "dp"), None),
        P(("fsdp", "dp"), None),
        P(("fsdp", "dp")),
        P(("fsdp", "dp")),
        P(("fsdp", "dp")),
    )
    staged = dict(mesh.shape) == {"fsdp": 16, "dp": 2}
    return jax.shard_map(
        functools.partial(on_device, staged),
        mesh=mesh,
        in_specs=placed,
        out_specs=(
            P(("fsdp", "dp"), None),
            P(("fsdp", "dp"), None),
            P(("fsdp", "dp"), None),
            P(("fsdp", "dp"), None),
            P(("fsdp", "dp"), None),
            P(("fsdp", "dp"), None),
            P(("fsdp", "dp"), None),
            P(("fsdp", "dp"), None),
            P(("fsdp", "dp"), None),
            P(("fsdp", "dp"), None),
            P(("fsdp", "dp")),
            P(("fsdp", "dp")),
            P(("fsdp", "dp")),
            P(("fsdp", "dp")),
            P(),
        ),
        check_vma=False,
    )
```

```python
import functools
import math

import jax
import numpy as np
import jax.numpy as jnp
from jax import lax
from jax.sharding import PartitionSpec as P

D = 768
HEADS = 12
HDIM = 64
FF = 3072
SEQ = 512


ln_epsilon = 1e-12
beta_first = 0.5
beta_second = 0.55
adam_epsilon = 1e-06
rate_matrix = 0.04
rate_small = 0.25
weight_decay = 0.01


def product(left_side, right_side):
    return jnp.dot(left_side, right_side, preferred_element_type=jnp.float32)


def product_rows(left_side, right_side):
    return lax.dot_general(
        left_side, right_side, (((0,), (0,)), ((), ())), preferred_element_type=jnp.float32
    )


def product_cols(left_side, right_side):
    return lax.dot_general(
        left_side, right_side, (((1,), (1,)), ((), ())), preferred_element_type=jnp.float32
    )


def column_total(entries):
    return jnp.sum(entries, axis=0, dtype=jnp.float32)


def layer_norm(entries, norm_gain, norm_shift):
    center = jnp.mean(entries, axis=-1, keepdims=True)
    offset = entries - center
    spread = jnp.mean(offset * offset, axis=-1, keepdims=True)
    return offset * lax.rsqrt(spread + ln_epsilon) * norm_gain + norm_shift


def gelu_exact(entries):
    return jax.nn.gelu(entries, approximate=False)


def gelu_derivative(entries):
    sqrt_half = np.sqrt(0.5).astype(np.float32)
    shifted_entries = -entries * sqrt_half
    return 0.5 * lax.erfc(shifted_entries) + entries * (
        jnp.exp(-(shifted_entries * shifted_entries)) * np.float32(sqrt_half / np.sqrt(np.pi))
    )


def split_small(small_full):
    pieces = []
    position = 0
    for length in (D, D, D, FF, D, D, D, D, D):
        pieces.append(small_full[position : position + length].astype(jnp.float32))
        position = position + length
    return pieces


def head_view(entries):
    return entries.reshape(SEQ, HEADS, HDIM)


def masked_scores(queries, key_vectors, key_valid):
    scores = jnp.einsum(
        "qhd,khd->hqk",
        head_view(queries),
        head_view(key_vectors),
        preferred_element_type=jnp.float32,
    ) * (1.0 / math.sqrt(HDIM))
    return jnp.where(key_valid[None, None, :] > 0, scores, -1e30)


def attend_forward(pieces):
    queries, key_vectors, values, key_valid = pieces
    scores = masked_scores(queries, key_vectors, key_valid)
    row_max = jnp.max(scores, axis=-1, keepdims=True)
    exponent = jnp.exp(scores - row_max)
    row_total = jnp.sum(exponent, axis=-1, keepdims=True)
    probability = (exponent / row_total).astype(jnp.bfloat16)
    attended = jnp.einsum(
        "hqk,khd->qhd", probability, head_view(values), preferred_element_type=jnp.float32
    )
    return (attended.reshape(SEQ, D).astype(jnp.bfloat16), (row_max + jnp.log(row_total))[:, :, 0])


def attend_backward(pieces):
    queries, key_vectors, values, key_valid, log_total, attended_grad = pieces
    scores = masked_scores(queries, key_vectors, key_valid)
    probability = jnp.exp(scores - log_total[:, :, None])
    probability_low = probability.astype(jnp.bfloat16)
    grad_heads = head_view(attended_grad)
    value_grad = jnp.einsum(
        "hqk,qhd->khd", probability_low, grad_heads, preferred_element_type=jnp.float32
    )
    probability_grad = jnp.einsum(
        "qhd,khd->hqk", grad_heads, head_view(values), preferred_element_type=jnp.float32
    )
    inner_total = jnp.sum(probability * probability_grad, axis=-1, keepdims=True)
    score_grad = (probability * (probability_grad - inner_total)).astype(jnp.bfloat16)
    score_scale = 1.0 / math.sqrt(HDIM)
    query_grad = (
        jnp.einsum(
            "hqk,khd->qhd", score_grad, head_view(key_vectors), preferred_element_type=jnp.float32
        )
        * score_scale
    )
    key_grad = (
        jnp.einsum(
            "hqk,qhd->khd", score_grad, head_view(queries), preferred_element_type=jnp.float32
        )
        * score_scale
    )
    return (
        query_grad.reshape(SEQ, D).astype(jnp.bfloat16),
        key_grad.reshape(SEQ, D).astype(jnp.bfloat16),
        value_grad.reshape(SEQ, D).astype(jnp.bfloat16),
    )


def adam_step(master, first_moment, second, gradient, step_rate, decay_rate, step_float):
    first_new = beta_first * first_moment + (1.0 - beta_first) * gradient
    second_new = beta_second * second + (1.0 - beta_second) * gradient * gradient
    first_hat = first_new / (1.0 - beta_first**step_float)
    second_hat = second_new / (1.0 - beta_second**step_float)
    master_new = master - step_rate * (
        first_hat / (jnp.sqrt(second_hat) + adam_epsilon) + decay_rate * master
    )
    return (master_new, first_new, second_new)


def padded_rows(rows, multiple):
    return -(-rows // multiple) * multiple


def gather_working(attention_master, feed_master, small_master):
    attention_rows = attention_master.shape[0]
    feed_rows = feed_master.shape[0]
    small_count = small_master.shape[0]
    main_rows = attention_rows + feed_rows
    extra_rows = padded_rows(main_rows + padded_rows(small_count, D) // D, 16) - main_rows
    small_flat = jnp.zeros((extra_rows * D,), jnp.bfloat16)
    small_flat = small_flat.at[:small_count].set(small_master.astype(jnp.bfloat16))
    block = jnp.concatenate(
        [
            attention_master.astype(jnp.bfloat16),
            feed_master.astype(jnp.bfloat16),
            small_flat.reshape(extra_rows, D),
        ],
        axis=0,
    )
    gathered = lax.all_gather(block, ("fsdp", "dp"), axis=0, tiled=False)
    owners = gathered.shape[0]
    attention_full = gathered[:, :attention_rows].reshape(owners * attention_rows, D)
    feed_full = gathered[:, attention_rows:main_rows].reshape(owners * feed_rows, D)
    small_full = gathered[:, main_rows:].reshape(owners, extra_rows * D)[:, :small_count]
    return attention_full, feed_full, small_full.reshape(owners * small_count)


def flat_coordinates():
    me = lax.axis_index(("fsdp", "dp"))
    return me, me % 2, (me // 2) % 2, (me // 4) % 2, me // 8


def shifted(distance, count=32):
    return [(d, d + distance) for d in range(count) if 0 <= d + distance < count]


def flipped(mask, count=32):
    return [(d, d ^ mask) for d in range(count)]


def permute(arrays, pairs):
    return lax.ppermute(tuple(arrays), ("fsdp", "dp"), pairs)


def staged_reduce_scatter(arrays, late=()):
    me, y_place, core, x_place, z_place = flat_coordinates()
    blocks = [jnp.moveaxis(entries.reshape((4, 2, 2, 2) + entries.shape[1:]), 2, 0) for entries in arrays]
    keep = [lax.dynamic_index_in_dim(b, core, axis=0, keepdims=False) for b in blocks]
    send = [lax.dynamic_index_in_dim(b, 1 - core, axis=0, keepdims=False).astype(jnp.bfloat16) for b in blocks]
    received = permute(send, flipped(2))
    plane = [k.astype(jnp.float32) + r.astype(jnp.float32) for k, r in zip(keep, received)]
    plane, late = lax.optimization_barrier((plane, late))

    def pick(entries, x_index, y_index):
        picked = lax.dynamic_index_in_dim(entries, x_index, axis=1, keepdims=False)
        return lax.dynamic_index_in_dim(picked, y_index, axis=1, keepdims=False)

    along_z = [pick(p, x_place, y_place) for p in plane]
    for mask, x_index, y_index in ((4, 1 - x_place, y_place), (1, x_place, 1 - y_place), (5, 1 - x_place, 1 - y_place)):
        got = permute([pick(p, x_index, y_index).astype(jnp.bfloat16) for p in plane], flipped(mask))
        along_z = [a + g.astype(jnp.float32) for a, g in zip(along_z, got)]
    owned = [lax.dynamic_index_in_dim(a, z_place, axis=0, keepdims=False) for a in along_z]
    for distance in (1, 2, 3):
        up = permute(
            [lax.dynamic_index_in_dim(a, jnp.minimum(z_place + distance, 3), axis=0, keepdims=False).astype(jnp.bfloat16) for a in along_z],
            shifted(8 * distance),
        )
        down = permute(
            [lax.dynamic_index_in_dim(a, jnp.maximum(z_place - distance, 0), axis=0, keepdims=False).astype(jnp.bfloat16) for a in along_z],
            shifted(-8 * distance),
        )
        owned = [o + u.astype(jnp.float32) + w.astype(jnp.float32) for o, u, w in zip(owned, up, down)]
    return owned, late


def staged_all_gather(arrays):
    me, y_place, core, x_place, z_place = flat_coordinates()
    slot = [lax.broadcasted_iota(jnp.int32, (4,) + (1,) * a.ndim, 0) for a in arrays]
    grown = [jnp.where(s == z_place, a[None], jnp.zeros((4,) + a.shape, a.dtype)) for s, a in zip(slot, arrays)]
    for distance in (1, 2, 3):
        from_below = permute(arrays, shifted(8 * distance))
        from_above = permute(arrays, shifted(-8 * distance))
        grown = [jnp.where(s == z_place - distance, b[None], g) for s, b, g in zip(slot, from_below, grown)]
        grown = [jnp.where(s == z_place + distance, b[None], g) for s, b, g in zip(slot, from_above, grown)]
    got_x = permute(grown, flipped(4))
    got_y = permute(grown, flipped(1))
    got_xy = permute(grown, flipped(5))
    planes = []
    for own, gx, gy, gxy in zip(grown, got_x, got_y, got_xy):
        shape = (own.shape[0], 2, 2) + own.shape[1:]
        xs = lax.broadcasted_iota(jnp.int32, (1, 2, 1) + (1,) * (own.ndim - 1), 1)
        ys = lax.broadcasted_iota(jnp.int32, (1, 1, 2) + (1,) * (own.ndim - 1), 2)
        same_x, same_y = xs == x_place, ys == y_place
        plane = jnp.where(
            same_x,
            jnp.where(same_y, own[:, None, None], gy[:, None, None]),
            jnp.where(same_y, gx[:, None, None], gxy[:, None, None]),
        )
        planes.append(jnp.broadcast_to(plane, shape))
    got_core = permute(planes, flipped(2))
    gathered = []
    for own, other in zip(planes, got_core):
        own = own[:, :, None]
        other = other[:, :, None]
        size = own.shape[2]
        shape = own.shape[:2] + (2,) + own.shape[3:]
        start = [0] * len(shape)
        start_other = [0] * len(shape)
        start[2] = core * size
        start_other[2] = (1 - core) * size
        full = jnp.zeros(shape, own.dtype)
        full = lax.dynamic_update_slice(full, own, start)
        full = lax.dynamic_update_slice(full, other, start_other)
        gathered.append(full.reshape((32 * full.shape[4],) + full.shape[5:]))
    return gathered


def staged_working(attention_master, feed_master, small_master):
    small_count = small_master.shape[0]
    small_row = jnp.zeros((1, D), jnp.bfloat16).at[0, :small_count].set(small_master.astype(jnp.bfloat16))
    attention_full, small_rows = staged_all_gather([attention_master.astype(jnp.bfloat16), small_row])
    small_full = small_rows[:, :small_count].reshape(32 * small_count)
    feed_full = lax.all_gather(feed_master.astype(jnp.bfloat16), ("fsdp", "dp"), axis=0, tiled=True)
    return attention_full, feed_full, small_full


def scatter_gradients(attention_pieces, feed_pieces, small_grad_all, partials, staged, late):
    owners = lax.psum(1, ("fsdp", "dp"))
    me = lax.axis_index(("fsdp", "dp"))
    attention_rows = sum(piece.shape[0] for piece in attention_pieces) // owners
    small_count = small_grad_all.shape[0] // owners
    if staged:
        feed_rows = feed_pieces.shape[0] // owners
        dp = lax.axis_index("dp")
        within = lax.psum_scatter(
            feed_pieces.reshape(owners // 2, 2 * feed_rows, D), "fsdp", scatter_dimension=0, tiled=True
        ).reshape(2, feed_rows, D)
        keep = lax.dynamic_index_in_dim(within, dp, axis=0, keepdims=False)
        send = lax.dynamic_index_in_dim(within, 1 - dp, axis=0, keepdims=False)
        feed_owned = keep.astype(jnp.float32) + lax.ppermute(send, "dp", [(0, 1), (1, 0)]).astype(jnp.float32)
    else:
        feed_owned = lax.psum_scatter(feed_pieces, ("fsdp", "dp"), scatter_dimension=0, tiled=True)
    partials_high = partials.astype(jnp.bfloat16)
    partials_low = (partials - partials_high.astype(jnp.float32)).astype(jnp.bfloat16)
    split_partials = jnp.concatenate([partials_high, partials_low])
    slots = split_partials.shape[0]
    extra_count = small_count + owners * slots
    extra_rows = padded_rows(attention_rows + padded_rows(extra_count, D) // D, 16) - attention_rows
    slot_row = jnp.zeros((owners * slots,), jnp.bfloat16)
    slot_row = lax.dynamic_update_slice(slot_row, split_partials, (me * slots,))
    extra = jnp.concatenate(
        [
            small_grad_all.astype(jnp.bfloat16).reshape(owners, small_count),
            jnp.broadcast_to(slot_row[None], (owners, owners * slots)),
            jnp.zeros((owners, extra_rows * D - extra_count), jnp.bfloat16),
        ],
        axis=1,
    ).reshape(owners, extra_rows, D)
    block_rows = attention_rows + extra_rows
    if staged:
        attention_grad_all = jnp.concatenate(attention_pieces, axis=0).astype(jnp.bfloat16)
        owned_parts, late = staged_reduce_scatter(
            [attention_grad_all.reshape(owners, attention_rows, D), extra], late
        )
        owned = jnp.concatenate(owned_parts, axis=0)
    else:
        packed = jnp.zeros((owners, block_rows, D), jnp.bfloat16)
        packed = lax.dynamic_update_slice(packed, extra, (0, attention_rows, 0))
        owner = 0
        for piece in attention_pieces:
            piece_owners = piece.shape[0] // attention_rows
            packed = lax.dynamic_update_slice(
                packed, piece.astype(jnp.bfloat16).reshape(piece_owners, attention_rows, D), (owner, 0, 0)
            )
            owner = owner + piece_owners
        owned = lax.psum_scatter(
            packed.reshape(owners * block_rows, D), ("fsdp", "dp"), scatter_dimension=0, tiled=True
        ).astype(jnp.float32)
    attention_owned = owned[:attention_rows]
    extra_owned = owned[attention_rows:].reshape(extra_rows * D)
    small_owned = extra_owned[:small_count]
    gathered_partials = extra_owned[small_count:extra_count].reshape(owners, slots)
    half = slots // 2
    totals = gathered_partials[0, :half] + gathered_partials[0, half:]
    for index in range(1, owners):
        totals = totals + (gathered_partials[index, :half] + gathered_partials[index, half:])
    return attention_owned, feed_owned.astype(jnp.float32), small_owned, totals, late


def on_device(
    staged,
    tokens,
    cotangent,
    lengths,
    step_count,
    attention_master,
    attention_first,
    attention_second,
    feed_master,
    feed_first,
    feed_second,
    small_master,
    small_first,
    small_second,
):
    row_count = tokens.shape[0]
    sequence_count = row_count // SEQ
    if staged:
        attention_full, feed_full, small_full = staged_working(attention_master, feed_master, small_master)
    else:
        attention_full, feed_full, small_full = gather_working(attention_master, feed_master, small_master)
    key_valid = (
        lax.broadcasted_iota(jnp.int32, (sequence_count, SEQ), 1) < lengths[:, None]
    ).astype(jnp.float32)
    token_valid = key_valid.reshape(row_count)
    (
        query_bias,
        value_bias,
        output_bias,
        inner_bias,
        outer_bias,
        first_gain,
        first_shift,
        second_gain,
        second_shift,
    ) = split_small(small_full)
    queries = (product(tokens, attention_full[0:D]) + query_bias).astype(jnp.bfloat16)
    key_vectors = product(tokens, attention_full[D : 2 * D]).astype(jnp.bfloat16)
    values = (product(tokens, attention_full[2 * D : 3 * D]) + value_bias).astype(jnp.bfloat16)
    seq_shape = (sequence_count, SEQ, D)
    attended, log_total = lax.map(
        attend_forward,
        (
            queries.reshape(seq_shape),
            key_vectors.reshape(seq_shape),
            values.reshape(seq_shape),
            key_valid,
        ),
    )
    attended = attended.reshape(row_count, D)
    branch_attention = product(attended, attention_full[3 * D : 4 * D]) + output_bias
    first_sum = tokens.astype(jnp.float32) + branch_attention
    normed = layer_norm(first_sum, first_gain, first_shift)
    normed_low = normed.astype(jnp.bfloat16)
    inner_sum = product_cols(normed_low, feed_full[0:FF]) + inner_bias
    active = gelu_exact(inner_sum).astype(jnp.bfloat16)
    gelu_slope = gelu_derivative(inner_sum)
    branch_feed = product(active, feed_full[FF : 2 * FF]) + outer_bias
    residual = normed + branch_feed
    column = token_valid[:, None]
    partials = jnp.stack(
        [
            jnp.sum(residual * residual * column),
            jnp.sum(branch_attention * branch_attention * column),
            jnp.sum(branch_feed * branch_feed * column),
            jnp.sum(token_valid),
        ]
    )
    query_weight = attention_full[0:D]
    key_weight = attention_full[D : 2 * D]
    value_weight = attention_full[2 * D : 3 * D]
    output_weight = attention_full[3 * D : 4 * D]
    outer_weight = feed_full[FF : 2 * FF]
    inner_weight = feed_full[0:FF]
    second_pull = jax.vjp(layer_norm, residual, second_gain, second_shift)[1]
    residual_grad, second_gain_grad, second_shift_grad = second_pull(cotangent)
    feed_out_grad = residual_grad.astype(jnp.bfloat16)
    outer_bias_grad = column_total(feed_out_grad)
    active_grad = product_cols(feed_out_grad, outer_weight)
    inner_grad = (active_grad * gelu_slope).astype(jnp.bfloat16)
    inner_bias_grad = column_total(inner_grad)
    feed_grad_all = (
        lax.dot_general(
            jnp.stack([inner_grad, active]),
            jnp.stack([normed_low, feed_out_grad]),
            (((1,), (1,)), ((0,), (0,))),
            preferred_element_type=jnp.float32,
        )
        .astype(jnp.bfloat16)
        .reshape(2 * FF, D)
    )
    feed_grad_all, inner_grad_late, partials = lax.optimization_barrier((feed_grad_all, inner_grad, partials))
    normed_grad = residual_grad + product(inner_grad_late, inner_weight)
    first_pull = jax.vjp(layer_norm, first_sum, first_gain, first_shift)[1]
    first_sum_grad, first_gain_grad, first_shift_grad = first_pull(normed_grad)
    branch_grad_low = first_sum_grad.astype(jnp.bfloat16)
    output_bias_grad = column_total(branch_grad_low)
    output_weight_grad = product_rows(attended, branch_grad_low)
    attended_grad = product_cols(branch_grad_low, output_weight).astype(jnp.bfloat16)
    query_grad, key_grad, value_grad = lax.map(
        attend_backward,
        (
            queries.reshape(seq_shape),
            key_vectors.reshape(seq_shape),
            values.reshape(seq_shape),
            key_valid,
            log_total,
            attended_grad.reshape(seq_shape),
        ),
    )
    query_grad = query_grad.reshape(row_count, D)
    key_grad = key_grad.reshape(row_count, D)
    value_grad = value_grad.reshape(row_count, D)
    query_weight_grad = product_rows(tokens, query_grad)
    key_weight_grad = product_rows(tokens, key_grad)
    value_weight_grad = product_rows(tokens, value_grad)
    query_bias_grad = column_total(query_grad)
    value_bias_grad = column_total(value_grad)
    small_grad_all = jnp.concatenate(
        [
            query_bias_grad,
            value_bias_grad,
            output_bias_grad,
            inner_bias_grad,
            outer_bias_grad,
            first_gain_grad,
            first_shift_grad,
            second_gain_grad,
            second_shift_grad,
        ]
    )
    attention_owned, feed_owned, small_owned, totals, late = scatter_gradients(
        [query_weight_grad, key_weight_grad, value_weight_grad, output_weight_grad],
        feed_grad_all,
        small_grad_all,
        partials,
        staged,
        (first_sum_grad, query_grad, key_grad, value_grad, residual),
    )
    first_sum_grad, query_grad, key_grad, value_grad, residual = late
    tokens_grad = (
        first_sum_grad
        + product_cols(query_grad, query_weight)
        + product_cols(key_grad, key_weight)
        + product_cols(value_grad, value_weight)
    )
    layer_out = layer_norm(residual, second_gain, second_shift).astype(jnp.bfloat16)
    rms_values = jnp.sqrt(totals[:3] / (totals[3] * D))
    step_float = step_count[0].astype(jnp.float32)
    attention_new, attention_first_new, attention_second_new = adam_step(
        attention_master,
        attention_first,
        attention_second,
        attention_owned,
        rate_matrix,
        weight_decay,
        step_float,
    )
    feed_new, feed_first_new, feed_second_new = adam_step(
        feed_master, feed_first, feed_second, feed_owned, rate_matrix, weight_decay, step_float
    )
    small_new, small_first_new, small_second_new = adam_step(
        small_master, small_first, small_second, small_owned, rate_small, 0.0, step_float
    )
    return (
        layer_out,
        tokens_grad,
        attention_new,
        attention_first_new,
        attention_second_new,
        attention_new.astype(jnp.bfloat16),
        feed_new,
        feed_first_new,
        feed_second_new,
        feed_new.astype(jnp.bfloat16),
        small_new,
        small_first_new,
        small_second_new,
        small_new.astype(jnp.bfloat16),
        rms_values,
    )


def solution(mesh):
    placed = (
        P(("fsdp", "dp"), None),
        P(("fsdp", "dp"), None),
        P(("fsdp", "dp")),
        P(),
        P(("fsdp", "dp"), None),
        P(("fsdp", "dp"), None),
        P(("fsdp", "dp"), None),
        P(("fsdp", "dp"), None),
        P(("fsdp", "dp"), None),
        P(("fsdp", "dp"), None),
        P(("fsdp", "dp")),
        P(("fsdp", "dp")),
        P(("fsdp", "dp")),
    )
    staged = dict(mesh.shape) == {"fsdp": 16, "dp": 2}
    return jax.shard_map(
        functools.partial(on_device, staged),
        mesh=mesh,
        in_specs=placed,
        out_specs=(
            P(("fsdp", "dp"), None),
            P(("fsdp", "dp"), None),
            P(("fsdp", "dp"), None),
            P(("fsdp", "dp"), None),
            P(("fsdp", "dp"), None),
            P(("fsdp", "dp"), None),
            P(("fsdp", "dp"), None),
            P(("fsdp", "dp"), None),
            P(("fsdp", "dp"), None),
            P(("fsdp", "dp"), None),
            P(("fsdp", "dp")),
            P(("fsdp", "dp")),
            P(("fsdp", "dp")),
            P(("fsdp", "dp")),
            P(),
        ),
        check_vma=False,
    )
```

```python
import functools
import math

import jax
import numpy as np
import jax.numpy as jnp
from jax import lax
from jax.sharding import PartitionSpec as P

D = 768
HEADS = 12
HDIM = 64
FF = 3072
SEQ = 512


ln_epsilon = 1e-12
beta_first = 0.5
beta_second = 0.55
adam_epsilon = 1e-06
rate_matrix = 0.04
rate_small = 0.25
weight_decay = 0.01


def product(left_side, right_side):
    return jnp.dot(left_side, right_side, preferred_element_type=jnp.float32)


def product_rows(left_side, right_side):
    return lax.dot_general(
        left_side, right_side, (((0,), (0,)), ((), ())), preferred_element_type=jnp.float32
    )


def product_cols(left_side, right_side):
    return lax.dot_general(
        left_side, right_side, (((1,), (1,)), ((), ())), preferred_element_type=jnp.float32
    )


def column_total(entries):
    return jnp.sum(entries, axis=0, dtype=jnp.float32)


def layer_norm(entries, norm_gain, norm_shift):
    center = jnp.mean(entries, axis=-1, keepdims=True)
    offset = entries - center
    spread = jnp.mean(offset * offset, axis=-1, keepdims=True)
    return offset * lax.rsqrt(spread + ln_epsilon) * norm_gain + norm_shift


def gelu_exact(entries):
    return jax.nn.gelu(entries, approximate=False)


def gelu_derivative(entries):
    sqrt_half = np.sqrt(0.5).astype(np.float32)
    shifted_entries = -entries * sqrt_half
    return 0.5 * lax.erfc(shifted_entries) + entries * (
        jnp.exp(-(shifted_entries * shifted_entries)) * np.float32(sqrt_half / np.sqrt(np.pi))
    )


def split_small(small_full):
    pieces = []
    position = 0
    for length in (D, D, D, FF, D, D, D, D, D):
        pieces.append(small_full[position : position + length].astype(jnp.float32))
        position = position + length
    return pieces


def head_view(entries):
    return entries.reshape(SEQ, HEADS, HDIM)


def masked_scores(queries, key_vectors, key_valid):
    scores = jnp.einsum(
        "qhd,khd->hqk",
        head_view(queries),
        head_view(key_vectors),
        preferred_element_type=jnp.float32,
    ) * (1.0 / math.sqrt(HDIM))
    return jnp.where(key_valid[None, None, :] > 0, scores, -1e30)


def attend_forward(pieces):
    queries, key_vectors, values, key_valid = pieces
    scores = masked_scores(queries, key_vectors, key_valid)
    row_max = jnp.max(scores, axis=-1, keepdims=True)
    exponent = jnp.exp(scores - row_max)
    row_total = jnp.sum(exponent, axis=-1, keepdims=True)
    probability = (exponent / row_total).astype(jnp.bfloat16)
    attended = jnp.einsum(
        "hqk,khd->qhd", probability, head_view(values), preferred_element_type=jnp.float32
    )
    return (attended.reshape(SEQ, D).astype(jnp.bfloat16), (row_max + jnp.log(row_total))[:, :, 0])


def attend_backward(pieces):
    queries, key_vectors, values, key_valid, log_total, attended_grad = pieces
    scores = masked_scores(queries, key_vectors, key_valid)
    probability = jnp.exp(scores - log_total[:, :, None])
    probability_low = probability.astype(jnp.bfloat16)
    grad_heads = head_view(attended_grad)
    value_grad = jnp.einsum(
        "hqk,qhd->khd", probability_low, grad_heads, preferred_element_type=jnp.float32
    )
    probability_grad = jnp.einsum(
        "qhd,khd->hqk", grad_heads, head_view(values), preferred_element_type=jnp.float32
    )
    inner_total = jnp.sum(probability * probability_grad, axis=-1, keepdims=True)
    score_grad = (probability * (probability_grad - inner_total)).astype(jnp.bfloat16)
    score_scale = 1.0 / math.sqrt(HDIM)
    query_grad = (
        jnp.einsum(
            "hqk,khd->qhd", score_grad, head_view(key_vectors), preferred_element_type=jnp.float32
        )
        * score_scale
    )
    key_grad = (
        jnp.einsum(
            "hqk,qhd->khd", score_grad, head_view(queries), preferred_element_type=jnp.float32
        )
        * score_scale
    )
    return (
        query_grad.reshape(SEQ, D).astype(jnp.bfloat16),
        key_grad.reshape(SEQ, D).astype(jnp.bfloat16),
        value_grad.reshape(SEQ, D).astype(jnp.bfloat16),
    )


def adam_step(master, first_moment, second, gradient, step_rate, decay_rate, step_float):
    first_new = beta_first * first_moment + (1.0 - beta_first) * gradient
    second_new = beta_second * second + (1.0 - beta_second) * gradient * gradient
    first_hat = first_new / (1.0 - beta_first**step_float)
    second_hat = second_new / (1.0 - beta_second**step_float)
    master_new = master - step_rate * (
        first_hat / (jnp.sqrt(second_hat) + adam_epsilon) + decay_rate * master
    )
    return (master_new, first_new, second_new)


def padded_rows(rows, multiple):
    return -(-rows // multiple) * multiple


def gather_working(attention_master, feed_master, small_master):
    attention_rows = attention_master.shape[0]
    feed_rows = feed_master.shape[0]
    small_count = small_master.shape[0]
    main_rows = attention_rows + feed_rows
    extra_rows = padded_rows(main_rows + padded_rows(small_count, D) // D, 16) - main_rows
    small_flat = jnp.zeros((extra_rows * D,), jnp.bfloat16)
    small_flat = small_flat.at[:small_count].set(small_master.astype(jnp.bfloat16))
    block = jnp.concatenate(
        [
            attention_master.astype(jnp.bfloat16),
            feed_master.astype(jnp.bfloat16),
            small_flat.reshape(extra_rows, D),
        ],
        axis=0,
    )
    gathered = lax.all_gather(block, ("fsdp", "dp"), axis=0, tiled=False)
    owners = gathered.shape[0]
    attention_full = gathered[:, :attention_rows].reshape(owners * attention_rows, D)
    feed_full = gathered[:, attention_rows:main_rows].reshape(owners * feed_rows, D)
    small_full = gathered[:, main_rows:].reshape(owners, extra_rows * D)[:, :small_count]
    return attention_full, feed_full, small_full.reshape(owners * small_count)


def flat_coordinates():
    me = lax.axis_index(("fsdp", "dp"))
    return me, me % 2, (me // 2) % 2, (me // 4) % 2, me // 8


def shifted(distance, count=32):
    return [(d, d + distance) for d in range(count) if 0 <= d + distance < count]


def flipped(mask, count=32):
    return [(d, d ^ mask) for d in range(count)]


def permute(arrays, pairs):
    return lax.ppermute(tuple(arrays), ("fsdp", "dp"), pairs)


def staged_reduce_scatter(arrays, late=()):
    me, y_place, core, x_place, z_place = flat_coordinates()
    blocks = [jnp.moveaxis(entries.reshape((4, 2, 2, 2) + entries.shape[1:]), 2, 0) for entries in arrays]
    keep = [lax.dynamic_index_in_dim(b, core, axis=0, keepdims=False) for b in blocks]
    send = [lax.dynamic_index_in_dim(b, 1 - core, axis=0, keepdims=False).astype(jnp.bfloat16) for b in blocks]
    received = permute(send, flipped(2))
    plane = [k.astype(jnp.float32) + r.astype(jnp.float32) for k, r in zip(keep, received)]
    plane, late = lax.optimization_barrier((plane, late))

    def pick(entries, x_index, y_index):
        picked = lax.dynamic_index_in_dim(entries, x_index, axis=1, keepdims=False)
        return lax.dynamic_index_in_dim(picked, y_index, axis=1, keepdims=False)

    along_z = [pick(p, x_place, y_place) for p in plane]
    for mask, x_index, y_index in ((4, 1 - x_place, y_place), (1, x_place, 1 - y_place), (5, 1 - x_place, 1 - y_place)):
        got = permute([pick(p, x_index, y_index).astype(jnp.bfloat16) for p in plane], flipped(mask))
        along_z = [a + g.astype(jnp.float32) for a, g in zip(along_z, got)]
    owned = [lax.dynamic_index_in_dim(a, z_place, axis=0, keepdims=False) for a in along_z]
    for distance in (1, 2, 3):
        up = permute(
            [lax.dynamic_index_in_dim(a, jnp.minimum(z_place + distance, 3), axis=0, keepdims=False).astype(jnp.bfloat16) for a in along_z],
            shifted(8 * distance),
        )
        down = permute(
            [lax.dynamic_index_in_dim(a, jnp.maximum(z_place - distance, 0), axis=0, keepdims=False).astype(jnp.bfloat16) for a in along_z],
            shifted(-8 * distance),
        )
        owned = [o + u.astype(jnp.float32) + w.astype(jnp.float32) for o, u, w in zip(owned, up, down)]
    return owned, late


def staged_all_gather(arrays):
    me, y_place, core, x_place, z_place = flat_coordinates()
    slot = [lax.broadcasted_iota(jnp.int32, (4,) + (1,) * a.ndim, 0) for a in arrays]
    grown = [jnp.where(s == z_place, a[None], jnp.zeros((4,) + a.shape, a.dtype)) for s, a in zip(slot, arrays)]
    for distance in (1, 2, 3):
        from_below = permute(arrays, shifted(8 * distance))
        from_above = permute(arrays, shifted(-8 * distance))
        grown = [jnp.where(s == z_place - distance, b[None], g) for s, b, g in zip(slot, from_below, grown)]
        grown = [jnp.where(s == z_place + distance, b[None], g) for s, b, g in zip(slot, from_above, grown)]
    got_x = permute(grown, flipped(4))
    got_y = permute(grown, flipped(1))
    got_xy = permute(grown, flipped(5))
    planes = []
    for own, gx, gy, gxy in zip(grown, got_x, got_y, got_xy):
        shape = (own.shape[0], 2, 2) + own.shape[1:]
        xs = lax.broadcasted_iota(jnp.int32, (1, 2, 1) + (1,) * (own.ndim - 1), 1)
        ys = lax.broadcasted_iota(jnp.int32, (1, 1, 2) + (1,) * (own.ndim - 1), 2)
        same_x, same_y = xs == x_place, ys == y_place
        plane = jnp.where(
            same_x,
            jnp.where(same_y, own[:, None, None], gy[:, None, None]),
            jnp.where(same_y, gx[:, None, None], gxy[:, None, None]),
        )
        planes.append(jnp.broadcast_to(plane, shape))
    got_core = permute(planes, flipped(2))
    gathered = []
    for own, other in zip(planes, got_core):
        own = own[:, :, None]
        other = other[:, :, None]
        size = own.shape[2]
        shape = own.shape[:2] + (2,) + own.shape[3:]
        start = [0] * len(shape)
        start_other = [0] * len(shape)
        start[2] = core * size
        start_other[2] = (1 - core) * size
        full = jnp.zeros(shape, own.dtype)
        full = lax.dynamic_update_slice(full, own, start)
        full = lax.dynamic_update_slice(full, other, start_other)
        gathered.append(full.reshape((32 * full.shape[4],) + full.shape[5:]))
    return gathered


def staged_working(attention_master, feed_master, small_master):
    small_count = small_master.shape[0]
    small_row = jnp.zeros((1, D), jnp.bfloat16).at[0, :small_count].set(small_master.astype(jnp.bfloat16))
    attention_full, small_rows = staged_all_gather([attention_master.astype(jnp.bfloat16), small_row])
    small_full = small_rows[:, :small_count].reshape(32 * small_count)
    feed_full = lax.all_gather(feed_master.astype(jnp.bfloat16), ("fsdp", "dp"), axis=0, tiled=True)
    return attention_full, feed_full, small_full


def scatter_gradients(attention_pieces, feed_pieces, small_grad_all, partials, staged, late):
    owners = lax.psum(1, ("fsdp", "dp"))
    me = lax.axis_index(("fsdp", "dp"))
    attention_rows = sum(piece.shape[0] for piece in attention_pieces) // owners
    small_count = small_grad_all.shape[0] // owners
    if staged:
        feed_rows = feed_pieces.shape[0] // owners
        dp = lax.axis_index("dp")
        within = lax.psum_scatter(
            feed_pieces.reshape(owners // 2, 2 * feed_rows, D), "fsdp", scatter_dimension=0, tiled=True
        ).reshape(2, feed_rows, D)
        keep = lax.dynamic_index_in_dim(within, dp, axis=0, keepdims=False)
        send = lax.dynamic_index_in_dim(within, 1 - dp, axis=0, keepdims=False)
        feed_owned = keep.astype(jnp.float32) + lax.ppermute(send, "dp", [(0, 1), (1, 0)]).astype(jnp.float32)
    else:
        feed_owned = lax.psum_scatter(feed_pieces, ("fsdp", "dp"), scatter_dimension=0, tiled=True)
    partials_high = partials.astype(jnp.bfloat16)
    partials_low = (partials - partials_high.astype(jnp.float32)).astype(jnp.bfloat16)
    split_partials = jnp.concatenate([partials_high, partials_low])
    slots = split_partials.shape[0]
    extra_count = small_count + owners * slots
    extra_rows = padded_rows(attention_rows + padded_rows(extra_count, D) // D, 16) - attention_rows
    slot_row = jnp.zeros((owners * slots,), jnp.bfloat16)
    slot_row = lax.dynamic_update_slice(slot_row, split_partials, (me * slots,))
    extra = jnp.concatenate(
        [
            small_grad_all.astype(jnp.bfloat16).reshape(owners, small_count),
            jnp.broadcast_to(slot_row[None], (owners, owners * slots)),
            jnp.zeros((owners, extra_rows * D - extra_count), jnp.bfloat16),
        ],
        axis=1,
    ).reshape(owners, extra_rows, D)
    block_rows = attention_rows + extra_rows
    if staged:
        attention_grad_all = jnp.concatenate(attention_pieces, axis=0).astype(jnp.bfloat16)
        packed = jnp.concatenate([attention_grad_all.reshape(owners, attention_rows, D), extra], axis=1)
        (owned,), late = staged_reduce_scatter([packed], late)
    else:
        packed = jnp.zeros((owners, block_rows, D), jnp.bfloat16)
        packed = lax.dynamic_update_slice(packed, extra, (0, attention_rows, 0))
        owner = 0
        for piece in attention_pieces:
            piece_owners = piece.shape[0] // attention_rows
            packed = lax.dynamic_update_slice(
                packed, piece.astype(jnp.bfloat16).reshape(piece_owners, attention_rows, D), (owner, 0, 0)
            )
            owner = owner + piece_owners
        owned = lax.psum_scatter(
            packed.reshape(owners * block_rows, D), ("fsdp", "dp"), scatter_dimension=0, tiled=True
        ).astype(jnp.float32)
    attention_owned = owned[:attention_rows]
    extra_owned = owned[attention_rows:].reshape(extra_rows * D)
    small_owned = extra_owned[:small_count]
    gathered_partials = extra_owned[small_count:extra_count].reshape(owners, slots)
    half = slots // 2
    totals = gathered_partials[0, :half] + gathered_partials[0, half:]
    for index in range(1, owners):
        totals = totals + (gathered_partials[index, :half] + gathered_partials[index, half:])
    return attention_owned, feed_owned.astype(jnp.float32), small_owned, totals, late


def on_device(
    staged,
    tokens,
    cotangent,
    lengths,
    step_count,
    attention_master,
    attention_first,
    attention_second,
    feed_master,
    feed_first,
    feed_second,
    small_master,
    small_first,
    small_second,
):
    row_count = tokens.shape[0]
    sequence_count = row_count // SEQ
    if staged:
        attention_full, feed_full, small_full = staged_working(attention_master, feed_master, small_master)
    else:
        attention_full, feed_full, small_full = gather_working(attention_master, feed_master, small_master)
    key_valid = (
        lax.broadcasted_iota(jnp.int32, (sequence_count, SEQ), 1) < lengths[:, None]
    ).astype(jnp.float32)
    token_valid = key_valid.reshape(row_count)
    (
        query_bias,
        value_bias,
        output_bias,
        inner_bias,
        outer_bias,
        first_gain,
        first_shift,
        second_gain,
        second_shift,
    ) = split_small(small_full)
    queries = (product(tokens, attention_full[0:D]) + query_bias).astype(jnp.bfloat16)
    key_vectors = product(tokens, attention_full[D : 2 * D]).astype(jnp.bfloat16)
    values = (product(tokens, attention_full[2 * D : 3 * D]) + value_bias).astype(jnp.bfloat16)
    seq_shape = (sequence_count, SEQ, D)
    attended, log_total = lax.map(
        attend_forward,
        (
            queries.reshape(seq_shape),
            key_vectors.reshape(seq_shape),
            values.reshape(seq_shape),
            key_valid,
        ),
    )
    attended = attended.reshape(row_count, D)
    branch_attention = product(attended, attention_full[3 * D : 4 * D]) + output_bias
    first_sum = tokens.astype(jnp.float32) + branch_attention
    normed = layer_norm(first_sum, first_gain, first_shift)
    normed_low = normed.astype(jnp.bfloat16)
    inner_sum = product_cols(normed_low, feed_full[0:FF]) + inner_bias
    active = gelu_exact(inner_sum).astype(jnp.bfloat16)
    gelu_slope = gelu_derivative(inner_sum)
    branch_feed = product(active, feed_full[FF : 2 * FF]) + outer_bias
    residual = normed + branch_feed
    column = token_valid[:, None]
    partials = jnp.stack(
        [
            jnp.sum(residual * residual * column),
            jnp.sum(branch_attention * branch_attention * column),
            jnp.sum(branch_feed * branch_feed * column),
            jnp.sum(token_valid),
        ]
    )
    query_weight = attention_full[0:D]
    key_weight = attention_full[D : 2 * D]
    value_weight = attention_full[2 * D : 3 * D]
    output_weight = attention_full[3 * D : 4 * D]
    outer_weight = feed_full[FF : 2 * FF]
    inner_weight = feed_full[0:FF]
    second_pull = jax.vjp(layer_norm, residual, second_gain, second_shift)[1]
    residual_grad, second_gain_grad, second_shift_grad = second_pull(cotangent)
    feed_out_grad = residual_grad.astype(jnp.bfloat16)
    outer_bias_grad = column_total(feed_out_grad)
    active_grad = product_cols(feed_out_grad, outer_weight)
    inner_grad = (active_grad * gelu_slope).astype(jnp.bfloat16)
    inner_bias_grad = column_total(inner_grad)
    feed_grad_all = (
        lax.dot_general(
            jnp.stack([inner_grad, active]),
            jnp.stack([normed_low, feed_out_grad]),
            (((1,), (1,)), ((0,), (0,))),
            preferred_element_type=jnp.float32,
        )
        .astype(jnp.bfloat16)
        .reshape(2 * FF, D)
    )
    feed_grad_all, inner_grad_late, partials = lax.optimization_barrier((feed_grad_all, inner_grad, partials))
    normed_grad = residual_grad + product(inner_grad_late, inner_weight)
    first_pull = jax.vjp(layer_norm, first_sum, first_gain, first_shift)[1]
    first_sum_grad, first_gain_grad, first_shift_grad = first_pull(normed_grad)
    branch_grad_low = first_sum_grad.astype(jnp.bfloat16)
    output_bias_grad = column_total(branch_grad_low)
    output_weight_grad = product_rows(attended, branch_grad_low)
    attended_grad = product_cols(branch_grad_low, output_weight).astype(jnp.bfloat16)
    query_grad, key_grad, value_grad = lax.map(
        attend_backward,
        (
            queries.reshape(seq_shape),
            key_vectors.reshape(seq_shape),
            values.reshape(seq_shape),
            key_valid,
            log_total,
            attended_grad.reshape(seq_shape),
        ),
    )
    query_grad = query_grad.reshape(row_count, D)
    key_grad = key_grad.reshape(row_count, D)
    value_grad = value_grad.reshape(row_count, D)
    query_weight_grad = product_rows(tokens, query_grad)
    key_weight_grad = product_rows(tokens, key_grad)
    value_weight_grad = product_rows(tokens, value_grad)
    query_bias_grad = column_total(query_grad)
    value_bias_grad = column_total(value_grad)
    small_grad_all = jnp.concatenate(
        [
            query_bias_grad,
            value_bias_grad,
            output_bias_grad,
            inner_bias_grad,
            outer_bias_grad,
            first_gain_grad,
            first_shift_grad,
            second_gain_grad,
            second_shift_grad,
        ]
    )
    attention_owned, feed_owned, small_owned, totals, late = scatter_gradients(
        [query_weight_grad, key_weight_grad, value_weight_grad, output_weight_grad],
        feed_grad_all,
        small_grad_all,
        partials,
        staged,
        (first_sum_grad, query_grad, key_grad, value_grad, residual),
    )
    first_sum_grad, query_grad, key_grad, value_grad, residual = late
    tokens_grad = (
        first_sum_grad
        + product_cols(query_grad, query_weight)
        + product_cols(key_grad, key_weight)
        + product_cols(value_grad, value_weight)
    )
    layer_out = layer_norm(residual, second_gain, second_shift).astype(jnp.bfloat16)
    rms_values = jnp.sqrt(totals[:3] / (totals[3] * D))
    step_float = step_count[0].astype(jnp.float32)
    attention_new, attention_first_new, attention_second_new = adam_step(
        attention_master,
        attention_first,
        attention_second,
        attention_owned,
        rate_matrix,
        weight_decay,
        step_float,
    )
    feed_new, feed_first_new, feed_second_new = adam_step(
        feed_master, feed_first, feed_second, feed_owned, rate_matrix, weight_decay, step_float
    )
    small_new, small_first_new, small_second_new = adam_step(
        small_master, small_first, small_second, small_owned, rate_small, 0.0, step_float
    )
    return (
        layer_out,
        tokens_grad,
        attention_new,
        attention_first_new,
        attention_second_new,
        attention_new.astype(jnp.bfloat16),
        feed_new,
        feed_first_new,
        feed_second_new,
        feed_new.astype(jnp.bfloat16),
        small_new,
        small_first_new,
        small_second_new,
        small_new.astype(jnp.bfloat16),
        rms_values,
    )


def solution(mesh):
    placed = (
        P(("fsdp", "dp"), None),
        P(("fsdp", "dp"), None),
        P(("fsdp", "dp")),
        P(),
        P(("fsdp", "dp"), None),
        P(("fsdp", "dp"), None),
        P(("fsdp", "dp"), None),
        P(("fsdp", "dp"), None),
        P(("fsdp", "dp"), None),
        P(("fsdp", "dp"), None),
        P(("fsdp", "dp")),
        P(("fsdp", "dp")),
        P(("fsdp", "dp")),
    )
    staged = dict(mesh.shape) == {"fsdp": 16, "dp": 2}
    return jax.shard_map(
        functools.partial(on_device, staged),
        mesh=mesh,
        in_specs=placed,
        out_specs=(
            P(("fsdp", "dp"), None),
            P(("fsdp", "dp"), None),
            P(("fsdp", "dp"), None),
            P(("fsdp", "dp"), None),
            P(("fsdp", "dp"), None),
            P(("fsdp", "dp"), None),
            P(("fsdp", "dp"), None),
            P(("fsdp", "dp"), None),
            P(("fsdp", "dp"), None),
            P(("fsdp", "dp"), None),
            P(("fsdp", "dp")),
            P(("fsdp", "dp")),
            P(("fsdp", "dp")),
            P(("fsdp", "dp")),
            P(),
        ),
        check_vma=False,
    )
```

```python
import functools
import math

import jax
import numpy as np
import jax.numpy as jnp
from jax import lax
from jax.sharding import PartitionSpec as P

D = 768
HEADS = 12
HDIM = 64
FF = 3072
SEQ = 512


ln_epsilon = 1e-12
beta_first = 0.5
beta_second = 0.55
adam_epsilon = 1e-06
rate_matrix = 0.04
rate_small = 0.25
weight_decay = 0.01


def product(left_side, right_side):
    return jnp.dot(left_side, right_side, preferred_element_type=jnp.float32)


def product_rows(left_side, right_side):
    return lax.dot_general(
        left_side, right_side, (((0,), (0,)), ((), ())), preferred_element_type=jnp.float32
    )


def product_cols(left_side, right_side):
    return lax.dot_general(
        left_side, right_side, (((1,), (1,)), ((), ())), preferred_element_type=jnp.float32
    )


def column_total(entries):
    return jnp.sum(entries, axis=0, dtype=jnp.float32)


def layer_norm(entries, norm_gain, norm_shift):
    center = jnp.mean(entries, axis=-1, keepdims=True)
    offset = entries - center
    spread = jnp.mean(offset * offset, axis=-1, keepdims=True)
    return offset * lax.rsqrt(spread + ln_epsilon) * norm_gain + norm_shift


def gelu_exact(entries):
    return jax.nn.gelu(entries, approximate=False)


def gelu_derivative(entries):
    sqrt_half = np.sqrt(0.5).astype(np.float32)
    shifted_entries = -entries * sqrt_half
    return 0.5 * lax.erfc(shifted_entries) + entries * (
        jnp.exp(-(shifted_entries * shifted_entries)) * np.float32(sqrt_half / np.sqrt(np.pi))
    )


def split_small(small_full):
    pieces = []
    position = 0
    for length in (D, D, D, FF, D, D, D, D, D):
        pieces.append(small_full[position : position + length].astype(jnp.float32))
        position = position + length
    return pieces


def head_view(entries):
    return entries.reshape(SEQ, HEADS, HDIM)


def masked_scores(queries, key_vectors, key_valid):
    scores = jnp.einsum(
        "qhd,khd->hqk",
        head_view(queries),
        head_view(key_vectors),
        preferred_element_type=jnp.float32,
    ) * (1.0 / math.sqrt(HDIM))
    return jnp.where(key_valid[None, None, :] > 0, scores, -1e30)


def attend_forward(pieces):
    queries, key_vectors, values, key_valid = pieces
    scores = masked_scores(queries, key_vectors, key_valid)
    row_max = jnp.max(scores, axis=-1, keepdims=True)
    exponent = jnp.exp(scores - row_max)
    row_total = jnp.sum(exponent, axis=-1, keepdims=True)
    probability = (exponent / row_total).astype(jnp.bfloat16)
    attended = jnp.einsum(
        "hqk,khd->qhd", probability, head_view(values), preferred_element_type=jnp.float32
    )
    return (attended.reshape(SEQ, D).astype(jnp.bfloat16), (row_max + jnp.log(row_total))[:, :, 0])


def attend_backward(pieces):
    queries, key_vectors, values, key_valid, log_total, attended_grad = pieces
    scores = masked_scores(queries, key_vectors, key_valid)
    probability = jnp.exp(scores - log_total[:, :, None])
    probability_low = probability.astype(jnp.bfloat16)
    grad_heads = head_view(attended_grad)
    value_grad = jnp.einsum(
        "hqk,qhd->khd", probability_low, grad_heads, preferred_element_type=jnp.float32
    )
    probability_grad = jnp.einsum(
        "qhd,khd->hqk", grad_heads, head_view(values), preferred_element_type=jnp.float32
    )
    inner_total = jnp.sum(probability * probability_grad, axis=-1, keepdims=True)
    score_grad = (probability * (probability_grad - inner_total)).astype(jnp.bfloat16)
    score_scale = 1.0 / math.sqrt(HDIM)
    query_grad = (
        jnp.einsum(
            "hqk,khd->qhd", score_grad, head_view(key_vectors), preferred_element_type=jnp.float32
        )
        * score_scale
    )
    key_grad = (
        jnp.einsum(
            "hqk,qhd->khd", score_grad, head_view(queries), preferred_element_type=jnp.float32
        )
        * score_scale
    )
    return (
        query_grad.reshape(SEQ, D).astype(jnp.bfloat16),
        key_grad.reshape(SEQ, D).astype(jnp.bfloat16),
        value_grad.reshape(SEQ, D).astype(jnp.bfloat16),
    )


def adam_step(master, first_moment, second, gradient, step_rate, decay_rate, step_float):
    first_new = beta_first * first_moment + (1.0 - beta_first) * gradient
    second_new = beta_second * second + (1.0 - beta_second) * gradient * gradient
    first_hat = first_new / (1.0 - beta_first**step_float)
    second_hat = second_new / (1.0 - beta_second**step_float)
    master_new = master - step_rate * (
        first_hat / (jnp.sqrt(second_hat) + adam_epsilon) + decay_rate * master
    )
    return (master_new, first_new, second_new)


def padded_rows(rows, multiple):
    return -(-rows // multiple) * multiple


def gather_working(attention_master, feed_master, small_master):
    attention_rows = attention_master.shape[0]
    feed_rows = feed_master.shape[0]
    small_count = small_master.shape[0]
    main_rows = attention_rows + feed_rows
    extra_rows = padded_rows(main_rows + padded_rows(small_count, D) // D, 16) - main_rows
    small_flat = jnp.zeros((extra_rows * D,), jnp.bfloat16)
    small_flat = small_flat.at[:small_count].set(small_master.astype(jnp.bfloat16))
    block = jnp.concatenate(
        [
            attention_master.astype(jnp.bfloat16),
            feed_master.astype(jnp.bfloat16),
            small_flat.reshape(extra_rows, D),
        ],
        axis=0,
    )
    gathered = lax.all_gather(block, ("fsdp", "dp"), axis=0, tiled=False)
    owners = gathered.shape[0]
    attention_full = gathered[:, :attention_rows].reshape(owners * attention_rows, D)
    feed_full = gathered[:, attention_rows:main_rows].reshape(owners * feed_rows, D)
    small_full = gathered[:, main_rows:].reshape(owners, extra_rows * D)[:, :small_count]
    return attention_full, feed_full, small_full.reshape(owners * small_count)


def flat_coordinates():
    me = lax.axis_index(("fsdp", "dp"))
    return me, me % 2, (me // 2) % 2, (me // 4) % 2, me // 8


def shifted(distance, count=32):
    return [(d, d + distance) for d in range(count) if 0 <= d + distance < count]


def rotated(distance, count=32):
    return [(d, (d + distance) % count) for d in range(count)]


def flipped(mask, count=32):
    return [(d, d ^ mask) for d in range(count)]


def permute(arrays, pairs):
    return lax.ppermute(tuple(arrays), ("fsdp", "dp"), pairs)


def staged_reduce_scatter(arrays, late=()):
    me, y_place, core, x_place, z_place = flat_coordinates()
    blocks = [jnp.moveaxis(entries.reshape((4, 2, 2, 2) + entries.shape[1:]), 2, 0) for entries in arrays]
    keep = [lax.dynamic_index_in_dim(b, core, axis=0, keepdims=False) for b in blocks]
    send = [lax.dynamic_index_in_dim(b, 1 - core, axis=0, keepdims=False).astype(jnp.bfloat16) for b in blocks]
    received = permute(send, flipped(2))
    plane = [k.astype(jnp.float32) + r.astype(jnp.float32) for k, r in zip(keep, received)]
    plane, late = lax.optimization_barrier((plane, late))

    def pick(entries, x_index, y_index):
        picked = lax.dynamic_index_in_dim(entries, x_index, axis=1, keepdims=False)
        return lax.dynamic_index_in_dim(picked, y_index, axis=1, keepdims=False)

    along_z = [pick(p, x_place, y_place) for p in plane]
    for mask, x_index, y_index in ((4, 1 - x_place, y_place), (1, x_place, 1 - y_place), (5, 1 - x_place, 1 - y_place)):
        got = permute([pick(p, x_index, y_index).astype(jnp.bfloat16) for p in plane], flipped(mask))
        along_z = [a + g.astype(jnp.float32) for a, g in zip(along_z, got)]
    owned = [lax.dynamic_index_in_dim(a, z_place, axis=0, keepdims=False) for a in along_z]
    for distance in (1, 2, 3):
        got = permute(
            [lax.dynamic_index_in_dim(a, (z_place + distance) % 4, axis=0, keepdims=False).astype(jnp.bfloat16) for a in along_z],
            rotated(8 * distance),
        )
        owned = [o + g.astype(jnp.float32) for o, g in zip(owned, got)]
    return owned, late


def staged_all_gather(arrays):
    me, y_place, core, x_place, z_place = flat_coordinates()
    slot = [lax.broadcasted_iota(jnp.int32, (4,) + (1,) * a.ndim, 0) for a in arrays]
    grown = [jnp.where(s == z_place, a[None], jnp.zeros((4,) + a.shape, a.dtype)) for s, a in zip(slot, arrays)]
    for distance in (1, 2, 3):
        received = permute(arrays, rotated(8 * distance))
        grown = [jnp.where(s == (z_place - distance) % 4, b[None], g) for s, b, g in zip(slot, received, grown)]
    got_x = permute(grown, flipped(4))
    got_y = permute(grown, flipped(1))
    got_xy = permute(grown, flipped(5))
    planes = []
    for own, gx, gy, gxy in zip(grown, got_x, got_y, got_xy):
        shape = (own.shape[0], 2, 2) + own.shape[1:]
        xs = lax.broadcasted_iota(jnp.int32, (1, 2, 1) + (1,) * (own.ndim - 1), 1)
        ys = lax.broadcasted_iota(jnp.int32, (1, 1, 2) + (1,) * (own.ndim - 1), 2)
        same_x, same_y = xs == x_place, ys == y_place
        plane = jnp.where(
            same_x,
            jnp.where(same_y, own[:, None, None], gy[:, None, None]),
            jnp.where(same_y, gx[:, None, None], gxy[:, None, None]),
        )
        planes.append(jnp.broadcast_to(plane, shape))
    got_core = permute(planes, flipped(2))
    gathered = []
    for own, other in zip(planes, got_core):
        own = own[:, :, None]
        other = other[:, :, None]
        size = own.shape[2]
        shape = own.shape[:2] + (2,) + own.shape[3:]
        start = [0] * len(shape)
        start_other = [0] * len(shape)
        start[2] = core * size
        start_other[2] = (1 - core) * size
        full = jnp.zeros(shape, own.dtype)
        full = lax.dynamic_update_slice(full, own, start)
        full = lax.dynamic_update_slice(full, other, start_other)
        gathered.append(full.reshape((32 * full.shape[4],) + full.shape[5:]))
    return gathered


def staged_working(attention_master, feed_master, small_master):
    small_count = small_master.shape[0]
    small_row = jnp.zeros((1, D), jnp.bfloat16).at[0, :small_count].set(small_master.astype(jnp.bfloat16))
    attention_full, small_rows = staged_all_gather([attention_master.astype(jnp.bfloat16), small_row])
    small_full = small_rows[:, :small_count].reshape(32 * small_count)
    feed_full = lax.all_gather(feed_master.astype(jnp.bfloat16), ("fsdp", "dp"), axis=0, tiled=True)
    return attention_full, feed_full, small_full


def scatter_gradients(attention_pieces, feed_pieces, small_grad_all, partials, staged, late):
    owners = lax.psum(1, ("fsdp", "dp"))
    me = lax.axis_index(("fsdp", "dp"))
    attention_rows = sum(piece.shape[0] for piece in attention_pieces) // owners
    small_count = small_grad_all.shape[0] // owners
    if staged:
        feed_rows = feed_pieces.shape[0] // owners
        dp = lax.axis_index("dp")
        within = lax.psum_scatter(
            feed_pieces.reshape(owners // 2, 2 * feed_rows, D), "fsdp", scatter_dimension=0, tiled=True
        ).reshape(2, feed_rows, D)
        keep = lax.dynamic_index_in_dim(within, dp, axis=0, keepdims=False)
        send = lax.dynamic_index_in_dim(within, 1 - dp, axis=0, keepdims=False)
        feed_owned = keep.astype(jnp.float32) + lax.ppermute(send, "dp", [(0, 1), (1, 0)]).astype(jnp.float32)
    else:
        feed_owned = lax.psum_scatter(feed_pieces, ("fsdp", "dp"), scatter_dimension=0, tiled=True)
    partials_high = partials.astype(jnp.bfloat16)
    partials_low = (partials - partials_high.astype(jnp.float32)).astype(jnp.bfloat16)
    split_partials = jnp.concatenate([partials_high, partials_low])
    slots = split_partials.shape[0]
    extra_count = small_count + owners * slots
    extra_rows = padded_rows(attention_rows + padded_rows(extra_count, D) // D, 16) - attention_rows
    slot_row = jnp.zeros((owners * slots,), jnp.bfloat16)
    slot_row = lax.dynamic_update_slice(slot_row, split_partials, (me * slots,))
    extra = jnp.concatenate(
        [
            small_grad_all.astype(jnp.bfloat16).reshape(owners, small_count),
            jnp.broadcast_to(slot_row[None], (owners, owners * slots)),
            jnp.zeros((owners, extra_rows * D - extra_count), jnp.bfloat16),
        ],
        axis=1,
    ).reshape(owners, extra_rows, D)
    block_rows = attention_rows + extra_rows
    if staged:
        attention_grad_all = jnp.concatenate(attention_pieces, axis=0).astype(jnp.bfloat16)
        owned_parts, late = staged_reduce_scatter(
            [attention_grad_all.reshape(owners, attention_rows, D), extra], late
        )
        owned = jnp.concatenate(owned_parts, axis=0)
    else:
        packed = jnp.zeros((owners, block_rows, D), jnp.bfloat16)
        packed = lax.dynamic_update_slice(packed, extra, (0, attention_rows, 0))
        owner = 0
        for piece in attention_pieces:
            piece_owners = piece.shape[0] // attention_rows
            packed = lax.dynamic_update_slice(
                packed, piece.astype(jnp.bfloat16).reshape(piece_owners, attention_rows, D), (owner, 0, 0)
            )
            owner = owner + piece_owners
        owned = lax.psum_scatter(
            packed.reshape(owners * block_rows, D), ("fsdp", "dp"), scatter_dimension=0, tiled=True
        ).astype(jnp.float32)
    attention_owned = owned[:attention_rows]
    extra_owned = owned[attention_rows:].reshape(extra_rows * D)
    small_owned = extra_owned[:small_count]
    gathered_partials = extra_owned[small_count:extra_count].reshape(owners, slots)
    half = slots // 2
    totals = gathered_partials[0, :half] + gathered_partials[0, half:]
    for index in range(1, owners):
        totals = totals + (gathered_partials[index, :half] + gathered_partials[index, half:])
    return attention_owned, feed_owned.astype(jnp.float32), small_owned, totals, late


def on_device(
    staged,
    tokens,
    cotangent,
    lengths,
    step_count,
    attention_master,
    attention_first,
    attention_second,
    feed_master,
    feed_first,
    feed_second,
    small_master,
    small_first,
    small_second,
):
    row_count = tokens.shape[0]
    sequence_count = row_count // SEQ
    if staged:
        attention_full, feed_full, small_full = staged_working(attention_master, feed_master, small_master)
    else:
        attention_full, feed_full, small_full = gather_working(attention_master, feed_master, small_master)
    key_valid = (
        lax.broadcasted_iota(jnp.int32, (sequence_count, SEQ), 1) < lengths[:, None]
    ).astype(jnp.float32)
    token_valid = key_valid.reshape(row_count)
    (
        query_bias,
        value_bias,
        output_bias,
        inner_bias,
        outer_bias,
        first_gain,
        first_shift,
        second_gain,
        second_shift,
    ) = split_small(small_full)
    queries = (product(tokens, attention_full[0:D]) + query_bias).astype(jnp.bfloat16)
    key_vectors = product(tokens, attention_full[D : 2 * D]).astype(jnp.bfloat16)
    values = (product(tokens, attention_full[2 * D : 3 * D]) + value_bias).astype(jnp.bfloat16)
    seq_shape = (sequence_count, SEQ, D)
    attended, log_total = lax.map(
        attend_forward,
        (
            queries.reshape(seq_shape),
            key_vectors.reshape(seq_shape),
            values.reshape(seq_shape),
            key_valid,
        ),
    )
    attended = attended.reshape(row_count, D)
    branch_attention = product(attended, attention_full[3 * D : 4 * D]) + output_bias
    first_sum = tokens.astype(jnp.float32) + branch_attention
    normed = layer_norm(first_sum, first_gain, first_shift)
    normed_low = normed.astype(jnp.bfloat16)
    inner_sum = product_cols(normed_low, feed_full[0:FF]) + inner_bias
    active = gelu_exact(inner_sum).astype(jnp.bfloat16)
    gelu_slope = gelu_derivative(inner_sum)
    branch_feed = product(active, feed_full[FF : 2 * FF]) + outer_bias
    residual = normed + branch_feed
    column = token_valid[:, None]
    partials = jnp.stack(
        [
            jnp.sum(residual * residual * column),
            jnp.sum(branch_attention * branch_attention * column),
            jnp.sum(branch_feed * branch_feed * column),
            jnp.sum(token_valid),
        ]
    )
    query_weight = attention_full[0:D]
    key_weight = attention_full[D : 2 * D]
    value_weight = attention_full[2 * D : 3 * D]
    output_weight = attention_full[3 * D : 4 * D]
    outer_weight = feed_full[FF : 2 * FF]
    inner_weight = feed_full[0:FF]
    second_pull = jax.vjp(layer_norm, residual, second_gain, second_shift)[1]
    residual_grad, second_gain_grad, second_shift_grad = second_pull(cotangent)
    feed_out_grad = residual_grad.astype(jnp.bfloat16)
    outer_bias_grad = column_total(feed_out_grad)
    active_grad = product_cols(feed_out_grad, outer_weight)
    inner_grad = (active_grad * gelu_slope).astype(jnp.bfloat16)
    inner_bias_grad = column_total(inner_grad)
    feed_grad_all = (
        lax.dot_general(
            jnp.stack([inner_grad, active]),
            jnp.stack([normed_low, feed_out_grad]),
            (((1,), (1,)), ((0,), (0,))),
            preferred_element_type=jnp.float32,
        )
        .astype(jnp.bfloat16)
        .reshape(2 * FF, D)
    )
    feed_grad_all, inner_grad_late, partials = lax.optimization_barrier((feed_grad_all, inner_grad, partials))
    normed_grad = residual_grad + product(inner_grad_late, inner_weight)
    first_pull = jax.vjp(layer_norm, first_sum, first_gain, first_shift)[1]
    first_sum_grad, first_gain_grad, first_shift_grad = first_pull(normed_grad)
    branch_grad_low = first_sum_grad.astype(jnp.bfloat16)
    output_bias_grad = column_total(branch_grad_low)
    output_weight_grad = product_rows(attended, branch_grad_low)
    attended_grad = product_cols(branch_grad_low, output_weight).astype(jnp.bfloat16)
    query_grad, key_grad, value_grad = lax.map(
        attend_backward,
        (
            queries.reshape(seq_shape),
            key_vectors.reshape(seq_shape),
            values.reshape(seq_shape),
            key_valid,
            log_total,
            attended_grad.reshape(seq_shape),
        ),
    )
    query_grad = query_grad.reshape(row_count, D)
    key_grad = key_grad.reshape(row_count, D)
    value_grad = value_grad.reshape(row_count, D)
    query_weight_grad = product_rows(tokens, query_grad)
    key_weight_grad = product_rows(tokens, key_grad)
    value_weight_grad = product_rows(tokens, value_grad)
    query_bias_grad = column_total(query_grad)
    value_bias_grad = column_total(value_grad)
    small_grad_all = jnp.concatenate(
        [
            query_bias_grad,
            value_bias_grad,
            output_bias_grad,
            inner_bias_grad,
            outer_bias_grad,
            first_gain_grad,
            first_shift_grad,
            second_gain_grad,
            second_shift_grad,
        ]
    )
    attention_owned, feed_owned, small_owned, totals, late = scatter_gradients(
        [query_weight_grad, key_weight_grad, value_weight_grad, output_weight_grad],
        feed_grad_all,
        small_grad_all,
        partials,
        staged,
        (first_sum_grad, query_grad, key_grad, value_grad, residual),
    )
    first_sum_grad, query_grad, key_grad, value_grad, residual = late
    tokens_grad = (
        first_sum_grad
        + product_cols(query_grad, query_weight)
        + product_cols(key_grad, key_weight)
        + product_cols(value_grad, value_weight)
    )
    layer_out = layer_norm(residual, second_gain, second_shift).astype(jnp.bfloat16)
    rms_values = jnp.sqrt(totals[:3] / (totals[3] * D))
    step_float = step_count[0].astype(jnp.float32)
    attention_new, attention_first_new, attention_second_new = adam_step(
        attention_master,
        attention_first,
        attention_second,
        attention_owned,
        rate_matrix,
        weight_decay,
        step_float,
    )
    feed_new, feed_first_new, feed_second_new = adam_step(
        feed_master, feed_first, feed_second, feed_owned, rate_matrix, weight_decay, step_float
    )
    small_new, small_first_new, small_second_new = adam_step(
        small_master, small_first, small_second, small_owned, rate_small, 0.0, step_float
    )
    return (
        layer_out,
        tokens_grad,
        attention_new,
        attention_first_new,
        attention_second_new,
        attention_new.astype(jnp.bfloat16),
        feed_new,
        feed_first_new,
        feed_second_new,
        feed_new.astype(jnp.bfloat16),
        small_new,
        small_first_new,
        small_second_new,
        small_new.astype(jnp.bfloat16),
        rms_values,
    )


def solution(mesh):
    placed = (
        P(("fsdp", "dp"), None),
        P(("fsdp", "dp"), None),
        P(("fsdp", "dp")),
        P(),
        P(("fsdp", "dp"), None),
        P(("fsdp", "dp"), None),
        P(("fsdp", "dp"), None),
        P(("fsdp", "dp"), None),
        P(("fsdp", "dp"), None),
        P(("fsdp", "dp"), None),
        P(("fsdp", "dp")),
        P(("fsdp", "dp")),
        P(("fsdp", "dp")),
    )
    staged = dict(mesh.shape) == {"fsdp": 16, "dp": 2}
    return jax.shard_map(
        functools.partial(on_device, staged),
        mesh=mesh,
        in_specs=placed,
        out_specs=(
            P(("fsdp", "dp"), None),
            P(("fsdp", "dp"), None),
            P(("fsdp", "dp"), None),
            P(("fsdp", "dp"), None),
            P(("fsdp", "dp"), None),
            P(("fsdp", "dp"), None),
            P(("fsdp", "dp"), None),
            P(("fsdp", "dp"), None),
            P(("fsdp", "dp"), None),
            P(("fsdp", "dp"), None),
            P(("fsdp", "dp")),
            P(("fsdp", "dp")),
            P(("fsdp", "dp")),
            P(("fsdp", "dp")),
            P(),
        ),
        check_vma=False,
    )
```

```python
import functools
import math

import jax
import numpy as np
import jax.numpy as jnp
from jax import lax
from jax.sharding import PartitionSpec as P

D = 768
HEADS = 12
HDIM = 64
FF = 3072
SEQ = 512


ln_epsilon = 1e-12
beta_first = 0.5
beta_second = 0.55
adam_epsilon = 1e-06
rate_matrix = 0.04
rate_small = 0.25
weight_decay = 0.01


def product(left_side, right_side):
    return jnp.dot(left_side, right_side, preferred_element_type=jnp.float32)


def product_rows(left_side, right_side):
    return lax.dot_general(
        left_side, right_side, (((0,), (0,)), ((), ())), preferred_element_type=jnp.float32
    )


def product_cols(left_side, right_side):
    return lax.dot_general(
        left_side, right_side, (((1,), (1,)), ((), ())), preferred_element_type=jnp.float32
    )


def column_total(entries):
    return jnp.sum(entries, axis=0, dtype=jnp.float32)


def layer_norm(entries, norm_gain, norm_shift):
    center = jnp.mean(entries, axis=-1, keepdims=True)
    offset = entries - center
    spread = jnp.mean(offset * offset, axis=-1, keepdims=True)
    return offset * lax.rsqrt(spread + ln_epsilon) * norm_gain + norm_shift


def gelu_exact(entries):
    return jax.nn.gelu(entries, approximate=False)


def gelu_derivative(entries):
    sqrt_half = np.sqrt(0.5).astype(np.float32)
    shifted_entries = -entries * sqrt_half
    return 0.5 * lax.erfc(shifted_entries) + entries * (
        jnp.exp(-(shifted_entries * shifted_entries)) * np.float32(sqrt_half / np.sqrt(np.pi))
    )


def split_small(small_full):
    pieces = []
    position = 0
    for length in (D, D, D, FF, D, D, D, D, D):
        pieces.append(small_full[position : position + length].astype(jnp.float32))
        position = position + length
    return pieces


def head_view(entries):
    return entries.reshape(SEQ, HEADS, HDIM)


def masked_scores(queries, key_vectors, key_valid):
    scores = jnp.einsum(
        "qhd,khd->hqk",
        head_view(queries),
        head_view(key_vectors),
        preferred_element_type=jnp.float32,
    ) * (1.0 / math.sqrt(HDIM))
    return jnp.where(key_valid[None, None, :] > 0, scores, -1e30)


def attend_forward(pieces):
    queries, key_vectors, values, key_valid = pieces
    scores = masked_scores(queries, key_vectors, key_valid)
    row_max = jnp.max(scores, axis=-1, keepdims=True)
    exponent = jnp.exp(scores - row_max)
    row_total = jnp.sum(exponent, axis=-1, keepdims=True)
    probability = (exponent / row_total).astype(jnp.bfloat16)
    attended = jnp.einsum(
        "hqk,khd->qhd", probability, head_view(values), preferred_element_type=jnp.float32
    )
    return (attended.reshape(SEQ, D).astype(jnp.bfloat16), (row_max + jnp.log(row_total))[:, :, 0])


def attend_backward(pieces):
    queries, key_vectors, values, key_valid, log_total, attended_grad = pieces
    scores = masked_scores(queries, key_vectors, key_valid)
    probability = jnp.exp(scores - log_total[:, :, None])
    probability_low = probability.astype(jnp.bfloat16)
    grad_heads = head_view(attended_grad)
    value_grad = jnp.einsum(
        "hqk,qhd->khd", probability_low, grad_heads, preferred_element_type=jnp.float32
    )
    probability_grad = jnp.einsum(
        "qhd,khd->hqk", grad_heads, head_view(values), preferred_element_type=jnp.float32
    )
    inner_total = jnp.sum(probability * probability_grad, axis=-1, keepdims=True)
    score_grad = (probability * (probability_grad - inner_total)).astype(jnp.bfloat16)
    score_scale = 1.0 / math.sqrt(HDIM)
    query_grad = (
        jnp.einsum(
            "hqk,khd->qhd", score_grad, head_view(key_vectors), preferred_element_type=jnp.float32
        )
        * score_scale
    )
    key_grad = (
        jnp.einsum(
            "hqk,qhd->khd", score_grad, head_view(queries), preferred_element_type=jnp.float32
        )
        * score_scale
    )
    return (
        query_grad.reshape(SEQ, D).astype(jnp.bfloat16),
        key_grad.reshape(SEQ, D).astype(jnp.bfloat16),
        value_grad.reshape(SEQ, D).astype(jnp.bfloat16),
    )


def adam_step(master, first_moment, second, gradient, step_rate, decay_rate, step_float):
    first_new = beta_first * first_moment + (1.0 - beta_first) * gradient
    second_new = beta_second * second + (1.0 - beta_second) * gradient * gradient
    first_hat = first_new / (1.0 - beta_first**step_float)
    second_hat = second_new / (1.0 - beta_second**step_float)
    master_new = master - step_rate * (
        first_hat / (jnp.sqrt(second_hat) + adam_epsilon) + decay_rate * master
    )
    return (master_new, first_new, second_new)


def padded_rows(rows, multiple):
    return -(-rows // multiple) * multiple


def gather_working(attention_master, feed_master, small_master):
    attention_rows = attention_master.shape[0]
    feed_rows = feed_master.shape[0]
    small_count = small_master.shape[0]
    main_rows = attention_rows + feed_rows
    extra_rows = padded_rows(main_rows + padded_rows(small_count, D) // D, 16) - main_rows
    small_flat = jnp.zeros((extra_rows * D,), jnp.bfloat16)
    small_flat = small_flat.at[:small_count].set(small_master.astype(jnp.bfloat16))
    block = jnp.concatenate(
        [
            attention_master.astype(jnp.bfloat16),
            feed_master.astype(jnp.bfloat16),
            small_flat.reshape(extra_rows, D),
        ],
        axis=0,
    )
    gathered = lax.all_gather(block, ("fsdp", "dp"), axis=0, tiled=False)
    owners = gathered.shape[0]
    attention_full = gathered[:, :attention_rows].reshape(owners * attention_rows, D)
    feed_full = gathered[:, attention_rows:main_rows].reshape(owners * feed_rows, D)
    small_full = gathered[:, main_rows:].reshape(owners, extra_rows * D)[:, :small_count]
    return attention_full, feed_full, small_full.reshape(owners * small_count)


def flat_coordinates():
    me = lax.axis_index(("fsdp", "dp"))
    return me, me % 2, (me // 2) % 2, (me // 4) % 2, me // 8


def shifted(distance, count=32):
    return [(d, d + distance) for d in range(count) if 0 <= d + distance < count]


def rotated(distance, count=32):
    return [(d, (d + distance) % count) for d in range(count)]


def flipped(mask, count=32):
    return [(d, d ^ mask) for d in range(count)]


def permute(arrays, pairs):
    return lax.ppermute(tuple(arrays), ("fsdp", "dp"), pairs)


def staged_reduce_scatter(arrays, late=()):
    me, y_place, core, x_place, z_place = flat_coordinates()
    blocks = [jnp.moveaxis(entries.reshape((4, 2, 2, 2) + entries.shape[1:]), 2, 0) for entries in arrays]
    keep = [lax.dynamic_index_in_dim(b, core, axis=0, keepdims=False) for b in blocks]
    send = [lax.dynamic_index_in_dim(b, 1 - core, axis=0, keepdims=False).astype(jnp.bfloat16) for b in blocks]
    received = permute(send, flipped(2))
    plane = [k.astype(jnp.float32) + r.astype(jnp.float32) for k, r in zip(keep, received)]
    plane, late = lax.optimization_barrier((plane, late))

    def pick(entries, x_index, y_index):
        picked = lax.dynamic_index_in_dim(entries, x_index, axis=1, keepdims=False)
        return lax.dynamic_index_in_dim(picked, y_index, axis=1, keepdims=False)

    along_z = [pick(p, x_place, y_place) for p in plane]
    for mask, x_index, y_index in ((4, 1 - x_place, y_place), (1, x_place, 1 - y_place), (5, 1 - x_place, 1 - y_place)):
        got = permute([pick(p, x_index, y_index).astype(jnp.bfloat16) for p in plane], flipped(mask))
        along_z = [a + g.astype(jnp.float32) for a, g in zip(along_z, got)]
    owned = [lax.dynamic_index_in_dim(a, z_place, axis=0, keepdims=False) for a in along_z]
    for distance in (1, 2, 3):
        got = permute(
            [lax.dynamic_index_in_dim(a, (z_place + distance) % 4, axis=0, keepdims=False).astype(jnp.bfloat16) for a in along_z],
            rotated(8 * distance),
        )
        owned = [o + g.astype(jnp.float32) for o, g in zip(owned, got)]
    return owned, late


def staged_all_gather(arrays):
    me, y_place, core, x_place, z_place = flat_coordinates()
    slot = [lax.broadcasted_iota(jnp.int32, (4,) + (1,) * a.ndim, 0) for a in arrays]
    grown = [jnp.where(s == z_place, a[None], jnp.zeros((4,) + a.shape, a.dtype)) for s, a in zip(slot, arrays)]
    for distance in (1, 2, 3):
        received = permute(arrays, rotated(8 * distance))
        grown = [jnp.where(s == (z_place - distance) % 4, b[None], g) for s, b, g in zip(slot, received, grown)]
    got_x = permute(grown, flipped(4))
    got_y = permute(grown, flipped(1))
    got_xy = permute(grown, flipped(5))
    planes = []
    for own, gx, gy, gxy in zip(grown, got_x, got_y, got_xy):
        shape = (own.shape[0], 2, 2) + own.shape[1:]
        xs = lax.broadcasted_iota(jnp.int32, (1, 2, 1) + (1,) * (own.ndim - 1), 1)
        ys = lax.broadcasted_iota(jnp.int32, (1, 1, 2) + (1,) * (own.ndim - 1), 2)
        same_x, same_y = xs == x_place, ys == y_place
        plane = jnp.where(
            same_x,
            jnp.where(same_y, own[:, None, None], gy[:, None, None]),
            jnp.where(same_y, gx[:, None, None], gxy[:, None, None]),
        )
        planes.append(jnp.broadcast_to(plane, shape))
    got_core = permute(planes, flipped(2))
    gathered = []
    for own, other in zip(planes, got_core):
        own = own[:, :, None]
        other = other[:, :, None]
        size = own.shape[2]
        shape = own.shape[:2] + (2,) + own.shape[3:]
        start = [0] * len(shape)
        start_other = [0] * len(shape)
        start[2] = core * size
        start_other[2] = (1 - core) * size
        full = jnp.zeros(shape, own.dtype)
        full = lax.dynamic_update_slice(full, own, start)
        full = lax.dynamic_update_slice(full, other, start_other)
        gathered.append(full.reshape((32 * full.shape[4],) + full.shape[5:]))
    return gathered


def staged_working(attention_master, feed_master, small_master):
    small_count = small_master.shape[0]
    small_row = jnp.zeros((1, D), jnp.bfloat16).at[0, :small_count].set(small_master.astype(jnp.bfloat16))
    attention_full, small_rows = staged_all_gather([attention_master.astype(jnp.bfloat16), small_row])
    small_full = small_rows[:, :small_count].reshape(32 * small_count)
    feed_full = lax.all_gather(feed_master.astype(jnp.bfloat16), ("fsdp", "dp"), axis=0, tiled=True)
    return attention_full, feed_full, small_full


def scatter_gradients(attention_pieces, feed_pieces, small_grad_all, partials, staged, late):
    owners = lax.psum(1, ("fsdp", "dp"))
    me = lax.axis_index(("fsdp", "dp"))
    attention_rows = sum(piece.shape[0] for piece in attention_pieces) // owners
    small_count = small_grad_all.shape[0] // owners
    if staged:
        feed_rows = feed_pieces.shape[0] // owners
        dp = lax.axis_index("dp")
        within = lax.psum_scatter(
            feed_pieces.reshape(owners // 2, 2 * feed_rows, D), "fsdp", scatter_dimension=0, tiled=True
        ).reshape(2, feed_rows, D)
        keep = lax.dynamic_index_in_dim(within, dp, axis=0, keepdims=False)
        send = lax.dynamic_index_in_dim(within, 1 - dp, axis=0, keepdims=False)
        feed_owned = keep.astype(jnp.float32) + lax.ppermute(send, "dp", [(0, 1), (1, 0)]).astype(jnp.float32)
    else:
        feed_owned = lax.psum_scatter(feed_pieces, ("fsdp", "dp"), scatter_dimension=0, tiled=True)
    partials_high = partials.astype(jnp.bfloat16)
    partials_low = (partials - partials_high.astype(jnp.float32)).astype(jnp.bfloat16)
    split_partials = jnp.concatenate([partials_high, partials_low])
    slots = split_partials.shape[0]
    extra_count = small_count + owners * slots
    extra_rows = padded_rows(attention_rows + padded_rows(extra_count, D) // D, 16) - attention_rows
    slot_row = jnp.zeros((owners * slots,), jnp.bfloat16)
    slot_row = lax.dynamic_update_slice(slot_row, split_partials, (me * slots,))
    extra = jnp.concatenate(
        [
            small_grad_all.astype(jnp.bfloat16).reshape(owners, small_count),
            jnp.broadcast_to(slot_row[None], (owners, owners * slots)),
            jnp.zeros((owners, extra_rows * D - extra_count), jnp.bfloat16),
        ],
        axis=1,
    ).reshape(owners, extra_rows, D)
    block_rows = attention_rows + extra_rows
    if staged:
        attention_grad_all = jnp.concatenate(attention_pieces, axis=0).astype(jnp.bfloat16)
        owned_parts, late = staged_reduce_scatter(
            [attention_grad_all.reshape(owners, attention_rows, D), extra], late
        )
        owned = jnp.concatenate(owned_parts, axis=0)
    else:
        packed = jnp.zeros((owners, block_rows, D), jnp.bfloat16)
        packed = lax.dynamic_update_slice(packed, extra, (0, attention_rows, 0))
        owner = 0
        for piece in attention_pieces:
            piece_owners = piece.shape[0] // attention_rows
            packed = lax.dynamic_update_slice(
                packed, piece.astype(jnp.bfloat16).reshape(piece_owners, attention_rows, D), (owner, 0, 0)
            )
            owner = owner + piece_owners
        owned = lax.psum_scatter(
            packed.reshape(owners * block_rows, D), ("fsdp", "dp"), scatter_dimension=0, tiled=True
        ).astype(jnp.float32)
    attention_owned = owned[:attention_rows]
    extra_owned = owned[attention_rows:].reshape(extra_rows * D)
    small_owned = extra_owned[:small_count]
    gathered_partials = extra_owned[small_count:extra_count].reshape(owners, slots)
    half = slots // 2
    totals = gathered_partials[0, :half] + gathered_partials[0, half:]
    for index in range(1, owners):
        totals = totals + (gathered_partials[index, :half] + gathered_partials[index, half:])
    return attention_owned, feed_owned.astype(jnp.float32), small_owned, totals, late


def on_device(
    staged,
    tokens,
    cotangent,
    lengths,
    step_count,
    attention_master,
    attention_first,
    attention_second,
    feed_master,
    feed_first,
    feed_second,
    small_master,
    small_first,
    small_second,
):
    row_count = tokens.shape[0]
    sequence_count = row_count // SEQ
    if staged:
        attention_full, feed_full, small_full = staged_working(attention_master, feed_master, small_master)
    else:
        attention_full, feed_full, small_full = gather_working(attention_master, feed_master, small_master)
    key_valid = (
        lax.broadcasted_iota(jnp.int32, (sequence_count, SEQ), 1) < lengths[:, None]
    ).astype(jnp.float32)
    token_valid = key_valid.reshape(row_count)
    (
        query_bias,
        value_bias,
        output_bias,
        inner_bias,
        outer_bias,
        first_gain,
        first_shift,
        second_gain,
        second_shift,
    ) = split_small(small_full)
    queries = (product(tokens, attention_full[0:D]) + query_bias).astype(jnp.bfloat16)
    key_vectors = product(tokens, attention_full[D : 2 * D]).astype(jnp.bfloat16)
    values = (product(tokens, attention_full[2 * D : 3 * D]) + value_bias).astype(jnp.bfloat16)
    seq_shape = (sequence_count, SEQ, D)
    attended, log_total = lax.map(
        attend_forward,
        (
            queries.reshape(seq_shape),
            key_vectors.reshape(seq_shape),
            values.reshape(seq_shape),
            key_valid,
        ),
    )
    attended = attended.reshape(row_count, D)
    branch_attention = product(attended, attention_full[3 * D : 4 * D]) + output_bias
    first_sum = tokens.astype(jnp.float32) + branch_attention
    normed = layer_norm(first_sum, first_gain, first_shift)
    normed_low = normed.astype(jnp.bfloat16)
    inner_sum = product_cols(normed_low, feed_full[0:FF]) + inner_bias
    active = gelu_exact(inner_sum).astype(jnp.bfloat16)
    gelu_slope = gelu_derivative(inner_sum)
    branch_feed = product(active, feed_full[FF : 2 * FF]) + outer_bias
    residual = normed + branch_feed
    column = token_valid[:, None]
    partials = jnp.stack(
        [
            jnp.sum(residual * residual * column),
            jnp.sum(branch_attention * branch_attention * column),
            jnp.sum(branch_feed * branch_feed * column),
            jnp.sum(token_valid),
        ]
    )
    query_weight = attention_full[0:D]
    key_weight = attention_full[D : 2 * D]
    value_weight = attention_full[2 * D : 3 * D]
    output_weight = attention_full[3 * D : 4 * D]
    outer_weight = feed_full[FF : 2 * FF]
    inner_weight = feed_full[0:FF]
    second_pull = jax.vjp(layer_norm, residual, second_gain, second_shift)[1]
    residual_grad, second_gain_grad, second_shift_grad = second_pull(cotangent)
    feed_out_grad = residual_grad.astype(jnp.bfloat16)
    outer_bias_grad = column_total(feed_out_grad)
    active_grad = product_cols(feed_out_grad, outer_weight)
    inner_grad = (active_grad * gelu_slope).astype(jnp.bfloat16)
    inner_bias_grad = column_total(inner_grad)
    feed_grad_all = (
        lax.dot_general(
            jnp.stack([inner_grad, active]),
            jnp.stack([normed_low, feed_out_grad]),
            (((1,), (1,)), ((0,), (0,))),
            preferred_element_type=jnp.float32,
        )
        .astype(jnp.bfloat16)
        .reshape(2 * FF, D)
    )
    feed_grad_all, inner_grad_late = lax.optimization_barrier((feed_grad_all, inner_grad))
    normed_grad = residual_grad + product(inner_grad_late, inner_weight)
    first_pull = jax.vjp(layer_norm, first_sum, first_gain, first_shift)[1]
    first_sum_grad, first_gain_grad, first_shift_grad = first_pull(normed_grad)
    branch_grad_low = first_sum_grad.astype(jnp.bfloat16)
    output_bias_grad = column_total(branch_grad_low)
    output_weight_grad = product_rows(attended, branch_grad_low)
    attended_grad = product_cols(branch_grad_low, output_weight).astype(jnp.bfloat16)
    query_grad, key_grad, value_grad = lax.map(
        attend_backward,
        (
            queries.reshape(seq_shape),
            key_vectors.reshape(seq_shape),
            values.reshape(seq_shape),
            key_valid,
            log_total,
            attended_grad.reshape(seq_shape),
        ),
    )
    query_grad = query_grad.reshape(row_count, D)
    key_grad = key_grad.reshape(row_count, D)
    value_grad = value_grad.reshape(row_count, D)
    query_weight_grad = product_rows(tokens, query_grad)
    key_weight_grad = product_rows(tokens, key_grad)
    value_weight_grad = product_rows(tokens, value_grad)
    query_bias_grad = column_total(query_grad)
    value_bias_grad = column_total(value_grad)
    small_grad_all = jnp.concatenate(
        [
            query_bias_grad,
            value_bias_grad,
            output_bias_grad,
            inner_bias_grad,
            outer_bias_grad,
            first_gain_grad,
            first_shift_grad,
            second_gain_grad,
            second_shift_grad,
        ]
    )
    attention_owned, feed_owned, small_owned, totals, late = scatter_gradients(
        [query_weight_grad, key_weight_grad, value_weight_grad, output_weight_grad],
        feed_grad_all,
        small_grad_all,
        partials,
        staged,
        (first_sum_grad, query_grad, key_grad, value_grad, residual),
    )
    first_sum_grad, query_grad, key_grad, value_grad, residual = late
    tokens_grad = (
        first_sum_grad
        + product_cols(query_grad, query_weight)
        + product_cols(key_grad, key_weight)
        + product_cols(value_grad, value_weight)
    )
    layer_out = layer_norm(residual, second_gain, second_shift).astype(jnp.bfloat16)
    rms_values = jnp.sqrt(totals[:3] / (totals[3] * D))
    step_float = step_count[0].astype(jnp.float32)
    attention_new, attention_first_new, attention_second_new = adam_step(
        attention_master,
        attention_first,
        attention_second,
        attention_owned,
        rate_matrix,
        weight_decay,
        step_float,
    )
    feed_new, feed_first_new, feed_second_new = adam_step(
        feed_master, feed_first, feed_second, feed_owned, rate_matrix, weight_decay, step_float
    )
    small_new, small_first_new, small_second_new = adam_step(
        small_master, small_first, small_second, small_owned, rate_small, 0.0, step_float
    )
    return (
        layer_out,
        tokens_grad,
        attention_new,
        attention_first_new,
        attention_second_new,
        attention_new.astype(jnp.bfloat16),
        feed_new,
        feed_first_new,
        feed_second_new,
        feed_new.astype(jnp.bfloat16),
        small_new,
        small_first_new,
        small_second_new,
        small_new.astype(jnp.bfloat16),
        rms_values,
    )


def solution(mesh):
    placed = (
        P(("fsdp", "dp"), None),
        P(("fsdp", "dp"), None),
        P(("fsdp", "dp")),
        P(),
        P(("fsdp", "dp"), None),
        P(("fsdp", "dp"), None),
        P(("fsdp", "dp"), None),
        P(("fsdp", "dp"), None),
        P(("fsdp", "dp"), None),
        P(("fsdp", "dp"), None),
        P(("fsdp", "dp")),
        P(("fsdp", "dp")),
        P(("fsdp", "dp")),
    )
    staged = dict(mesh.shape) == {"fsdp": 16, "dp": 2}
    return jax.shard_map(
        functools.partial(on_device, staged),
        mesh=mesh,
        in_specs=placed,
        out_specs=(
            P(("fsdp", "dp"), None),
            P(("fsdp", "dp"), None),
            P(("fsdp", "dp"), None),
            P(("fsdp", "dp"), None),
            P(("fsdp", "dp"), None),
            P(("fsdp", "dp"), None),
            P(("fsdp", "dp"), None),
            P(("fsdp", "dp"), None),
            P(("fsdp", "dp"), None),
            P(("fsdp", "dp"), None),
            P(("fsdp", "dp")),
            P(("fsdp", "dp")),
            P(("fsdp", "dp")),
            P(("fsdp", "dp")),
            P(),
        ),
        check_vma=False,
    )
```

```python
import functools
import math

import jax
import numpy as np
import jax.numpy as jnp
from jax import lax
from jax.sharding import PartitionSpec as P

D = 768
HEADS = 12
HDIM = 64
FF = 3072
SEQ = 512


ln_epsilon = 1e-12
beta_first = 0.5
beta_second = 0.55
adam_epsilon = 1e-06
rate_matrix = 0.04
rate_small = 0.25
weight_decay = 0.01


def product(left_side, right_side):
    return jnp.dot(left_side, right_side, preferred_element_type=jnp.float32)


def product_rows(left_side, right_side):
    return lax.dot_general(
        left_side, right_side, (((0,), (0,)), ((), ())), preferred_element_type=jnp.float32
    )


def product_cols(left_side, right_side):
    return lax.dot_general(
        left_side, right_side, (((1,), (1,)), ((), ())), preferred_element_type=jnp.float32
    )


def column_total(entries):
    return jnp.sum(entries, axis=0, dtype=jnp.float32)


def layer_norm(entries, norm_gain, norm_shift):
    center = jnp.mean(entries, axis=-1, keepdims=True)
    offset = entries - center
    spread = jnp.mean(offset * offset, axis=-1, keepdims=True)
    return offset * lax.rsqrt(spread + ln_epsilon) * norm_gain + norm_shift


def gelu_exact(entries):
    return jax.nn.gelu(entries, approximate=False)


def gelu_derivative(entries):
    sqrt_half = np.sqrt(0.5).astype(np.float32)
    shifted_entries = -entries * sqrt_half
    return 0.5 * lax.erfc(shifted_entries) + entries * (
        jnp.exp(-(shifted_entries * shifted_entries)) * np.float32(sqrt_half / np.sqrt(np.pi))
    )


def split_small(small_full):
    pieces = []
    position = 0
    for length in (D, D, D, FF, D, D, D, D, D):
        pieces.append(small_full[position : position + length].astype(jnp.float32))
        position = position + length
    return pieces


def head_view(entries):
    return entries.reshape(SEQ, HEADS, HDIM)


def masked_scores(queries, key_vectors, key_valid):
    scores = jnp.einsum(
        "qhd,khd->hqk",
        head_view(queries),
        head_view(key_vectors),
        preferred_element_type=jnp.float32,
    ) * (1.0 / math.sqrt(HDIM))
    return jnp.where(key_valid[None, None, :] > 0, scores, -1e30)


def attend_forward(pieces):
    queries, key_vectors, values, key_valid = pieces
    scores = masked_scores(queries, key_vectors, key_valid)
    row_max = jnp.max(scores, axis=-1, keepdims=True)
    exponent = jnp.exp(scores - row_max)
    row_total = jnp.sum(exponent, axis=-1, keepdims=True)
    probability = (exponent / row_total).astype(jnp.bfloat16)
    attended = jnp.einsum(
        "hqk,khd->qhd", probability, head_view(values), preferred_element_type=jnp.float32
    )
    return (attended.reshape(SEQ, D).astype(jnp.bfloat16), (row_max + jnp.log(row_total))[:, :, 0])


def attend_backward(pieces):
    queries, key_vectors, values, key_valid, log_total, attended_grad = pieces
    scores = masked_scores(queries, key_vectors, key_valid)
    probability = jnp.exp(scores - log_total[:, :, None])
    probability_low = probability.astype(jnp.bfloat16)
    grad_heads = head_view(attended_grad)
    value_grad = jnp.einsum(
        "hqk,qhd->khd", probability_low, grad_heads, preferred_element_type=jnp.float32
    )
    probability_grad = jnp.einsum(
        "qhd,khd->hqk", grad_heads, head_view(values), preferred_element_type=jnp.float32
    )
    inner_total = jnp.sum(probability * probability_grad, axis=-1, keepdims=True)
    score_grad = (probability * (probability_grad - inner_total)).astype(jnp.bfloat16)
    score_scale = 1.0 / math.sqrt(HDIM)
    query_grad = (
        jnp.einsum(
            "hqk,khd->qhd", score_grad, head_view(key_vectors), preferred_element_type=jnp.float32
        )
        * score_scale
    )
    key_grad = (
        jnp.einsum(
            "hqk,qhd->khd", score_grad, head_view(queries), preferred_element_type=jnp.float32
        )
        * score_scale
    )
    return (
        query_grad.reshape(SEQ, D).astype(jnp.bfloat16),
        key_grad.reshape(SEQ, D).astype(jnp.bfloat16),
        value_grad.reshape(SEQ, D).astype(jnp.bfloat16),
    )


def adam_step(master, first_moment, second, gradient, step_rate, decay_rate, step_float):
    first_new = beta_first * first_moment + (1.0 - beta_first) * gradient
    second_new = beta_second * second + (1.0 - beta_second) * gradient * gradient
    first_hat = first_new / (1.0 - beta_first**step_float)
    second_hat = second_new / (1.0 - beta_second**step_float)
    master_new = master - step_rate * (
        first_hat / (jnp.sqrt(second_hat) + adam_epsilon) + decay_rate * master
    )
    return (master_new, first_new, second_new)


def padded_rows(rows, multiple):
    return -(-rows // multiple) * multiple


def gather_working(attention_master, feed_master, small_master):
    attention_rows = attention_master.shape[0]
    feed_rows = feed_master.shape[0]
    small_count = small_master.shape[0]
    main_rows = attention_rows + feed_rows
    extra_rows = padded_rows(main_rows + padded_rows(small_count, D) // D, 16) - main_rows
    small_flat = jnp.zeros((extra_rows * D,), jnp.bfloat16)
    small_flat = small_flat.at[:small_count].set(small_master.astype(jnp.bfloat16))
    block = jnp.concatenate(
        [
            attention_master.astype(jnp.bfloat16),
            feed_master.astype(jnp.bfloat16),
            small_flat.reshape(extra_rows, D),
        ],
        axis=0,
    )
    gathered = lax.all_gather(block, ("fsdp", "dp"), axis=0, tiled=False)
    owners = gathered.shape[0]
    attention_full = gathered[:, :attention_rows].reshape(owners * attention_rows, D)
    feed_full = gathered[:, attention_rows:main_rows].reshape(owners * feed_rows, D)
    small_full = gathered[:, main_rows:].reshape(owners, extra_rows * D)[:, :small_count]
    return attention_full, feed_full, small_full.reshape(owners * small_count)


def flat_coordinates():
    me = lax.axis_index(("fsdp", "dp"))
    return me, me % 2, (me // 2) % 2, (me // 4) % 2, me // 8


def shifted(distance, count=32):
    return [(d, d + distance) for d in range(count) if 0 <= d + distance < count]


def rotated(distance, count=32):
    return [(d, (d + distance) % count) for d in range(count)]


def flipped(mask, count=32):
    return [(d, d ^ mask) for d in range(count)]


def permute(arrays, pairs):
    return lax.ppermute(tuple(arrays), ("fsdp", "dp"), pairs)


def staged_reduce_scatter(arrays, late=()):
    me, y_place, core, x_place, z_place = flat_coordinates()
    blocks = [jnp.moveaxis(entries.reshape((4, 2, 2, 2) + entries.shape[1:]), 2, 0) for entries in arrays]
    keep = [lax.dynamic_index_in_dim(b, core, axis=0, keepdims=False) for b in blocks]
    send = [lax.dynamic_index_in_dim(b, 1 - core, axis=0, keepdims=False).astype(jnp.bfloat16) for b in blocks]
    received = permute(send, flipped(2))
    plane = [k.astype(jnp.float32) + r.astype(jnp.float32) for k, r in zip(keep, received)]
    plane, late = lax.optimization_barrier((plane, late))

    def pick(entries, x_index, y_index):
        picked = lax.dynamic_index_in_dim(entries, x_index, axis=1, keepdims=False)
        return lax.dynamic_index_in_dim(picked, y_index, axis=1, keepdims=False)

    along_z = [pick(p, x_place, y_place) for p in plane]
    for mask, x_index, y_index in ((4, 1 - x_place, y_place), (1, x_place, 1 - y_place), (5, 1 - x_place, 1 - y_place)):
        got = permute([pick(p, x_index, y_index).astype(jnp.bfloat16) for p in plane], flipped(mask))
        along_z = [a + g.astype(jnp.float32) for a, g in zip(along_z, got)]
    owned = [lax.dynamic_index_in_dim(a, z_place, axis=0, keepdims=False) for a in along_z]
    for distance in (1, 2, 3):
        got = permute(
            [lax.dynamic_index_in_dim(a, (z_place + distance) % 4, axis=0, keepdims=False).astype(jnp.bfloat16) for a in along_z],
            rotated(8 * distance),
        )
        owned = [o + g.astype(jnp.float32) for o, g in zip(owned, got)]
    return owned, late


def staged_all_gather(arrays):
    me, y_place, core, x_place, z_place = flat_coordinates()
    slot = [lax.broadcasted_iota(jnp.int32, (4,) + (1,) * a.ndim, 0) for a in arrays]
    grown = [jnp.where(s == z_place, a[None], jnp.zeros((4,) + a.shape, a.dtype)) for s, a in zip(slot, arrays)]
    for distance in (1, 2, 3):
        received = permute(arrays, rotated(8 * distance))
        grown = [jnp.where(s == (z_place - distance) % 4, b[None], g) for s, b, g in zip(slot, received, grown)]
    got_x = permute(grown, flipped(4))
    got_y = permute(grown, flipped(1))
    got_xy = permute(grown, flipped(5))
    planes = []
    for own, gx, gy, gxy in zip(grown, got_x, got_y, got_xy):
        shape = (own.shape[0], 2, 2) + own.shape[1:]
        xs = lax.broadcasted_iota(jnp.int32, (1, 2, 1) + (1,) * (own.ndim - 1), 1)
        ys = lax.broadcasted_iota(jnp.int32, (1, 1, 2) + (1,) * (own.ndim - 1), 2)
        same_x, same_y = xs == x_place, ys == y_place
        plane = jnp.where(
            same_x,
            jnp.where(same_y, own[:, None, None], gy[:, None, None]),
            jnp.where(same_y, gx[:, None, None], gxy[:, None, None]),
        )
        planes.append(jnp.broadcast_to(plane, shape))
    got_core = permute(planes, flipped(2))
    gathered = []
    for own, other in zip(planes, got_core):
        own = own[:, :, None]
        other = other[:, :, None]
        size = own.shape[2]
        shape = own.shape[:2] + (2,) + own.shape[3:]
        start = [0] * len(shape)
        start_other = [0] * len(shape)
        start[2] = core * size
        start_other[2] = (1 - core) * size
        full = jnp.zeros(shape, own.dtype)
        full = lax.dynamic_update_slice(full, own, start)
        full = lax.dynamic_update_slice(full, other, start_other)
        gathered.append(full.reshape((32 * full.shape[4],) + full.shape[5:]))
    return gathered


def staged_working(attention_master, feed_master, small_master):
    small_count = small_master.shape[0]
    small_row = jnp.zeros((1, D), jnp.bfloat16).at[0, :small_count].set(small_master.astype(jnp.bfloat16))
    attention_full, small_rows = staged_all_gather([attention_master.astype(jnp.bfloat16), small_row])
    small_full = small_rows[:, :small_count].reshape(32 * small_count)
    feed_full = lax.all_gather(feed_master.astype(jnp.bfloat16), ("fsdp", "dp"), axis=0, tiled=True)
    return attention_full, feed_full, small_full


def scatter_gradients(attention_pieces, feed_pieces, small_grad_all, partials, staged, late):
    owners = lax.psum(1, ("fsdp", "dp"))
    me = lax.axis_index(("fsdp", "dp"))
    attention_rows = sum(piece.shape[0] for piece in attention_pieces) // owners
    small_count = small_grad_all.shape[0] // owners
    if staged:
        feed_rows = feed_pieces.shape[0] // owners
        dp = lax.axis_index("dp")
        within = lax.psum_scatter(
            feed_pieces.reshape(owners // 2, 2 * feed_rows, D), "fsdp", scatter_dimension=0, tiled=True
        ).reshape(2, feed_rows, D)
        keep = lax.dynamic_index_in_dim(within, dp, axis=0, keepdims=False)
        send = lax.dynamic_index_in_dim(within, 1 - dp, axis=0, keepdims=False)
        feed_owned = keep.astype(jnp.float32) + lax.ppermute(send, "dp", [(0, 1), (1, 0)]).astype(jnp.float32)
    else:
        feed_owned = lax.psum_scatter(feed_pieces, ("fsdp", "dp"), scatter_dimension=0, tiled=True)
    partials_high = partials.astype(jnp.bfloat16)
    partials_low = (partials - partials_high.astype(jnp.float32)).astype(jnp.bfloat16)
    split_partials = jnp.concatenate([partials_high, partials_low])
    slots = split_partials.shape[0]
    extra_count = small_count + owners * slots
    extra_rows = padded_rows(attention_rows + padded_rows(extra_count, D) // D, 16) - attention_rows
    slot_row = jnp.zeros((owners * slots,), jnp.bfloat16)
    slot_row = lax.dynamic_update_slice(slot_row, split_partials, (me * slots,))
    extra = jnp.concatenate(
        [
            small_grad_all.astype(jnp.bfloat16).reshape(owners, small_count),
            jnp.broadcast_to(slot_row[None], (owners, owners * slots)),
            jnp.zeros((owners, extra_rows * D - extra_count), jnp.bfloat16),
        ],
        axis=1,
    ).reshape(owners, extra_rows, D)
    block_rows = attention_rows + extra_rows
    if staged:
        attention_grad_all = jnp.concatenate(attention_pieces, axis=0).astype(jnp.bfloat16)
        owned_parts, late = staged_reduce_scatter(
            [attention_grad_all.reshape(owners, attention_rows, D), extra], late
        )
        owned = jnp.concatenate(owned_parts, axis=0)
    else:
        packed = jnp.zeros((owners, block_rows, D), jnp.bfloat16)
        packed = lax.dynamic_update_slice(packed, extra, (0, attention_rows, 0))
        owner = 0
        for piece in attention_pieces:
            piece_owners = piece.shape[0] // attention_rows
            packed = lax.dynamic_update_slice(
                packed, piece.astype(jnp.bfloat16).reshape(piece_owners, attention_rows, D), (owner, 0, 0)
            )
            owner = owner + piece_owners
        owned = lax.psum_scatter(
            packed.reshape(owners * block_rows, D), ("fsdp", "dp"), scatter_dimension=0, tiled=True
        ).astype(jnp.float32)
    attention_owned = owned[:attention_rows]
    extra_owned = owned[attention_rows:].reshape(extra_rows * D)
    small_owned = extra_owned[:small_count]
    gathered_partials = extra_owned[small_count:extra_count].reshape(owners, slots)
    half = slots // 2
    totals = gathered_partials[0, :half] + gathered_partials[0, half:]
    for index in range(1, owners):
        totals = totals + (gathered_partials[index, :half] + gathered_partials[index, half:])
    return attention_owned, feed_owned.astype(jnp.float32), small_owned, totals, late


def on_device(
    staged,
    tokens,
    cotangent,
    lengths,
    step_count,
    attention_master,
    attention_first,
    attention_second,
    feed_master,
    feed_first,
    feed_second,
    small_master,
    small_first,
    small_second,
):
    row_count = tokens.shape[0]
    sequence_count = row_count // SEQ
    if staged:
        attention_full, feed_full, small_full = staged_working(attention_master, feed_master, small_master)
    else:
        attention_full, feed_full, small_full = gather_working(attention_master, feed_master, small_master)
    key_valid = (
        lax.broadcasted_iota(jnp.int32, (sequence_count, SEQ), 1) < lengths[:, None]
    ).astype(jnp.float32)
    token_valid = key_valid.reshape(row_count)
    (
        query_bias,
        value_bias,
        output_bias,
        inner_bias,
        outer_bias,
        first_gain,
        first_shift,
        second_gain,
        second_shift,
    ) = split_small(small_full)
    queries = (product(tokens, attention_full[0:D]) + query_bias).astype(jnp.bfloat16)
    key_vectors = product(tokens, attention_full[D : 2 * D]).astype(jnp.bfloat16)
    values = (product(tokens, attention_full[2 * D : 3 * D]) + value_bias).astype(jnp.bfloat16)
    seq_shape = (sequence_count, SEQ, D)
    attended, log_total = lax.map(
        attend_forward,
        (
            queries.reshape(seq_shape),
            key_vectors.reshape(seq_shape),
            values.reshape(seq_shape),
            key_valid,
        ),
    )
    attended = attended.reshape(row_count, D)
    branch_attention = product(attended, attention_full[3 * D : 4 * D]) + output_bias
    first_sum = tokens.astype(jnp.float32) + branch_attention
    normed = layer_norm(first_sum, first_gain, first_shift)
    normed_low = normed.astype(jnp.bfloat16)
    inner_sum = product_cols(normed_low, feed_full[0:FF]) + inner_bias
    active = gelu_exact(inner_sum).astype(jnp.bfloat16)
    gelu_slope = gelu_derivative(inner_sum)
    active, gelu_slope = lax.optimization_barrier((active, gelu_slope))
    branch_feed = product(active, feed_full[FF : 2 * FF]) + outer_bias
    residual = normed + branch_feed
    column = token_valid[:, None]
    partials = jnp.stack(
        [
            jnp.sum(residual * residual * column),
            jnp.sum(branch_attention * branch_attention * column),
            jnp.sum(branch_feed * branch_feed * column),
            jnp.sum(token_valid),
        ]
    )
    query_weight = attention_full[0:D]
    key_weight = attention_full[D : 2 * D]
    value_weight = attention_full[2 * D : 3 * D]
    output_weight = attention_full[3 * D : 4 * D]
    outer_weight = feed_full[FF : 2 * FF]
    inner_weight = feed_full[0:FF]
    second_pull = jax.vjp(layer_norm, residual, second_gain, second_shift)[1]
    residual_grad, second_gain_grad, second_shift_grad = second_pull(cotangent)
    feed_out_grad = residual_grad.astype(jnp.bfloat16)
    outer_bias_grad = column_total(feed_out_grad)
    active_grad = product_cols(feed_out_grad, outer_weight)
    inner_grad = (active_grad * gelu_slope).astype(jnp.bfloat16)
    inner_bias_grad = column_total(inner_grad)
    feed_grad_all = (
        lax.dot_general(
            jnp.stack([inner_grad, active]),
            jnp.stack([normed_low, feed_out_grad]),
            (((1,), (1,)), ((0,), (0,))),
            preferred_element_type=jnp.float32,
        )
        .astype(jnp.bfloat16)
        .reshape(2 * FF, D)
    )
    feed_grad_all, inner_grad_late, partials = lax.optimization_barrier((feed_grad_all, inner_grad, partials))
    normed_grad = residual_grad + product(inner_grad_late, inner_weight)
    first_pull = jax.vjp(layer_norm, first_sum, first_gain, first_shift)[1]
    first_sum_grad, first_gain_grad, first_shift_grad = first_pull(normed_grad)
    branch_grad_low = first_sum_grad.astype(jnp.bfloat16)
    output_bias_grad = column_total(branch_grad_low)
    output_weight_grad = product_rows(attended, branch_grad_low)
    attended_grad = product_cols(branch_grad_low, output_weight).astype(jnp.bfloat16)
    query_grad, key_grad, value_grad = lax.map(
        attend_backward,
        (
            queries.reshape(seq_shape),
            key_vectors.reshape(seq_shape),
            values.reshape(seq_shape),
            key_valid,
            log_total,
            attended_grad.reshape(seq_shape),
        ),
    )
    query_grad = query_grad.reshape(row_count, D)
    key_grad = key_grad.reshape(row_count, D)
    value_grad = value_grad.reshape(row_count, D)
    query_weight_grad = product_rows(tokens, query_grad)
    key_weight_grad = product_rows(tokens, key_grad)
    value_weight_grad = product_rows(tokens, value_grad)
    query_bias_grad = column_total(query_grad)
    value_bias_grad = column_total(value_grad)
    small_grad_all = jnp.concatenate(
        [
            query_bias_grad,
            value_bias_grad,
            output_bias_grad,
            inner_bias_grad,
            outer_bias_grad,
            first_gain_grad,
            first_shift_grad,
            second_gain_grad,
            second_shift_grad,
        ]
    )
    attention_owned, feed_owned, small_owned, totals, late = scatter_gradients(
        [query_weight_grad, key_weight_grad, value_weight_grad, output_weight_grad],
        feed_grad_all,
        small_grad_all,
        partials,
        staged,
        (first_sum_grad, query_grad, key_grad, value_grad, residual),
    )
    first_sum_grad, query_grad, key_grad, value_grad, residual = late
    tokens_grad = (
        first_sum_grad
        + product_cols(query_grad, query_weight)
        + product_cols(key_grad, key_weight)
        + product_cols(value_grad, value_weight)
    )
    layer_out = layer_norm(residual, second_gain, second_shift).astype(jnp.bfloat16)
    rms_values = jnp.sqrt(totals[:3] / (totals[3] * D))
    step_float = step_count[0].astype(jnp.float32)
    attention_new, attention_first_new, attention_second_new = adam_step(
        attention_master,
        attention_first,
        attention_second,
        attention_owned,
        rate_matrix,
        weight_decay,
        step_float,
    )
    feed_new, feed_first_new, feed_second_new = adam_step(
        feed_master, feed_first, feed_second, feed_owned, rate_matrix, weight_decay, step_float
    )
    small_new, small_first_new, small_second_new = adam_step(
        small_master, small_first, small_second, small_owned, rate_small, 0.0, step_float
    )
    return (
        layer_out,
        tokens_grad,
        attention_new,
        attention_first_new,
        attention_second_new,
        attention_new.astype(jnp.bfloat16),
        feed_new,
        feed_first_new,
        feed_second_new,
        feed_new.astype(jnp.bfloat16),
        small_new,
        small_first_new,
        small_second_new,
        small_new.astype(jnp.bfloat16),
        rms_values,
    )


def solution(mesh):
    placed = (
        P(("fsdp", "dp"), None),
        P(("fsdp", "dp"), None),
        P(("fsdp", "dp")),
        P(),
        P(("fsdp", "dp"), None),
        P(("fsdp", "dp"), None),
        P(("fsdp", "dp"), None),
        P(("fsdp", "dp"), None),
        P(("fsdp", "dp"), None),
        P(("fsdp", "dp"), None),
        P(("fsdp", "dp")),
        P(("fsdp", "dp")),
        P(("fsdp", "dp")),
    )
    staged = dict(mesh.shape) == {"fsdp": 16, "dp": 2}
    return jax.shard_map(
        functools.partial(on_device, staged),
        mesh=mesh,
        in_specs=placed,
        out_specs=(
            P(("fsdp", "dp"), None),
            P(("fsdp", "dp"), None),
            P(("fsdp", "dp"), None),
            P(("fsdp", "dp"), None),
            P(("fsdp", "dp"), None),
            P(("fsdp", "dp"), None),
            P(("fsdp", "dp"), None),
            P(("fsdp", "dp"), None),
            P(("fsdp", "dp"), None),
            P(("fsdp", "dp"), None),
            P(("fsdp", "dp")),
            P(("fsdp", "dp")),
            P(("fsdp", "dp")),
            P(("fsdp", "dp")),
            P(),
        ),
        check_vma=False,
    )
```
